32 devices in a mesh: ctx: 8 (over z, x), tp: 4 (over y, core).
Axes of the slice: x: 2, y: 2, z: 4, core: 2. Of those that a mesh axis runs over, the one named last changes fastest.
Arguments:
- tokens: bfloat16 [2048, 16384], P('ctx', 'tp')
- document: int32 [2048], P('ctx'), may hold values from 0 to 5, as said below
- place: int32 [2048], P('ctx'), may hold values from 0 to 1023, as said below
- w_qkv: bfloat16 [1280, 16384], P(None, 'tp')
- w_out: bfloat16 [1024, 16384], P(None, 'tp'), may hold values from -0.1875 to 0.1875
- grad_out: bfloat16 [2048, 16384], P('ctx', 'tp'), may hold values from -6 to 6
Outputs:
- out: bfloat16 [2048, 16384], P('ctx', 'tp')
- grad_x: bfloat16 [2048, 16384], P('ctx', 'tp')
- grad_w_qkv: float32 [1280, 16384], P('ctx', 'tp')
- grad_w_out: float32 [1024, 16384], P('ctx', 'tp')
The draws below stay inside these ranges and needn't reach their ends.
Inputs may be any that keep to these rules, and one draw needn't show every extreme that they name: Each document's tokens carry the positions 0 to its length minus 1, each once; one document holds 1024 tokens. `place`: position of a token within its document, as described for document.
All inputs are finite; a program needn't handle non-finite values.
Results may differ from the reference program's by a relative error of at most 0.028.
Values may be sent and summed in bfloat16 or wider, within the bound.
No kernel may reach another device: no remote copies, remote signals or barrier semaphores. Data moves between devices by JAX's collectives and lax.ppermute only.
A program may use at most 128 MiB of HBM per device.

```python
import math
import jax
import jax.numpy as jnp
from jax import lax

D = 16384
HD = 128
HQ = 8
NDOCS = 6
TOK_CTX = 256
QKV = 1280
PACK = 2048
N_CTX = 8


def layout(key):
    half = PACK // 2
    cut_key, long_key = jax.random.split(jax.random.fold_in(key, 7))
    cuts = jnp.sort(jax.random.choice(cut_key, half - 1, (NDOCS - 2,), replace=False).astype(jnp.int32) + 1)
    edges = jnp.concatenate([jnp.zeros((1,), jnp.int32), cuts, jnp.full((1,), half, jnp.int32)])
    short = edges[1:] - edges[:-1]
    long_index = jax.random.randint(long_key, (), 0, NDOCS)
    index = jnp.arange(NDOCS, dtype=jnp.int32)
    picked = jnp.take(short, jnp.clip(jnp.where(index < long_index, index, index - 1), 0, NDOCS - 2))
    lengths = jnp.where(index == long_index, half, picked).astype(jnp.int32)
    starts = jnp.cumsum(lengths) - lengths
    stored = jnp.arange(PACK, dtype=jnp.int32)
    shard = stored // TOK_CTX
    inner = stored % TOK_CTX
    piece = TOK_CTX // 2
    block = jnp.where(inner < piece, shard, 2 * N_CTX - 1 - shard)
    anchor = block * piece + inner % piece
    document = jnp.sum((anchor[:, None] >= starts[None, 1:]).astype(jnp.int32), axis=1).astype(jnp.int32)
    place = (anchor - jnp.take(starts, document)).astype(jnp.int32)
    return (document, place)


def draw_document(key, part):
    return layout(key)[0]


def draw_place(key, part):
    return layout(key)[1]


def draw_tokens(key, part):
    base = jax.random.normal(jax.random.fold_in(key, 11), (PACK, D), jnp.float32)
    return jnp.clip(base, -24.0, 24.0).astype(jnp.bfloat16)


def draw_w_qkv(key, part):
    base = jax.random.normal(jax.random.fold_in(key, 13), (QKV, D), jnp.float32) * D ** (-0.5)
    return base.astype(jnp.bfloat16)


def shard_levels(stream_key, dims, pieces, smallest, high):
    def one(axis_at, parts):
        draws = jax.random.uniform(jax.random.fold_in(jax.random.fold_in(stream_key, 6), axis_at), (parts,), jnp.float32, smallest / len(pieces), high / len(pieces))
        return jnp.repeat(jnp.exp(draws), dims[axis_at] // parts).reshape((-1,) + (1,) * (len(dims) - axis_at - 1))

    factor_of = one(*pieces[0])
    for cut in pieces[1:]:
        factor_of = factor_of * one(*cut)
    return factor_of


def gaussian(stream_key, shape, scale, limit, pieces=(), kind=jnp.bfloat16):
    result = jax.random.normal(stream_key, shape, jnp.float32) * scale
    if len(pieces) > 0:
        result = shard_levels(stream_key, shape, pieces, -0.22, 0.18) * result
    return jnp.clip(result, min=-limit, max=limit).astype(kind)


def setup_inputs(seed: int = 0) -> dict:
    splits = jax.random.split(jax.random.key(seed), 7)
    tokens = draw_tokens(jax.random.fold_in(splits[6], 71), 0)
    document = draw_document(jax.random.fold_in(splits[6], 71), 0)
    place = draw_place(jax.random.fold_in(splits[6], 71), 0)
    w_qkv = draw_w_qkv(jax.random.fold_in(splits[6], 71), 0)
    w_out = gaussian(splits[4], (HQ * HD, D), (HQ * HD) ** -0.5, 0.1875, ((1, 4),))
    grad_out = gaussian(splits[5], (PACK, D), 1.0, 6.0, ((0, 8), (1, 4)))
    return dict(tokens=tokens, document=document, place=place, w_qkv=w_qkv, w_out=w_out, grad_out=grad_out)


THETA = 500000.0
NEG = -1e+30

def angles(place, width):
    half = width // 2
    freq = THETA ** (-(jnp.arange(half, dtype=jnp.float32) * 2.0 / width))
    turn = place.astype(jnp.float32)[:, None] * freq[None, :]
    return (jnp.cos(turn), jnp.sin(turn))

def rotate(vector, cosine, sine):
    half = vector.shape[-1] // 2
    first = vector[..., :half]
    second = vector[..., half:]
    return jnp.concatenate([first * cosine - second * sine, second * cosine + first * sine], axis=-1)

def reference(tokens, document, place, w_qkv, w_out, grad_out):
    heads_width = HQ * HD
    factor = 1.0 / math.sqrt(HD)
    qkv = jnp.dot(tokens, w_qkv.T, preferred_element_type=jnp.float32)
    cosine, sine = angles(place, HD)
    queries = rotate(qkv[:, :heads_width].reshape(PACK, HQ, HD), cosine[:, None, :], sine[:, None, :]).astype(jnp.bfloat16)
    keys = rotate(qkv[:, heads_width:heads_width + HD], cosine, sine).astype(jnp.bfloat16)
    values = qkv[:, heads_width + HD:].astype(jnp.bfloat16)
    keys_wide = keys.astype(jnp.float32)
    values_wide = values.astype(jnp.float32)
    blocks = PACK // TOK_CTX

    def block_scores(index):
        start = index * TOK_CTX
        block_query = lax.dynamic_slice_in_dim(queries, start, TOK_CTX, 0).astype(jnp.float32)
        block_doc = lax.dynamic_slice_in_dim(document, start, TOK_CTX, 0)
        block_place = lax.dynamic_slice_in_dim(place, start, TOK_CTX, 0)
        allowed = (block_doc[:, None] == document[None, :]) & (place[None, :] <= block_place[:, None])
        scores = jnp.einsum('rhd,kd->hrk', block_query, keys_wide) * factor
        return (block_query, allowed, scores)

    def forward_block(index):
        block_query, allowed, scores = block_scores(index)
        scores = jnp.where(allowed[None], scores, NEG)
        top = lax.optimization_barrier(jnp.max(scores, axis=-1, keepdims=True))
        weights = jnp.where(allowed[None], jnp.exp(scores - top), 0.0)
        total = lax.optimization_barrier(jnp.sum(weights, axis=-1, keepdims=True))
        rounded = lax.optimization_barrier(weights.astype(jnp.bfloat16)).astype(jnp.float32)
        mixed = jnp.einsum('hrk,kd->rhd', rounded, values_wide) / jnp.transpose(total, (1, 0, 2))
        logsum = (top + jnp.log(total))[..., 0]
        return (mixed.astype(jnp.bfloat16).reshape(TOK_CTX, heads_width), logsum)
    attended, logsums = lax.map(forward_block, jnp.arange(blocks))
    attended = attended.reshape(PACK, heads_width)
    out = jnp.dot(attended, w_out, preferred_element_type=jnp.float32).astype(jnp.bfloat16)
    grad_w_out = jnp.dot(attended.T, grad_out, preferred_element_type=jnp.float32)
    d_attended = jnp.dot(grad_out, w_out.T, preferred_element_type=jnp.float32).astype(jnp.bfloat16)

    def backward_block(carry, index):
        dkeys, dvalues = carry
        block_query, allowed, scores = block_scores(index)
        start = index * TOK_CTX
        prob = jnp.where(allowed[None], jnp.exp(scores - logsums[index][..., None]), 0.0)
        rounded = lax.optimization_barrier(prob.astype(jnp.bfloat16)).astype(jnp.float32)
        grad_block = lax.dynamic_slice_in_dim(d_attended, start, TOK_CTX, 0).reshape(TOK_CTX, HQ, HD).astype(jnp.float32)
        out_block = lax.dynamic_slice_in_dim(attended, start, TOK_CTX, 0).reshape(TOK_CTX, HQ, HD).astype(jnp.float32)
        delta = lax.optimization_barrier(jnp.sum(grad_block * out_block, axis=-1))
        dprob = jnp.einsum('rhd,kd->hrk', grad_block, values_wide)
        dscore = prob * (dprob - jnp.transpose(delta)[..., None])
        dscore = lax.optimization_barrier(dscore.astype(jnp.bfloat16)).astype(jnp.float32)
        dquery = jnp.einsum('hrk,kd->rhd', dscore, keys_wide) * factor
        dkeys = dkeys + jnp.einsum('hrk,rhd->kd', dscore, block_query) * factor
        dvalues = dvalues + jnp.einsum('hrk,rhd->kd', rounded, grad_block)
        return ((dkeys, dvalues), dquery)
    start_grads = (jnp.zeros((PACK, HD), jnp.float32), jnp.zeros((PACK, HD), jnp.float32))
    (dkeys, dvalues), dquery = lax.scan(backward_block, start_grads, jnp.arange(blocks))
    dquery = dquery.reshape(PACK, HQ, HD)
    query_raw = rotate(dquery, cosine[:, None, :], -sine[:, None, :]).reshape(PACK, heads_width)
    key_raw = rotate(dkeys, cosine, -sine)
    d_qkv = jnp.concatenate([query_raw, key_raw, dvalues], axis=1).astype(jnp.bfloat16)
    grad_x = jnp.dot(d_qkv, w_qkv, preferred_element_type=jnp.float32).astype(jnp.bfloat16)
    grad_w_qkv = jnp.dot(d_qkv.T, tokens, preferred_element_type=jnp.float32)
    return (out, grad_x, grad_w_qkv, grad_w_out)
```

```python
import math

import jax
import jax.numpy as jnp
from jax import lax
from jax.sharding import PartitionSpec as P

HD = 128
HQ = 8


THETA = 500000.0
NEG = -1e30
PIECE = 64


def angles(place, width):
    half = width // 2
    freq = THETA ** (-(jnp.arange(half, dtype=jnp.float32) * 2.0 / width))
    turn = place.astype(jnp.float32)[:, None] * freq[None, :]
    return (jnp.cos(turn), jnp.sin(turn))


def rotate(vector, cosine, sine):
    half = vector.shape[-1] // 2
    first = vector[..., :half]
    second = vector[..., half:]
    return jnp.concatenate(
        [first * cosine - second * sine, second * cosine + first * sine], axis=-1
    )


def against(left, right):
    return lax.dot_general(
        left, right, (((1,), (1,)), ((), ())), preferred_element_type=jnp.float32
    )


def across(left, right):
    return lax.dot_general(
        left, right, (((0,), (0,)), ((), ())), preferred_element_type=jnp.float32
    )


def shards(tokens, document, place, w_qkv, w_out, grad_out):
    rows_ctx, slice_width = tokens.shape
    ctx_size = lax.axis_size("ctx")
    tp_size = lax.axis_size("tp")
    rows_mine = rows_ctx // tp_size
    tp_rank = lax.axis_index("tp")
    head_dim = HD
    heads = HQ
    heads_width = heads * head_dim
    pair_width = 2 * head_dim
    factor = 1.0 / math.sqrt(head_dim)
    first_row = tp_rank * rows_mine
    stacked = heads * rows_mine
    total_rows = ctx_size * rows_ctx

    grad_rows = lax.psum_scatter(
        against(grad_out, w_out).astype(jnp.bfloat16), "tp", scatter_dimension=0, tiled=True
    )

    cosine_all, sine_all = angles(place, head_dim)
    cosine_mine = lax.dynamic_slice_in_dim(cosine_all, first_row, rows_mine, 0)
    sine_mine = lax.dynamic_slice_in_dim(sine_all, first_row, rows_mine, 0)
    query_doc = lax.dynamic_slice_in_dim(document, first_row, rows_mine, 0)
    query_place = lax.dynamic_slice_in_dim(place, first_row, rows_mine, 0)

    qkv = lax.psum(against(tokens, w_qkv), "tp")
    keys = rotate(qkv[:, heads_width : heads_width + head_dim], cosine_all, sine_all).astype(
        jnp.bfloat16
    )
    values = qkv[:, heads_width + head_dim :].astype(jnp.bfloat16)

    info = jnp.concatenate(
        [document, place // PIECE, place % PIECE], axis=0
    ).astype(jnp.float32)
    info_rows = -(-info.shape[0] // pair_width)
    info = jnp.pad(info, (0, info_rows * pair_width - info.shape[0]))
    info = info.reshape(info_rows, pair_width).astype(jnp.bfloat16)
    packed = jnp.concatenate([keys, values, ], axis=1)
    packed = jnp.concatenate([packed, info], axis=0)
    gathered = lax.all_gather(packed, "ctx", axis=0, tiled=False)
    keys_all = gathered[:, :rows_ctx, :head_dim].reshape(total_rows, head_dim)
    values_all = gathered[:, :rows_ctx, head_dim:].reshape(total_rows, head_dim)
    info_all = gathered[:, rows_ctx:, :].reshape(ctx_size, info_rows * pair_width).astype(
        jnp.float32
    )
    key_doc = info_all[:, :rows_ctx].reshape(total_rows)
    key_place = (
        info_all[:, rows_ctx : 2 * rows_ctx] * PIECE + info_all[:, 2 * rows_ctx : 3 * rows_ctx]
    ).reshape(total_rows)

    allowed = (query_doc.astype(jnp.float32)[:, None] == key_doc[None, :]) & (
        key_place[None, :] <= query_place.astype(jnp.float32)[:, None]
    )
    allowed = jnp.broadcast_to(allowed[None], (heads, rows_mine, total_rows)).reshape(
        stacked, total_rows
    )

    mine = lax.dynamic_slice_in_dim(qkv, first_row, rows_mine, 0)
    raw_query = mine[:, :heads_width].reshape(rows_mine, heads, head_dim)
    rotated = rotate(raw_query, cosine_mine[:, None, :], sine_mine[:, None, :]).astype(jnp.bfloat16)
    queries = jnp.transpose(rotated, (1, 0, 2)).reshape(stacked, head_dim)

    scores = against(queries, keys_all) * factor
    masked = jnp.where(allowed, scores, NEG)
    top = jnp.max(masked, axis=1)
    weights = jnp.where(allowed, jnp.exp(masked - top[:, None]), 0.0)
    total = jnp.sum(weights, axis=1)
    summed = jnp.dot(weights.astype(jnp.bfloat16), values_all, preferred_element_type=jnp.float32)
    attended = (summed / total[:, None]).astype(jnp.bfloat16)
    logsum = top + jnp.log(total)

    rows_attended = jnp.transpose(attended.reshape(heads, rows_mine, head_dim), (1, 0, 2)).reshape(
        rows_mine, heads_width
    )
    piece = lax.all_gather(rows_attended, "tp", axis=0, tiled=True)
    out = jnp.dot(piece, w_out, preferred_element_type=jnp.float32).astype(jnp.bfloat16)
    out_weight_grad = across(piece, grad_out)

    grad_stack = jnp.transpose(grad_rows.reshape(rows_mine, heads, head_dim), (1, 0, 2)).reshape(
        stacked, head_dim
    )
    delta = jnp.sum(grad_stack.astype(jnp.float32) * attended.astype(jnp.float32), axis=1)
    prob = jnp.where(allowed, jnp.exp(scores - logsum[:, None]), 0.0)
    dprob = against(grad_stack, values_all)
    dscore = (prob * (dprob - delta[:, None])).astype(jnp.bfloat16)
    query_sum = jnp.dot(dscore, keys_all, preferred_element_type=jnp.float32)
    key_part = across(dscore, queries) * factor
    value_part = across(prob.astype(jnp.bfloat16), grad_stack)
    pair_all = jnp.concatenate([key_part, value_part], axis=1)
    pair_grad = lax.psum_scatter(pair_all, ("ctx", "tp"), scatter_dimension=0, tiled=True)

    key_raw = rotate(pair_grad[:, :head_dim], cosine_mine, -sine_mine)
    query_grad = jnp.transpose((query_sum * factor).reshape(heads, rows_mine, head_dim), (1, 0, 2))
    query_raw = rotate(query_grad, cosine_mine[:, None, :], -sine_mine[:, None, :]).reshape(
        rows_mine, heads_width
    )
    d_mine = jnp.concatenate([query_raw, key_raw, pair_grad[:, head_dim:]], axis=1).astype(
        jnp.bfloat16
    )
    d_qkv = lax.all_gather(d_mine, "tp", axis=0, tiled=True)
    grad_x = jnp.dot(d_qkv, w_qkv, preferred_element_type=jnp.float32).astype(jnp.bfloat16)
    joint_weight = across(d_qkv, tokens)
    grad_w_qkv = lax.psum_scatter(
        joint_weight.astype(jnp.bfloat16), "ctx", scatter_dimension=0, tiled=True
    ).astype(jnp.float32)
    grad_w_out = lax.psum_scatter(
        out_weight_grad.astype(jnp.bfloat16), "ctx", scatter_dimension=0, tiled=True
    ).astype(jnp.float32)
    return (out, grad_x, grad_w_qkv, grad_w_out)


def solution(mesh):
    return jax.shard_map(
        shards,
        mesh=mesh,
        in_specs=(P("ctx", "tp"), P("ctx"), P("ctx"), P(None, "tp"), P(None, "tp"), P("ctx", "tp")),
        out_specs=(P("ctx", "tp"), P("ctx", "tp"), P("ctx", "tp"), P("ctx", "tp")),
        check_vma=False,
    )
```

```python
import functools
import math

import jax
import jax.numpy as jnp
from jax import lax
from jax.sharding import PartitionSpec as P

HD = 128
HQ = 8


THETA = 500000.0
NEG = -1e30
PIECE = 64


def angles(place, width):
    half = width // 2
    freq = THETA ** (-(jnp.arange(half, dtype=jnp.float32) * 2.0 / width))
    turn = place.astype(jnp.float32)[:, None] * freq[None, :]
    return (jnp.cos(turn), jnp.sin(turn))


def rotate(vector, cosine, sine):
    half = vector.shape[-1] // 2
    first = vector[..., :half]
    second = vector[..., half:]
    return jnp.concatenate(
        [first * cosine - second * sine, second * cosine + first * sine], axis=-1
    )


def against(left, right):
    return lax.dot_general(
        left, right, (((1,), (1,)), ((), ())), preferred_element_type=jnp.float32
    )


def across(left, right):
    return lax.dot_general(
        left, right, (((0,), (0,)), ((), ())), preferred_element_type=jnp.float32
    )


def ring_of(mesh):
    count = mesh.shape["ctx"]
    try:
        grid = mesh.devices.reshape(count, -1)
        coords = [tuple(grid[i, 0].coords) for i in range(count)]
    except Exception:
        return list(range(count))
    varying = [d for d in range(len(coords[0])) if len({c[d] for c in coords}) > 1]
    if len(varying) == 1:
        return sorted(range(count), key=lambda i: coords[i][varying[0]])
    if len(varying) != 2:
        return list(range(count))
    for short, long in (varying, varying[::-1]):
        levels = sorted({c[short] for c in coords})
        if len(levels) == 2:
            there = sorted(
                (i for i in range(count) if coords[i][short] == levels[0]),
                key=lambda i: coords[i][long],
            )
            back = sorted(
                (i for i in range(count) if coords[i][short] == levels[1]),
                key=lambda i: -coords[i][long],
            )
            return there + back
    return list(range(count))


def ring_scatter(partial, ring, axis):
    count = len(ring)
    where = [0] * count
    for spot, member in enumerate(ring):
        where[member] = spot
    spot = jnp.asarray(where, jnp.int32)[lax.axis_index(axis)]
    order = jnp.asarray(ring, jnp.int32)
    rows = partial.shape[0] // count
    half = partial.shape[1] // 2
    blocks = partial.reshape(count, rows, partial.shape[1])
    left = blocks[:, :, :half]
    right = blocks[:, :, half:]

    def block(side, offset):
        return lax.dynamic_index_in_dim(side, order[(spot + offset) % count], 0, keepdims=False)

    forward = [(ring[p], ring[(p + 1) % count]) for p in range(count)]
    backward = [(ring[p], ring[(p - 1) % count]) for p in range(count)]
    send_left = block(left, count - 1)
    send_right = block(right, 1)
    for step in range(count - 1):
        got_left = lax.ppermute(send_left.astype(jnp.bfloat16), axis, forward)
        got_right = lax.ppermute(send_right.astype(jnp.bfloat16), axis, backward)
        send_left = got_left.astype(jnp.float32) + block(left, 2 * count - step - 2)
        send_right = got_right.astype(jnp.float32) + block(right, step + 2)
    return jnp.concatenate([send_left, send_right], axis=1)


def shards(ring, tokens, document, place, w_qkv, w_out, grad_out):
    rows_ctx, slice_width = tokens.shape
    ctx_size = lax.axis_size("ctx")
    tp_size = lax.axis_size("tp")
    rows_mine = rows_ctx // tp_size
    tp_rank = lax.axis_index("tp")
    head_dim = HD
    heads = HQ
    heads_width = heads * head_dim
    pair_width = 2 * head_dim
    factor = 1.0 / math.sqrt(head_dim)
    first_row = tp_rank * rows_mine
    stacked = heads * rows_mine
    total_rows = ctx_size * rows_ctx

    grad_rows = lax.psum_scatter(
        against(grad_out, w_out).astype(jnp.bfloat16), "tp", scatter_dimension=0, tiled=True
    )

    cosine_all, sine_all = angles(place, head_dim)
    cosine_mine = lax.dynamic_slice_in_dim(cosine_all, first_row, rows_mine, 0)
    sine_mine = lax.dynamic_slice_in_dim(sine_all, first_row, rows_mine, 0)
    query_doc = lax.dynamic_slice_in_dim(document, first_row, rows_mine, 0)
    query_place = lax.dynamic_slice_in_dim(place, first_row, rows_mine, 0)

    qkv = lax.psum(against(tokens, w_qkv), "tp")
    keys = rotate(qkv[:, heads_width : heads_width + head_dim], cosine_all, sine_all).astype(
        jnp.bfloat16
    )
    values = qkv[:, heads_width + head_dim :].astype(jnp.bfloat16)

    info = jnp.concatenate(
        [document, place // PIECE, place % PIECE], axis=0
    ).astype(jnp.float32)
    info_rows = -(-info.shape[0] // pair_width)
    info = jnp.pad(info, (0, info_rows * pair_width - info.shape[0]))
    info = info.reshape(info_rows, pair_width).astype(jnp.bfloat16)
    packed = jnp.concatenate([keys, values, ], axis=1)
    packed = jnp.concatenate([packed, info], axis=0)
    gathered = lax.all_gather(packed, "ctx", axis=0, tiled=False)
    keys_all = gathered[:, :rows_ctx, :head_dim].reshape(total_rows, head_dim)
    values_all = gathered[:, :rows_ctx, head_dim:].reshape(total_rows, head_dim)
    info_all = gathered[:, rows_ctx:, :].reshape(ctx_size, info_rows * pair_width).astype(
        jnp.float32
    )
    key_doc = info_all[:, :rows_ctx].reshape(total_rows)
    key_place = (
        info_all[:, rows_ctx : 2 * rows_ctx] * PIECE + info_all[:, 2 * rows_ctx : 3 * rows_ctx]
    ).reshape(total_rows)

    allowed = (query_doc.astype(jnp.float32)[:, None] == key_doc[None, :]) & (
        key_place[None, :] <= query_place.astype(jnp.float32)[:, None]
    )
    allowed = jnp.broadcast_to(allowed[None], (heads, rows_mine, total_rows)).reshape(
        stacked, total_rows
    )

    mine = lax.dynamic_slice_in_dim(qkv, first_row, rows_mine, 0)
    raw_query = mine[:, :heads_width].reshape(rows_mine, heads, head_dim)
    rotated = rotate(raw_query, cosine_mine[:, None, :], sine_mine[:, None, :]).astype(jnp.bfloat16)
    queries = jnp.transpose(rotated, (1, 0, 2)).reshape(stacked, head_dim)

    scores = against(queries, keys_all) * factor
    masked = jnp.where(allowed, scores, NEG)
    top = jnp.max(masked, axis=1)
    weights = jnp.where(allowed, jnp.exp(masked - top[:, None]), 0.0)
    total = jnp.sum(weights, axis=1)
    summed = jnp.dot(weights.astype(jnp.bfloat16), values_all, preferred_element_type=jnp.float32)
    attended = (summed / total[:, None]).astype(jnp.bfloat16)
    logsum = top + jnp.log(total)

    rows_attended = jnp.transpose(attended.reshape(heads, rows_mine, head_dim), (1, 0, 2)).reshape(
        rows_mine, heads_width
    )
    piece = lax.all_gather(rows_attended, "tp", axis=0, tiled=True)
    out = jnp.dot(piece, w_out, preferred_element_type=jnp.float32).astype(jnp.bfloat16)
    out_weight_grad = across(piece, grad_out)

    grad_stack = jnp.transpose(grad_rows.reshape(rows_mine, heads, head_dim), (1, 0, 2)).reshape(
        stacked, head_dim
    )
    delta = jnp.sum(grad_stack.astype(jnp.float32) * attended.astype(jnp.float32), axis=1)
    prob = jnp.where(allowed, jnp.exp(scores - logsum[:, None]), 0.0)
    dprob = against(grad_stack, values_all)
    dscore = (prob * (dprob - delta[:, None])).astype(jnp.bfloat16)
    query_sum = jnp.dot(dscore, keys_all, preferred_element_type=jnp.float32)
    key_part = across(dscore, queries) * factor
    value_part = across(prob.astype(jnp.bfloat16), grad_stack)
    pair_all = jnp.concatenate([key_part, value_part], axis=1)
    pair_grad = lax.psum(
        lax.psum_scatter(pair_all, "ctx", scatter_dimension=0, tiled=True), "tp"
    )
    pair_grad = lax.dynamic_slice_in_dim(pair_grad, first_row, rows_mine, 0)

    key_raw = rotate(pair_grad[:, :head_dim], cosine_mine, -sine_mine)
    query_grad = jnp.transpose((query_sum * factor).reshape(heads, rows_mine, head_dim), (1, 0, 2))
    query_raw = rotate(query_grad, cosine_mine[:, None, :], -sine_mine[:, None, :]).reshape(
        rows_mine, heads_width
    )
    d_mine = jnp.concatenate([query_raw, key_raw, pair_grad[:, head_dim:]], axis=1).astype(
        jnp.bfloat16
    )
    d_qkv = lax.all_gather(d_mine, "tp", axis=0, tiled=True)
    grad_x = jnp.dot(d_qkv, w_qkv, preferred_element_type=jnp.float32).astype(jnp.bfloat16)
    joint_weight = across(d_qkv, tokens)
    grad_w_qkv = ring_scatter(joint_weight, ring, "ctx")
    grad_w_out = ring_scatter(out_weight_grad, ring, "ctx")
    return (out, grad_x, grad_w_qkv, grad_w_out)


def solution(mesh):
    return jax.shard_map(
        functools.partial(shards, ring_of(mesh)),
        mesh=mesh,
        in_specs=(P("ctx", "tp"), P("ctx"), P("ctx"), P(None, "tp"), P(None, "tp"), P("ctx", "tp")),
        out_specs=(P("ctx", "tp"), P("ctx", "tp"), P("ctx", "tp"), P("ctx", "tp")),
        check_vma=False,
    )
```

```python
import functools
import math

import jax
import jax.numpy as jnp
from jax import lax
from jax.sharding import PartitionSpec as P

HD = 128
HQ = 8


THETA = 500000.0
NEG = -1e30
PIECE = 64


def angles(place, width):
    half = width // 2
    freq = THETA ** (-(jnp.arange(half, dtype=jnp.float32) * 2.0 / width))
    turn = place.astype(jnp.float32)[:, None] * freq[None, :]
    return (jnp.cos(turn), jnp.sin(turn))


def rotate(vector, cosine, sine):
    half = vector.shape[-1] // 2
    first = vector[..., :half]
    second = vector[..., half:]
    return jnp.concatenate(
        [first * cosine - second * sine, second * cosine + first * sine], axis=-1
    )


def against(left, right):
    return lax.dot_general(
        left, right, (((1,), (1,)), ((), ())), preferred_element_type=jnp.float32
    )


def across(left, right):
    return lax.dot_general(
        left, right, (((0,), (0,)), ((), ())), preferred_element_type=jnp.float32
    )


def ring_of(mesh):
    count = mesh.shape["ctx"]
    try:
        grid = mesh.devices.reshape(count, -1)
        coords = [tuple(grid[i, 0].coords) for i in range(count)]
    except Exception:
        return list(range(count))
    varying = [d for d in range(len(coords[0])) if len({c[d] for c in coords}) > 1]
    if len(varying) == 1:
        return sorted(range(count), key=lambda i: coords[i][varying[0]])
    if len(varying) != 2:
        return list(range(count))
    for short, long in (varying, varying[::-1]):
        levels = sorted({c[short] for c in coords})
        if len(levels) == 2:
            there = sorted(
                (i for i in range(count) if coords[i][short] == levels[0]),
                key=lambda i: coords[i][long],
            )
            back = sorted(
                (i for i in range(count) if coords[i][short] == levels[1]),
                key=lambda i: -coords[i][long],
            )
            return there + back
    return list(range(count))


def ring_scatter(partial, ring, axis):
    count = len(ring)
    where = [0] * count
    for spot, member in enumerate(ring):
        where[member] = spot
    spot = jnp.asarray(where, jnp.int32)[lax.axis_index(axis)]
    order = jnp.asarray(ring, jnp.int32)
    rows = partial.shape[0] // count
    half = partial.shape[1] // 2
    blocks = partial.reshape(count, rows, partial.shape[1])
    left = blocks[:, :, :half]
    right = blocks[:, :, half:]

    def block(side, offset):
        return lax.dynamic_index_in_dim(side, order[(spot + offset) % count], 0, keepdims=False)

    forward = [(ring[p], ring[(p + 1) % count]) for p in range(count)]
    backward = [(ring[p], ring[(p - 1) % count]) for p in range(count)]
    send_left = block(left, count - 1)
    send_right = block(right, 1)
    for step in range(count - 1):
        got_left = lax.ppermute(send_left.astype(jnp.bfloat16), axis, forward)
        got_right = lax.ppermute(send_right.astype(jnp.bfloat16), axis, backward)
        send_left = got_left.astype(jnp.float32) + block(left, 2 * count - step - 2)
        send_right = got_right.astype(jnp.float32) + block(right, step + 2)
    return jnp.concatenate([send_left, send_right], axis=1)


def butterfly_sum(value, axis):
    count = lax.axis_size(axis)
    stride = 1
    while stride < count:
        pairs = [(i, i ^ stride) for i in range(count)]
        value = value + lax.ppermute(value, axis, pairs)
        stride *= 2
    return value


def shards(ring, tokens, document, place, w_qkv, w_out, grad_out):
    rows_ctx, slice_width = tokens.shape
    ctx_size = lax.axis_size("ctx")
    tp_size = lax.axis_size("tp")
    rows_mine = rows_ctx // tp_size
    tp_rank = lax.axis_index("tp")
    head_dim = HD
    heads = HQ
    heads_width = heads * head_dim
    pair_width = 2 * head_dim
    factor = 1.0 / math.sqrt(head_dim)
    first_row = tp_rank * rows_mine
    stacked = heads * rows_mine
    total_rows = ctx_size * rows_ctx

    grad_part = against(grad_out, w_out).astype(jnp.bfloat16)

    cosine_all, sine_all = angles(place, head_dim)
    cosine_mine = lax.dynamic_slice_in_dim(cosine_all, first_row, rows_mine, 0)
    sine_mine = lax.dynamic_slice_in_dim(sine_all, first_row, rows_mine, 0)
    query_doc = lax.dynamic_slice_in_dim(document, first_row, rows_mine, 0)
    query_place = lax.dynamic_slice_in_dim(place, first_row, rows_mine, 0)

    qkv = lax.psum(against(tokens, w_qkv), "tp")
    keys = rotate(qkv[:, heads_width : heads_width + head_dim], cosine_all, sine_all).astype(
        jnp.bfloat16
    )
    values = qkv[:, heads_width + head_dim :].astype(jnp.bfloat16)

    info = jnp.concatenate(
        [document, place // PIECE, place % PIECE], axis=0
    ).astype(jnp.float32)
    info_rows = -(-info.shape[0] // pair_width)
    info = jnp.pad(info, (0, info_rows * pair_width - info.shape[0]))
    info = info.reshape(info_rows, pair_width).astype(jnp.bfloat16)
    packed = jnp.concatenate([keys, values, ], axis=1)
    packed = jnp.concatenate([packed, info], axis=0)
    gathered = lax.all_gather(packed, "ctx", axis=0, tiled=False)
    grad_part, gathered = lax.optimization_barrier((grad_part, gathered))
    grad_rows = lax.psum_scatter(grad_part, "tp", scatter_dimension=0, tiled=True)
    keys_all = gathered[:, :rows_ctx, :head_dim].reshape(total_rows, head_dim)
    values_all = gathered[:, :rows_ctx, head_dim:].reshape(total_rows, head_dim)
    info_all = gathered[:, rows_ctx:, :].reshape(ctx_size, info_rows * pair_width).astype(
        jnp.float32
    )
    key_doc = info_all[:, :rows_ctx].reshape(total_rows)
    key_place = (
        info_all[:, rows_ctx : 2 * rows_ctx] * PIECE + info_all[:, 2 * rows_ctx : 3 * rows_ctx]
    ).reshape(total_rows)

    allowed = (query_doc.astype(jnp.float32)[:, None] == key_doc[None, :]) & (
        key_place[None, :] <= query_place.astype(jnp.float32)[:, None]
    )
    allowed = jnp.broadcast_to(allowed[None], (heads, rows_mine, total_rows)).reshape(
        stacked, total_rows
    )

    mine = lax.dynamic_slice_in_dim(qkv, first_row, rows_mine, 0)
    raw_query = mine[:, :heads_width].reshape(rows_mine, heads, head_dim)
    rotated = rotate(raw_query, cosine_mine[:, None, :], sine_mine[:, None, :]).astype(jnp.bfloat16)
    queries = jnp.transpose(rotated, (1, 0, 2)).reshape(stacked, head_dim)

    scores = against(queries, keys_all) * factor
    masked = jnp.where(allowed, scores, NEG)
    top = jnp.max(masked, axis=1)
    weights = jnp.where(allowed, jnp.exp(masked - top[:, None]), 0.0)
    total = jnp.sum(weights, axis=1)
    summed = jnp.dot(weights.astype(jnp.bfloat16), values_all, preferred_element_type=jnp.float32)
    attended = (summed / total[:, None]).astype(jnp.bfloat16)
    logsum = top + jnp.log(total)

    rows_attended = jnp.transpose(attended.reshape(heads, rows_mine, head_dim), (1, 0, 2)).reshape(
        rows_mine, heads_width
    )
    piece = lax.all_gather(rows_attended, "tp", axis=0, tiled=True)
    out = jnp.dot(piece, w_out, preferred_element_type=jnp.float32).astype(jnp.bfloat16)
    out_weight_grad = across(piece, grad_out)

    grad_stack = jnp.transpose(grad_rows.reshape(rows_mine, heads, head_dim), (1, 0, 2)).reshape(
        stacked, head_dim
    )
    delta = jnp.sum(grad_stack.astype(jnp.float32) * attended.astype(jnp.float32), axis=1)
    prob = jnp.where(allowed, jnp.exp(scores - logsum[:, None]), 0.0)
    dprob = against(grad_stack, values_all)
    dscore = (prob * (dprob - delta[:, None])).astype(jnp.bfloat16)
    query_sum = jnp.dot(dscore, keys_all, preferred_element_type=jnp.float32)
    key_part = across(dscore, queries) * factor
    value_part = across(prob.astype(jnp.bfloat16), grad_stack)
    pair_all = jnp.concatenate([key_part, value_part], axis=1)
    pair_grad = butterfly_sum(ring_scatter(pair_all, ring, "ctx"), "tp")

    key_raw = rotate(pair_grad[:, :head_dim], cosine_all, -sine_all)
    query_grad = jnp.transpose((query_sum * factor).reshape(heads, rows_mine, head_dim), (1, 0, 2))
    query_raw = rotate(query_grad, cosine_mine[:, None, :], -sine_mine[:, None, :]).reshape(
        rows_mine, heads_width
    )
    query_rows = lax.all_gather(query_raw.astype(jnp.bfloat16), "tp", axis=0, tiled=True)
    d_qkv = jnp.concatenate(
        [query_rows, key_raw.astype(jnp.bfloat16), pair_grad[:, head_dim:].astype(jnp.bfloat16)],
        axis=1,
    )
    grad_x = jnp.dot(d_qkv, w_qkv, preferred_element_type=jnp.float32).astype(jnp.bfloat16)
    joint_weight = across(d_qkv, tokens)
    grad_w_qkv = ring_scatter(joint_weight, ring, "ctx")
    grad_w_out = ring_scatter(out_weight_grad, ring, "ctx")
    return (out, grad_x, grad_w_qkv, grad_w_out)


def solution(mesh):
    return jax.shard_map(
        functools.partial(shards, ring_of(mesh)),
        mesh=mesh,
        in_specs=(P("ctx", "tp"), P("ctx"), P("ctx"), P(None, "tp"), P(None, "tp"), P("ctx", "tp")),
        out_specs=(P("ctx", "tp"), P("ctx", "tp"), P("ctx", "tp"), P("ctx", "tp")),
        check_vma=False,
    )
```

```python
import functools
import math

import jax
import jax.numpy as jnp
from jax import lax
from jax.sharding import PartitionSpec as P

HD = 128
HQ = 8


THETA = 500000.0
NEG = -1e30
PIECE = 64


def angles(place, width):
    half = width // 2
    freq = THETA ** (-(jnp.arange(half, dtype=jnp.float32) * 2.0 / width))
    turn = place.astype(jnp.float32)[:, None] * freq[None, :]
    return (jnp.cos(turn), jnp.sin(turn))


def rotate(vector, cosine, sine):
    half = vector.shape[-1] // 2
    first = vector[..., :half]
    second = vector[..., half:]
    return jnp.concatenate(
        [first * cosine - second * sine, second * cosine + first * sine], axis=-1
    )


def against(left, right):
    return lax.dot_general(
        left, right, (((1,), (1,)), ((), ())), preferred_element_type=jnp.float32
    )


def across(left, right):
    return lax.dot_general(
        left, right, (((0,), (0,)), ((), ())), preferred_element_type=jnp.float32
    )


def ring_of(mesh):
    count = mesh.shape["ctx"]
    try:
        grid = mesh.devices.reshape(count, -1)
        coords = [tuple(grid[i, 0].coords) for i in range(count)]
    except Exception:
        return list(range(count))
    varying = [d for d in range(len(coords[0])) if len({c[d] for c in coords}) > 1]
    if len(varying) == 1:
        return sorted(range(count), key=lambda i: coords[i][varying[0]])
    if len(varying) != 2:
        return list(range(count))
    for short, long in (varying, varying[::-1]):
        levels = sorted({c[short] for c in coords})
        if len(levels) == 2:
            there = sorted(
                (i for i in range(count) if coords[i][short] == levels[0]),
                key=lambda i: coords[i][long],
            )
            back = sorted(
                (i for i in range(count) if coords[i][short] == levels[1]),
                key=lambda i: -coords[i][long],
            )
            return there + back
    return list(range(count))


class Ring:
    def __init__(self, partial, ring, axis):
        count = len(ring)
        where = [0] * count
        for spot, member in enumerate(ring):
            where[member] = spot
        self.count = count
        self.axis = axis
        self.spot = jnp.asarray(where, jnp.int32)[lax.axis_index(axis)]
        self.order = jnp.asarray(ring, jnp.int32)
        rows = partial.shape[0] // count
        half = partial.shape[1] // 2
        blocks = partial.reshape(count, rows, partial.shape[1])
        self.left = blocks[:, :, :half]
        self.right = blocks[:, :, half:]
        self.forward = [(ring[p], ring[(p + 1) % count]) for p in range(count)]
        self.backward = [(ring[p], ring[(p - 1) % count]) for p in range(count)]
        self.state = (self.block(self.left, count - 1), self.block(self.right, 1))
        self.done = 0

    def block(self, side, offset):
        index = self.order[(self.spot + offset) % self.count]
        return lax.dynamic_index_in_dim(side, index, 0, keepdims=False)

    def advance(self, upto):
        count = self.count
        send_left, send_right = self.state
        for step in range(self.done, min(upto, count - 1)):
            got_left = lax.ppermute(send_left.astype(jnp.bfloat16), self.axis, self.forward)
            got_right = lax.ppermute(send_right.astype(jnp.bfloat16), self.axis, self.backward)
            send_left = got_left.astype(jnp.float32) + self.block(self.left, 2 * count - step - 2)
            send_right = got_right.astype(jnp.float32) + self.block(self.right, step + 2)
            self.done = step + 1
        self.state = (send_left, send_right)
        return self

    def result(self):
        self.advance(self.count - 1)
        return jnp.concatenate(list(self.state), axis=1)


def ring_scatter(partial, ring, axis):
    return Ring(partial, ring, axis).result()

def butterfly_sum(value, axis):
    count = lax.axis_size(axis)
    stride = 1
    while stride < count:
        pairs = [(i, i ^ stride) for i in range(count)]
        value = value + lax.ppermute(value, axis, pairs)
        stride *= 2
    return value


def shards(ring, tokens, document, place, w_qkv, w_out, grad_out):
    rows_ctx, slice_width = tokens.shape
    ctx_size = lax.axis_size("ctx")
    tp_size = lax.axis_size("tp")
    rows_mine = rows_ctx // tp_size
    tp_rank = lax.axis_index("tp")
    head_dim = HD
    heads = HQ
    heads_width = heads * head_dim
    pair_width = 2 * head_dim
    factor = 1.0 / math.sqrt(head_dim)
    first_row = tp_rank * rows_mine
    stacked = heads * rows_mine
    total_rows = ctx_size * rows_ctx

    grad_part = against(grad_out, w_out).astype(jnp.bfloat16)

    cosine_all, sine_all = angles(place, head_dim)
    cosine_mine = lax.dynamic_slice_in_dim(cosine_all, first_row, rows_mine, 0)
    sine_mine = lax.dynamic_slice_in_dim(sine_all, first_row, rows_mine, 0)
    query_doc = lax.dynamic_slice_in_dim(document, first_row, rows_mine, 0)
    query_place = lax.dynamic_slice_in_dim(place, first_row, rows_mine, 0)

    qkv = lax.psum(against(tokens, w_qkv), "tp")
    keys = rotate(qkv[:, heads_width : heads_width + head_dim], cosine_all, sine_all).astype(
        jnp.bfloat16
    )
    values = qkv[:, heads_width + head_dim :].astype(jnp.bfloat16)

    info = jnp.concatenate(
        [document, place // PIECE, place % PIECE], axis=0
    ).astype(jnp.float32)
    info_rows = -(-info.shape[0] // pair_width)
    info = jnp.pad(info, (0, info_rows * pair_width - info.shape[0]))
    info = info.reshape(info_rows, pair_width).astype(jnp.bfloat16)
    packed = jnp.concatenate([keys, values, ], axis=1)
    packed = jnp.concatenate([packed, info], axis=0)
    gathered = lax.all_gather(packed, "ctx", axis=0, tiled=False)
    grad_part, gathered = lax.optimization_barrier((grad_part, gathered))
    grad_rows = lax.psum_scatter(grad_part, "tp", scatter_dimension=0, tiled=True)
    keys_all = gathered[:, :rows_ctx, :head_dim].reshape(total_rows, head_dim)
    values_all = gathered[:, :rows_ctx, head_dim:].reshape(total_rows, head_dim)
    info_all = gathered[:, rows_ctx:, :].reshape(ctx_size, info_rows * pair_width).astype(
        jnp.float32
    )
    key_doc = info_all[:, :rows_ctx].reshape(total_rows)
    key_place = (
        info_all[:, rows_ctx : 2 * rows_ctx] * PIECE + info_all[:, 2 * rows_ctx : 3 * rows_ctx]
    ).reshape(total_rows)

    allowed = (query_doc.astype(jnp.float32)[:, None] == key_doc[None, :]) & (
        key_place[None, :] <= query_place.astype(jnp.float32)[:, None]
    )
    allowed = jnp.broadcast_to(allowed[None], (heads, rows_mine, total_rows)).reshape(
        stacked, total_rows
    )

    mine = lax.dynamic_slice_in_dim(qkv, first_row, rows_mine, 0)
    raw_query = mine[:, :heads_width].reshape(rows_mine, heads, head_dim)
    rotated = rotate(raw_query, cosine_mine[:, None, :], sine_mine[:, None, :]).astype(jnp.bfloat16)
    queries = jnp.transpose(rotated, (1, 0, 2)).reshape(stacked, head_dim)

    scores = against(queries, keys_all) * factor
    masked = jnp.where(allowed, scores, NEG)
    top = jnp.max(masked, axis=1)
    weights = jnp.where(allowed, jnp.exp(masked - top[:, None]), 0.0)
    total = jnp.sum(weights, axis=1)
    summed = jnp.dot(weights.astype(jnp.bfloat16), values_all, preferred_element_type=jnp.float32)
    attended = (summed / total[:, None]).astype(jnp.bfloat16)
    logsum = top + jnp.log(total)

    rows_attended = jnp.transpose(attended.reshape(heads, rows_mine, head_dim), (1, 0, 2)).reshape(
        rows_mine, heads_width
    )
    piece = lax.all_gather(rows_attended, "tp", axis=0, tiled=True)
    out = jnp.dot(piece, w_out, preferred_element_type=jnp.float32).astype(jnp.bfloat16)
    out_weight_grad = across(piece, grad_out)

    grad_stack = jnp.transpose(grad_rows.reshape(rows_mine, heads, head_dim), (1, 0, 2)).reshape(
        stacked, head_dim
    )
    delta = jnp.sum(grad_stack.astype(jnp.float32) * attended.astype(jnp.float32), axis=1)
    prob = jnp.where(allowed, jnp.exp(scores - logsum[:, None]), 0.0)
    dprob = against(grad_stack, values_all)
    dscore = (prob * (dprob - delta[:, None])).astype(jnp.bfloat16)
    query_sum = jnp.dot(dscore, keys_all, preferred_element_type=jnp.float32)
    key_part = across(dscore, queries) * factor
    value_part = across(prob.astype(jnp.bfloat16), grad_stack)
    pair_all = jnp.concatenate([key_part, value_part], axis=1)
    out_ring = Ring(out_weight_grad, ring, "ctx").advance(len(ring) // 2 - 1)
    out_ring.state, pair_all = lax.optimization_barrier((out_ring.state, pair_all))
    pair_grad = butterfly_sum(ring_scatter(pair_all, ring, "ctx"), "tp")
    out_ring.advance(len(ring) - 1)
    out_ring.state, pair_grad = lax.optimization_barrier((out_ring.state, pair_grad))

    key_raw = rotate(pair_grad[:, :head_dim], cosine_all, -sine_all)
    query_grad = jnp.transpose((query_sum * factor).reshape(heads, rows_mine, head_dim), (1, 0, 2))
    query_raw = rotate(query_grad, cosine_mine[:, None, :], -sine_mine[:, None, :]).reshape(
        rows_mine, heads_width
    )
    query_rows = lax.all_gather(query_raw.astype(jnp.bfloat16), "tp", axis=0, tiled=True)
    d_qkv = jnp.concatenate(
        [query_rows, key_raw.astype(jnp.bfloat16), pair_grad[:, head_dim:].astype(jnp.bfloat16)],
        axis=1,
    )
    grad_x = jnp.dot(d_qkv, w_qkv, preferred_element_type=jnp.float32).astype(jnp.bfloat16)
    joint_weight = across(d_qkv, tokens)
    grad_w_qkv = ring_scatter(joint_weight, ring, "ctx")
    grad_w_out = out_ring.result()
    return (out, grad_x, grad_w_qkv, grad_w_out)


def solution(mesh):
    return jax.shard_map(
        functools.partial(shards, ring_of(mesh)),
        mesh=mesh,
        in_specs=(P("ctx", "tp"), P("ctx"), P("ctx"), P(None, "tp"), P(None, "tp"), P("ctx", "tp")),
        out_specs=(P("ctx", "tp"), P("ctx", "tp"), P("ctx", "tp"), P("ctx", "tp")),
        check_vma=False,
    )
```

```python
import functools
import math

import jax
import jax.numpy as jnp
from jax import lax
from jax.sharding import PartitionSpec as P

HD = 128
HQ = 8


THETA = 500000.0
NEG = -1e30
PIECE = 64


def angles(place, width):
    half = width // 2
    freq = THETA ** (-(jnp.arange(half, dtype=jnp.float32) * 2.0 / width))
    turn = place.astype(jnp.float32)[:, None] * freq[None, :]
    return (jnp.cos(turn), jnp.sin(turn))


def rotate(vector, cosine, sine):
    half = vector.shape[-1] // 2
    first = vector[..., :half]
    second = vector[..., half:]
    return jnp.concatenate(
        [first * cosine - second * sine, second * cosine + first * sine], axis=-1
    )


def against(left, right):
    return lax.dot_general(
        left, right, (((1,), (1,)), ((), ())), preferred_element_type=jnp.float32
    )


def across(left, right):
    return lax.dot_general(
        left, right, (((0,), (0,)), ((), ())), preferred_element_type=jnp.float32
    )


def ring_of(mesh):
    count = mesh.shape["ctx"]
    try:
        grid = mesh.devices.reshape(count, -1)
        coords = [tuple(grid[i, 0].coords) for i in range(count)]
    except Exception:
        return list(range(count))
    varying = [d for d in range(len(coords[0])) if len({c[d] for c in coords}) > 1]
    if len(varying) == 1:
        return sorted(range(count), key=lambda i: coords[i][varying[0]])
    if len(varying) != 2:
        return list(range(count))
    for short, long in (varying, varying[::-1]):
        levels = sorted({c[short] for c in coords})
        if len(levels) == 2:
            there = sorted(
                (i for i in range(count) if coords[i][short] == levels[0]),
                key=lambda i: coords[i][long],
            )
            back = sorted(
                (i for i in range(count) if coords[i][short] == levels[1]),
                key=lambda i: -coords[i][long],
            )
            return there + back
    return list(range(count))


def ring_scatter(partial, ring, axis):
    count = len(ring)
    where = [0] * count
    for spot, member in enumerate(ring):
        where[member] = spot
    spot = jnp.asarray(where, jnp.int32)[lax.axis_index(axis)]
    order = jnp.asarray(ring, jnp.int32)
    rows = partial.shape[0] // count
    half = partial.shape[1] // 2
    blocks = partial.reshape(count, rows, partial.shape[1])
    left = blocks[:, :, :half]
    right = blocks[:, :, half:]

    def block(side, offset):
        return lax.dynamic_index_in_dim(side, order[(spot + offset) % count], 0, keepdims=False)

    forward = [(ring[p], ring[(p + 1) % count]) for p in range(count)]
    backward = [(ring[p], ring[(p - 1) % count]) for p in range(count)]
    send_left = block(left, count - 1)
    send_right = block(right, 1)
    for step in range(count - 1):
        got_left = lax.ppermute(send_left.astype(jnp.bfloat16), axis, forward)
        got_right = lax.ppermute(send_right.astype(jnp.bfloat16), axis, backward)
        send_left = got_left.astype(jnp.float32) + block(left, 2 * count - step - 2)
        send_right = got_right.astype(jnp.float32) + block(right, step + 2)
    return jnp.concatenate([send_left, send_right], axis=1)


def ring_spot(ring, axis):
    where = [0] * len(ring)
    for spot, member in enumerate(ring):
        where[member] = spot
    return jnp.asarray(where, jnp.int32)[lax.axis_index(axis)]


def ring_gather(value, ring, axis):
    count = len(ring)
    forward = [(ring[p], ring[(p + 1) % count]) for p in range(count)]
    backward = [(ring[p], ring[(p - 1) % count]) for p in range(count)]
    ahead = count // 2
    behind = count - 1 - ahead
    got = [value] + [None] * (count - 1)
    from_left = value
    from_right = value
    for step in range(max(ahead, behind)):
        if step < ahead:
            from_left = lax.ppermute(from_left, axis, forward)
            got[count - step - 1] = from_left
        if step < behind:
            from_right = lax.ppermute(from_right, axis, backward)
            got[step + 1] = from_right
    return jnp.stack(got, axis=0)


def ring_scatter_relative(partial, ring, axis):
    count = len(ring)
    rows = partial.shape[0] // count
    half = partial.shape[1] // 2
    blocks = partial.reshape(count, rows, partial.shape[1])
    left = blocks[:, :, :half]
    right = blocks[:, :, half:]
    forward = [(ring[p], ring[(p + 1) % count]) for p in range(count)]
    backward = [(ring[p], ring[(p - 1) % count]) for p in range(count)]
    send_left = left[count - 1]
    send_right = right[1 % count]
    for step in range(count - 1):
        got_left = lax.ppermute(send_left.astype(jnp.bfloat16), axis, forward)
        got_right = lax.ppermute(send_right.astype(jnp.bfloat16), axis, backward)
        send_left = got_left.astype(jnp.float32) + left[(2 * count - step - 2) % count]
        send_right = got_right.astype(jnp.float32) + right[(step + 2) % count]
    return jnp.concatenate([send_left, send_right], axis=1)


def tp_project(partial, rows_mine, split, axis):
    rank = lax.axis_index(axis)
    core = rank % 2
    near = [(i, i ^ 1) for i in range(4)]
    far = [(i, i ^ 2) for i in range(4)]
    chip = partial + lax.ppermute(partial, axis, near)
    head = chip[:, :split]
    tail = chip[:, split:]
    half_rows = tail.shape[0] // 2
    mine = lax.dynamic_slice_in_dim(head, rank * rows_mine, rows_mine, 0)
    theirs = lax.dynamic_slice_in_dim(head, (rank ^ 2) * rows_mine, rows_mine, 0)
    own_head = mine + lax.ppermute(theirs, axis, far)
    tail_half = lax.dynamic_slice_in_dim(tail, core * half_rows, half_rows, 0)
    tail_half = tail_half + lax.ppermute(tail_half, axis, far)
    other_half = lax.ppermute(tail_half, axis, near)
    first = jnp.where(core == 0, tail_half, other_half)
    second = jnp.where(core == 0, other_half, tail_half)
    return own_head, jnp.concatenate([first, second], axis=0)


def butterfly_sum(value, axis):
    count = lax.axis_size(axis)
    stride = 1
    while stride < count:
        pairs = [(i, i ^ stride) for i in range(count)]
        value = value + lax.ppermute(value, axis, pairs)
        stride *= 2
    return value


def shards(ring, tokens, document, place, w_qkv, w_out, grad_out):
    rows_ctx, slice_width = tokens.shape
    ctx_size = lax.axis_size("ctx")
    tp_size = lax.axis_size("tp")
    rows_mine = rows_ctx // tp_size
    tp_rank = lax.axis_index("tp")
    head_dim = HD
    heads = HQ
    heads_width = heads * head_dim
    pair_width = 2 * head_dim
    factor = 1.0 / math.sqrt(head_dim)
    first_row = tp_rank * rows_mine
    stacked = heads * rows_mine
    total_rows = ctx_size * rows_ctx

    grad_part = against(grad_out, w_out).astype(jnp.bfloat16)

    cosine_all, sine_all = angles(place, head_dim)
    cosine_mine = lax.dynamic_slice_in_dim(cosine_all, first_row, rows_mine, 0)
    sine_mine = lax.dynamic_slice_in_dim(sine_all, first_row, rows_mine, 0)
    query_doc = lax.dynamic_slice_in_dim(document, first_row, rows_mine, 0)
    query_place = lax.dynamic_slice_in_dim(place, first_row, rows_mine, 0)

    projected = against(tokens, w_qkv)
    if tp_size == 4 and rows_ctx % (2 * tp_size) == 0:
        query_block, pair_rows = tp_project(projected, rows_mine, heads_width, "tp")
    else:
        qkv = lax.psum(projected, "tp")
        query_block = lax.dynamic_slice_in_dim(qkv[:, :heads_width], first_row, rows_mine, 0)
        pair_rows = qkv[:, heads_width:]
    keys = rotate(pair_rows[:, :head_dim], cosine_all, sine_all).astype(jnp.bfloat16)
    values = pair_rows[:, head_dim:].astype(jnp.bfloat16)

    info = jnp.concatenate(
        [document, place // PIECE, place % PIECE], axis=0
    ).astype(jnp.float32)
    info_rows = -(-info.shape[0] // pair_width)
    info = jnp.pad(info, (0, info_rows * pair_width - info.shape[0]))
    info = info.reshape(info_rows, pair_width).astype(jnp.bfloat16)
    packed = jnp.concatenate([keys, values], axis=1)
    packed = jnp.concatenate([packed, info], axis=0)
    gathered = ring_gather(packed, ring, "ctx")
    grad_rows = lax.psum_scatter(grad_part, "tp", scatter_dimension=0, tiled=True)
    keys_all = gathered[:, :rows_ctx, :head_dim].reshape(total_rows, head_dim)
    values_all = gathered[:, :rows_ctx, head_dim:].reshape(total_rows, head_dim)
    info_all = gathered[:, rows_ctx:, :].reshape(ctx_size, info_rows * pair_width).astype(
        jnp.float32
    )
    key_doc = info_all[:, :rows_ctx].reshape(total_rows)
    key_place = (
        info_all[:, rows_ctx : 2 * rows_ctx] * PIECE + info_all[:, 2 * rows_ctx : 3 * rows_ctx]
    ).reshape(total_rows)

    allowed = (query_doc.astype(jnp.float32)[:, None] == key_doc[None, :]) & (
        key_place[None, :] <= query_place.astype(jnp.float32)[:, None]
    )
    allowed = jnp.broadcast_to(allowed[None], (heads, rows_mine, total_rows)).reshape(
        stacked, total_rows
    )

    raw_query = query_block.reshape(rows_mine, heads, head_dim)
    rotated = rotate(raw_query, cosine_mine[:, None, :], sine_mine[:, None, :]).astype(jnp.bfloat16)
    queries = jnp.transpose(rotated, (1, 0, 2)).reshape(stacked, head_dim)

    scores = against(queries, keys_all) * factor
    masked = jnp.where(allowed, scores, NEG)
    top = jnp.max(masked, axis=1)
    weights = jnp.where(allowed, jnp.exp(masked - top[:, None]), 0.0)
    total = jnp.sum(weights, axis=1)
    summed = jnp.dot(weights.astype(jnp.bfloat16), values_all, preferred_element_type=jnp.float32)
    attended = (summed / total[:, None]).astype(jnp.bfloat16)
    logsum = top + jnp.log(total)

    rows_attended = jnp.transpose(attended.reshape(heads, rows_mine, head_dim), (1, 0, 2)).reshape(
        rows_mine, heads_width
    )
    piece = lax.all_gather(rows_attended, "tp", axis=0, tiled=True)
    out = jnp.dot(piece, w_out, preferred_element_type=jnp.float32).astype(jnp.bfloat16)
    out_weight_grad = across(piece, grad_out)

    grad_stack = jnp.transpose(grad_rows.reshape(rows_mine, heads, head_dim), (1, 0, 2)).reshape(
        stacked, head_dim
    )
    delta = jnp.sum(grad_stack.astype(jnp.float32) * attended.astype(jnp.float32), axis=1)
    prob = jnp.where(allowed, jnp.exp(scores - logsum[:, None]), 0.0)
    dprob = against(grad_stack, values_all)
    dscore = (prob * (dprob - delta[:, None])).astype(jnp.bfloat16)
    query_sum = jnp.dot(dscore, keys_all, preferred_element_type=jnp.float32)
    key_part = across(dscore, queries) * factor
    value_part = across(prob.astype(jnp.bfloat16), grad_stack)
    pair_all = jnp.concatenate([key_part, value_part], axis=1)
    pair_grad = butterfly_sum(ring_scatter_relative(pair_all, ring, "ctx"), "tp")

    key_raw = rotate(pair_grad[:, :head_dim], cosine_all, -sine_all)
    query_grad = jnp.transpose((query_sum * factor).reshape(heads, rows_mine, head_dim), (1, 0, 2))
    query_raw = rotate(query_grad, cosine_mine[:, None, :], -sine_mine[:, None, :]).reshape(
        rows_mine, heads_width
    )
    query_rows = lax.all_gather(query_raw.astype(jnp.bfloat16), "tp", axis=0, tiled=True)
    d_qkv = jnp.concatenate(
        [query_rows, key_raw.astype(jnp.bfloat16), pair_grad[:, head_dim:].astype(jnp.bfloat16)],
        axis=1,
    )
    grad_x = jnp.dot(d_qkv, w_qkv, preferred_element_type=jnp.float32).astype(jnp.bfloat16)
    joint_weight = across(d_qkv, tokens)
    grad_w_qkv = ring_scatter(joint_weight, ring, "ctx")
    grad_w_out = ring_scatter(out_weight_grad, ring, "ctx")
    return (out, grad_x, grad_w_qkv, grad_w_out)


def solution(mesh):
    return jax.shard_map(
        functools.partial(shards, ring_of(mesh)),
        mesh=mesh,
        in_specs=(P("ctx", "tp"), P("ctx"), P("ctx"), P(None, "tp"), P(None, "tp"), P("ctx", "tp")),
        out_specs=(P("ctx", "tp"), P("ctx", "tp"), P("ctx", "tp"), P("ctx", "tp")),
        check_vma=False,
    )
```

```python
import functools
import math

import jax
import jax.numpy as jnp
from jax import lax
from jax.sharding import PartitionSpec as P

HD = 128
HQ = 8


THETA = 500000.0
NEG = -1e30
PIECE = 64


def angles(place, width):
    half = width // 2
    freq = THETA ** (-(jnp.arange(half, dtype=jnp.float32) * 2.0 / width))
    turn = place.astype(jnp.float32)[:, None] * freq[None, :]
    return (jnp.cos(turn), jnp.sin(turn))


def rotate(vector, cosine, sine):
    half = vector.shape[-1] // 2
    first = vector[..., :half]
    second = vector[..., half:]
    return jnp.concatenate(
        [first * cosine - second * sine, second * cosine + first * sine], axis=-1
    )


def against(left, right):
    return lax.dot_general(
        left, right, (((1,), (1,)), ((), ())), preferred_element_type=jnp.float32
    )


def across(left, right):
    return lax.dot_general(
        left, right, (((0,), (0,)), ((), ())), preferred_element_type=jnp.float32
    )


def ring_of(mesh):
    count = mesh.shape["ctx"]
    try:
        grid = mesh.devices.reshape(count, -1)
        coords = [tuple(grid[i, 0].coords) for i in range(count)]
    except Exception:
        return list(range(count))
    varying = [d for d in range(len(coords[0])) if len({c[d] for c in coords}) > 1]
    if len(varying) == 1:
        return sorted(range(count), key=lambda i: coords[i][varying[0]])
    if len(varying) != 2:
        return list(range(count))
    for short, long in (varying, varying[::-1]):
        levels = sorted({c[short] for c in coords})
        if len(levels) == 2:
            there = sorted(
                (i for i in range(count) if coords[i][short] == levels[0]),
                key=lambda i: coords[i][long],
            )
            back = sorted(
                (i for i in range(count) if coords[i][short] == levels[1]),
                key=lambda i: -coords[i][long],
            )
            return there + back
    return list(range(count))


def ring_scatter(partial, ring, axis):
    count = len(ring)
    where = [0] * count
    for spot, member in enumerate(ring):
        where[member] = spot
    spot = jnp.asarray(where, jnp.int32)[lax.axis_index(axis)]
    order = jnp.asarray(ring, jnp.int32)
    rows = partial.shape[0] // count
    half = partial.shape[1] // 2
    blocks = partial.reshape(count, rows, partial.shape[1])
    left = blocks[:, :, :half]
    right = blocks[:, :, half:]

    def block(side, offset):
        return lax.dynamic_index_in_dim(side, order[(spot + offset) % count], 0, keepdims=False)

    forward = [(ring[p], ring[(p + 1) % count]) for p in range(count)]
    backward = [(ring[p], ring[(p - 1) % count]) for p in range(count)]
    send_left = block(left, count - 1)
    send_right = block(right, 1)
    for step in range(count - 1):
        got_left = lax.ppermute(send_left.astype(jnp.bfloat16), axis, forward)
        got_right = lax.ppermute(send_right.astype(jnp.bfloat16), axis, backward)
        send_left = got_left.astype(jnp.float32) + block(left, 2 * count - step - 2)
        send_right = got_right.astype(jnp.float32) + block(right, step + 2)
    return jnp.concatenate([send_left, send_right], axis=1)


def ring_spot(ring, axis):
    where = [0] * len(ring)
    for spot, member in enumerate(ring):
        where[member] = spot
    return jnp.asarray(where, jnp.int32)[lax.axis_index(axis)]


def ring_gather(value, ring, axis):
    count = len(ring)
    forward = [(ring[p], ring[(p + 1) % count]) for p in range(count)]
    backward = [(ring[p], ring[(p - 1) % count]) for p in range(count)]
    ahead = count // 2
    behind = count - 1 - ahead
    got = [value] + [None] * (count - 1)
    from_left = value
    from_right = value
    for step in range(max(ahead, behind)):
        if step < ahead:
            from_left = lax.ppermute(from_left, axis, forward)
            got[count - step - 1] = from_left
        if step < behind:
            from_right = lax.ppermute(from_right, axis, backward)
            got[step + 1] = from_right
    return jnp.stack(got, axis=0)


def ring_scatter_relative(partial, ring, axis):
    count = len(ring)
    rows = partial.shape[0] // count
    half = partial.shape[1] // 2
    blocks = partial.reshape(count, rows, partial.shape[1])
    left = blocks[:, :, :half]
    right = blocks[:, :, half:]
    forward = [(ring[p], ring[(p + 1) % count]) for p in range(count)]
    backward = [(ring[p], ring[(p - 1) % count]) for p in range(count)]
    send_left = left[count - 1]
    send_right = right[1 % count]
    for step in range(count - 1):
        got_left = lax.ppermute(send_left.astype(jnp.bfloat16), axis, forward)
        got_right = lax.ppermute(send_right.astype(jnp.bfloat16), axis, backward)
        send_left = got_left.astype(jnp.float32) + left[(2 * count - step - 2) % count]
        send_right = got_right.astype(jnp.float32) + right[(step + 2) % count]
    return jnp.concatenate([send_left, send_right], axis=1)


def tp_project(partial, rows_mine, split, axis):
    rank = lax.axis_index(axis)
    core = rank % 2
    near = [(i, i ^ 1) for i in range(4)]
    far = [(i, i ^ 2) for i in range(4)]
    chip = partial + lax.ppermute(partial, axis, near)
    head = chip[:, :split]
    tail = chip[:, split:]
    half_rows = tail.shape[0] // 2
    mine = lax.dynamic_slice_in_dim(head, rank * rows_mine, rows_mine, 0)
    theirs = lax.dynamic_slice_in_dim(head, (rank ^ 2) * rows_mine, rows_mine, 0)
    own_head = mine + lax.ppermute(theirs, axis, far)
    tail_half = lax.dynamic_slice_in_dim(tail, core * half_rows, half_rows, 0)
    tail_half = tail_half + lax.ppermute(tail_half, axis, far)
    other_half = lax.ppermute(tail_half, axis, near)
    first = jnp.where(core == 0, tail_half, other_half)
    second = jnp.where(core == 0, other_half, tail_half)
    return own_head, jnp.concatenate([first, second], axis=0)


def tp_scatter(partial, rows_mine, axis):
    rank = lax.axis_index(axis)
    far = [(i, i ^ 2) for i in range(4)]
    near = [(i, i ^ 1) for i in range(4)]
    pair_rows = 2 * rows_mine
    chip = rank // 2
    kept = lax.dynamic_slice_in_dim(partial, chip * pair_rows, pair_rows, 0)
    sent = lax.dynamic_slice_in_dim(partial, (1 - chip) * pair_rows, pair_rows, 0)
    kept = kept.astype(jnp.float32) + lax.ppermute(
        sent.astype(jnp.bfloat16), axis, far
    ).astype(jnp.float32)
    core = rank % 2
    mine = lax.dynamic_slice_in_dim(kept, core * rows_mine, rows_mine, 0)
    other = lax.dynamic_slice_in_dim(kept, (1 - core) * rows_mine, rows_mine, 0)
    return mine + lax.ppermute(other.astype(jnp.bfloat16), axis, near).astype(jnp.float32)


def butterfly_sum(value, axis):
    count = lax.axis_size(axis)
    stride = 1
    while stride < count:
        pairs = [(i, i ^ stride) for i in range(count)]
        value = value + lax.ppermute(value, axis, pairs)
        stride *= 2
    return value


def shards(ring, tokens, document, place, w_qkv, w_out, grad_out):
    rows_ctx, slice_width = tokens.shape
    ctx_size = lax.axis_size("ctx")
    tp_size = lax.axis_size("tp")
    rows_mine = rows_ctx // tp_size
    tp_rank = lax.axis_index("tp")
    head_dim = HD
    heads = HQ
    heads_width = heads * head_dim
    pair_width = 2 * head_dim
    factor = 1.0 / math.sqrt(head_dim)
    first_row = tp_rank * rows_mine
    stacked = heads * rows_mine
    total_rows = ctx_size * rows_ctx

    grad_part = against(grad_out, w_out).astype(jnp.bfloat16)

    cosine_all, sine_all = angles(place, head_dim)
    cosine_mine = lax.dynamic_slice_in_dim(cosine_all, first_row, rows_mine, 0)
    sine_mine = lax.dynamic_slice_in_dim(sine_all, first_row, rows_mine, 0)
    query_doc = lax.dynamic_slice_in_dim(document, first_row, rows_mine, 0)
    query_place = lax.dynamic_slice_in_dim(place, first_row, rows_mine, 0)

    projected = against(tokens, w_qkv)
    if tp_size == 4 and rows_ctx % (2 * tp_size) == 0:
        query_block, pair_rows = tp_project(projected, rows_mine, heads_width, "tp")
    else:
        qkv = lax.psum(projected, "tp")
        query_block = lax.dynamic_slice_in_dim(qkv[:, :heads_width], first_row, rows_mine, 0)
        pair_rows = qkv[:, heads_width:]
    keys = rotate(pair_rows[:, :head_dim], cosine_all, sine_all).astype(jnp.bfloat16)
    values = pair_rows[:, head_dim:].astype(jnp.bfloat16)

    info = jnp.concatenate(
        [document, place // PIECE, place % PIECE], axis=0
    ).astype(jnp.float32)
    info_rows = -(-info.shape[0] // pair_width)
    info = jnp.pad(info, (0, info_rows * pair_width - info.shape[0]))
    info = info.reshape(info_rows, pair_width).astype(jnp.bfloat16)
    packed = jnp.concatenate([keys, values], axis=1)
    packed = jnp.concatenate([packed, info], axis=0)
    gathered = ring_gather(packed, ring, "ctx")
    if tp_size == 4 and rows_ctx % (2 * tp_size) == 0:
        grad_rows = tp_scatter(grad_part, rows_mine, "tp").astype(jnp.bfloat16)
    else:
        grad_rows = lax.psum_scatter(grad_part, "tp", scatter_dimension=0, tiled=True)
    keys_all = gathered[:, :rows_ctx, :head_dim].reshape(total_rows, head_dim)
    values_all = gathered[:, :rows_ctx, head_dim:].reshape(total_rows, head_dim)
    info_all = gathered[:, rows_ctx:, :].reshape(ctx_size, info_rows * pair_width).astype(
        jnp.float32
    )
    key_doc = info_all[:, :rows_ctx].reshape(total_rows)
    key_place = (
        info_all[:, rows_ctx : 2 * rows_ctx] * PIECE + info_all[:, 2 * rows_ctx : 3 * rows_ctx]
    ).reshape(total_rows)

    allowed = (query_doc.astype(jnp.float32)[:, None] == key_doc[None, :]) & (
        key_place[None, :] <= query_place.astype(jnp.float32)[:, None]
    )
    allowed = jnp.broadcast_to(allowed[None], (heads, rows_mine, total_rows)).reshape(
        stacked, total_rows
    )

    raw_query = query_block.reshape(rows_mine, heads, head_dim)
    rotated = rotate(raw_query, cosine_mine[:, None, :], sine_mine[:, None, :]).astype(jnp.bfloat16)
    queries = jnp.transpose(rotated, (1, 0, 2)).reshape(stacked, head_dim)

    scores = against(queries, keys_all) * factor
    masked = jnp.where(allowed, scores, NEG)
    top = jnp.max(masked, axis=1)
    weights = jnp.where(allowed, jnp.exp(masked - top[:, None]), 0.0)
    total = jnp.sum(weights, axis=1)
    summed = jnp.dot(weights.astype(jnp.bfloat16), values_all, preferred_element_type=jnp.float32)
    attended = (summed / total[:, None]).astype(jnp.bfloat16)
    logsum = top + jnp.log(total)

    rows_attended = jnp.transpose(attended.reshape(heads, rows_mine, head_dim), (1, 0, 2)).reshape(
        rows_mine, heads_width
    )
    piece = lax.all_gather(rows_attended, "tp", axis=0, tiled=True)
    out = jnp.dot(piece, w_out, preferred_element_type=jnp.float32).astype(jnp.bfloat16)
    out_weight_grad = across(piece, grad_out)

    grad_stack = jnp.transpose(grad_rows.reshape(rows_mine, heads, head_dim), (1, 0, 2)).reshape(
        stacked, head_dim
    )
    delta = jnp.sum(grad_stack.astype(jnp.float32) * attended.astype(jnp.float32), axis=1)
    prob = jnp.where(allowed, jnp.exp(scores - logsum[:, None]), 0.0)
    dprob = against(grad_stack, values_all)
    dscore = (prob * (dprob - delta[:, None])).astype(jnp.bfloat16)
    query_sum = jnp.dot(dscore, keys_all, preferred_element_type=jnp.float32)
    key_part = across(dscore, queries) * factor
    value_part = across(prob.astype(jnp.bfloat16), grad_stack)
    pair_all = jnp.concatenate([key_part, value_part], axis=1)
    pair_grad = butterfly_sum(ring_scatter_relative(pair_all, ring, "ctx"), "tp")

    key_raw = rotate(pair_grad[:, :head_dim], cosine_all, -sine_all)
    query_grad = jnp.transpose((query_sum * factor).reshape(heads, rows_mine, head_dim), (1, 0, 2))
    query_raw = rotate(query_grad, cosine_mine[:, None, :], -sine_mine[:, None, :]).reshape(
        rows_mine, heads_width
    )
    query_rows = lax.all_gather(query_raw.astype(jnp.bfloat16), "tp", axis=0, tiled=True)
    d_qkv = jnp.concatenate(
        [query_rows, key_raw.astype(jnp.bfloat16), pair_grad[:, head_dim:].astype(jnp.bfloat16)],
        axis=1,
    )
    grad_x = jnp.dot(d_qkv, w_qkv, preferred_element_type=jnp.float32).astype(jnp.bfloat16)
    joint_weight = across(d_qkv, tokens)
    grad_w_qkv = ring_scatter(joint_weight, ring, "ctx")
    grad_w_out = ring_scatter(out_weight_grad, ring, "ctx")
    return (out, grad_x, grad_w_qkv, grad_w_out)


def solution(mesh):
    return jax.shard_map(
        functools.partial(shards, ring_of(mesh)),
        mesh=mesh,
        in_specs=(P("ctx", "tp"), P("ctx"), P("ctx"), P(None, "tp"), P(None, "tp"), P("ctx", "tp")),
        out_specs=(P("ctx", "tp"), P("ctx", "tp"), P("ctx", "tp"), P("ctx", "tp")),
        check_vma=False,
    )
```

```python
import functools
import math

import jax
import jax.numpy as jnp
from jax import lax
from jax.sharding import PartitionSpec as P

HD = 128
HQ = 8


THETA = 500000.0
NEG = -1e30
PIECE = 64


def angles(place, width):
    half = width // 2
    freq = THETA ** (-(jnp.arange(half, dtype=jnp.float32) * 2.0 / width))
    turn = place.astype(jnp.float32)[:, None] * freq[None, :]
    return (jnp.cos(turn), jnp.sin(turn))


def rotate(vector, cosine, sine):
    half = vector.shape[-1] // 2
    first = vector[..., :half]
    second = vector[..., half:]
    return jnp.concatenate(
        [first * cosine - second * sine, second * cosine + first * sine], axis=-1
    )


def against(left, right):
    return lax.dot_general(
        left, right, (((1,), (1,)), ((), ())), preferred_element_type=jnp.float32
    )


def across(left, right):
    return lax.dot_general(
        left, right, (((0,), (0,)), ((), ())), preferred_element_type=jnp.float32
    )


def ring_of(mesh):
    count = mesh.shape["ctx"]
    try:
        grid = mesh.devices.reshape(count, -1)
        coords = [tuple(grid[i, 0].coords) for i in range(count)]
    except Exception:
        return list(range(count))
    varying = [d for d in range(len(coords[0])) if len({c[d] for c in coords}) > 1]
    if len(varying) == 1:
        return sorted(range(count), key=lambda i: coords[i][varying[0]])
    if len(varying) != 2:
        return list(range(count))
    for short, long in (varying, varying[::-1]):
        levels = sorted({c[short] for c in coords})
        if len(levels) == 2:
            there = sorted(
                (i for i in range(count) if coords[i][short] == levels[0]),
                key=lambda i: coords[i][long],
            )
            back = sorted(
                (i for i in range(count) if coords[i][short] == levels[1]),
                key=lambda i: -coords[i][long],
            )
            return there + back
    return list(range(count))


def ring_scatter(partial, ring, axis):
    count = len(ring)
    where = [0] * count
    for spot, member in enumerate(ring):
        where[member] = spot
    spot = jnp.asarray(where, jnp.int32)[lax.axis_index(axis)]
    order = jnp.asarray(ring, jnp.int32)
    rows = partial.shape[0] // count
    half = partial.shape[1] // 2
    blocks = partial.reshape(count, rows, partial.shape[1])
    left = blocks[:, :, :half]
    right = blocks[:, :, half:]

    def block(side, offset):
        return lax.dynamic_index_in_dim(side, order[(spot + offset) % count], 0, keepdims=False)

    forward = [(ring[p], ring[(p + 1) % count]) for p in range(count)]
    backward = [(ring[p], ring[(p - 1) % count]) for p in range(count)]
    send_left = block(left, count - 1)
    send_right = block(right, 1)
    for step in range(count - 1):
        got_left = lax.ppermute(send_left.astype(jnp.bfloat16), axis, forward)
        got_right = lax.ppermute(send_right.astype(jnp.bfloat16), axis, backward)
        send_left = got_left.astype(jnp.float32) + block(left, 2 * count - step - 2)
        send_right = got_right.astype(jnp.float32) + block(right, step + 2)
    return jnp.concatenate([send_left, send_right], axis=1)


def ring_spot(ring, axis):
    where = [0] * len(ring)
    for spot, member in enumerate(ring):
        where[member] = spot
    return jnp.asarray(where, jnp.int32)[lax.axis_index(axis)]


def ring_gather(value, ring, axis):
    count = len(ring)
    forward = [(ring[p], ring[(p + 1) % count]) for p in range(count)]
    backward = [(ring[p], ring[(p - 1) % count]) for p in range(count)]
    ahead = count // 2
    behind = count - 1 - ahead
    got = [value] + [None] * (count - 1)
    from_left = value
    from_right = value
    for step in range(max(ahead, behind)):
        if step < ahead:
            from_left = lax.ppermute(from_left, axis, forward)
            got[count - step - 1] = from_left
        if step < behind:
            from_right = lax.ppermute(from_right, axis, backward)
            got[step + 1] = from_right
    return jnp.stack(got, axis=0)


def ring_scatter_relative(partial, ring, axis):
    count = len(ring)
    rows = partial.shape[0] // count
    half = partial.shape[1] // 2
    blocks = partial.reshape(count, rows, partial.shape[1])
    left = blocks[:, :, :half]
    right = blocks[:, :, half:]
    forward = [(ring[p], ring[(p + 1) % count]) for p in range(count)]
    backward = [(ring[p], ring[(p - 1) % count]) for p in range(count)]
    send_left = left[count - 1]
    send_right = right[1 % count]
    for step in range(count - 1):
        got_left = lax.ppermute(send_left.astype(jnp.bfloat16), axis, forward)
        got_right = lax.ppermute(send_right.astype(jnp.bfloat16), axis, backward)
        send_left = got_left.astype(jnp.float32) + left[(2 * count - step - 2) % count]
        send_right = got_right.astype(jnp.float32) + right[(step + 2) % count]
    return jnp.concatenate([send_left, send_right], axis=1)


class Ring:
    def __init__(self, partial, ring, axis):
        count = len(ring)
        self.count = count
        self.axis = axis
        self.spot = ring_spot(ring, axis)
        self.order = jnp.asarray(ring, jnp.int32)
        rows = partial.shape[0] // count
        half = partial.shape[1] // 2
        blocks = partial.reshape(count, rows, partial.shape[1])
        self.left = blocks[:, :, :half]
        self.right = blocks[:, :, half:]
        self.forward = [(ring[p], ring[(p + 1) % count]) for p in range(count)]
        self.backward = [(ring[p], ring[(p - 1) % count]) for p in range(count)]
        self.state = (self.block(self.left, count - 1), self.block(self.right, 1))
        self.done = 0

    def block(self, side, offset):
        index = self.order[(self.spot + offset) % self.count]
        return lax.dynamic_index_in_dim(side, index, 0, keepdims=False)

    def advance(self, upto):
        count = self.count
        send_left, send_right = self.state
        for step in range(self.done, min(upto, count - 1)):
            got_left = lax.ppermute(send_left.astype(jnp.bfloat16), self.axis, self.forward)
            got_right = lax.ppermute(send_right.astype(jnp.bfloat16), self.axis, self.backward)
            send_left = got_left.astype(jnp.float32) + self.block(self.left, 2 * count - step - 2)
            send_right = got_right.astype(jnp.float32) + self.block(self.right, step + 2)
            self.done = step + 1
        self.state = (send_left, send_right)
        return self

    def result(self):
        self.advance(self.count - 1)
        return jnp.concatenate(list(self.state), axis=1)


def tp_project(partial, rows_mine, split, axis):
    rank = lax.axis_index(axis)
    core = rank % 2
    near = [(i, i ^ 1) for i in range(4)]
    far = [(i, i ^ 2) for i in range(4)]
    chip = partial + lax.ppermute(partial, axis, near)
    head = chip[:, :split]
    tail = chip[:, split:]
    half_rows = tail.shape[0] // 2
    mine = lax.dynamic_slice_in_dim(head, rank * rows_mine, rows_mine, 0)
    theirs = lax.dynamic_slice_in_dim(head, (rank ^ 2) * rows_mine, rows_mine, 0)
    own_head = mine + lax.ppermute(theirs, axis, far)
    tail_half = lax.dynamic_slice_in_dim(tail, core * half_rows, half_rows, 0)
    tail_half = tail_half + lax.ppermute(tail_half, axis, far)
    other_half = lax.ppermute(tail_half, axis, near)
    first = jnp.where(core == 0, tail_half, other_half)
    second = jnp.where(core == 0, other_half, tail_half)
    return own_head, jnp.concatenate([first, second], axis=0)


def tp_scatter(partial, rows_mine, axis):
    rank = lax.axis_index(axis)
    far = [(i, i ^ 2) for i in range(4)]
    near = [(i, i ^ 1) for i in range(4)]
    pair_rows = 2 * rows_mine
    chip = rank // 2
    kept = lax.dynamic_slice_in_dim(partial, chip * pair_rows, pair_rows, 0)
    sent = lax.dynamic_slice_in_dim(partial, (1 - chip) * pair_rows, pair_rows, 0)
    kept = kept.astype(jnp.float32) + lax.ppermute(
        sent.astype(jnp.bfloat16), axis, far
    ).astype(jnp.float32)
    core = rank % 2
    mine = lax.dynamic_slice_in_dim(kept, core * rows_mine, rows_mine, 0)
    other = lax.dynamic_slice_in_dim(kept, (1 - core) * rows_mine, rows_mine, 0)
    return mine + lax.ppermute(other.astype(jnp.bfloat16), axis, near).astype(jnp.float32)


def butterfly_sum(value, axis):
    count = lax.axis_size(axis)
    stride = 1
    while stride < count:
        pairs = [(i, i ^ stride) for i in range(count)]
        value = value + lax.ppermute(value, axis, pairs)
        stride *= 2
    return value


def shards(ring, tokens, document, place, w_qkv, w_out, grad_out):
    rows_ctx, slice_width = tokens.shape
    ctx_size = lax.axis_size("ctx")
    tp_size = lax.axis_size("tp")
    rows_mine = rows_ctx // tp_size
    tp_rank = lax.axis_index("tp")
    head_dim = HD
    heads = HQ
    heads_width = heads * head_dim
    pair_width = 2 * head_dim
    factor = 1.0 / math.sqrt(head_dim)
    first_row = tp_rank * rows_mine
    stacked = heads * rows_mine
    total_rows = ctx_size * rows_ctx

    grad_part = against(grad_out, w_out).astype(jnp.bfloat16)

    cosine_all, sine_all = angles(place, head_dim)
    cosine_mine = lax.dynamic_slice_in_dim(cosine_all, first_row, rows_mine, 0)
    sine_mine = lax.dynamic_slice_in_dim(sine_all, first_row, rows_mine, 0)
    query_doc = lax.dynamic_slice_in_dim(document, first_row, rows_mine, 0)
    query_place = lax.dynamic_slice_in_dim(place, first_row, rows_mine, 0)

    projected = against(tokens, w_qkv)
    if tp_size == 4 and rows_ctx % (2 * tp_size) == 0:
        query_block, pair_rows = tp_project(projected, rows_mine, heads_width, "tp")
    else:
        qkv = lax.psum(projected, "tp")
        query_block = lax.dynamic_slice_in_dim(qkv[:, :heads_width], first_row, rows_mine, 0)
        pair_rows = qkv[:, heads_width:]
    keys = rotate(pair_rows[:, :head_dim], cosine_all, sine_all).astype(jnp.bfloat16)
    values = pair_rows[:, head_dim:].astype(jnp.bfloat16)

    info = jnp.concatenate(
        [document, place // PIECE, place % PIECE], axis=0
    ).astype(jnp.float32)
    info_rows = -(-info.shape[0] // pair_width)
    info = jnp.pad(info, (0, info_rows * pair_width - info.shape[0]))
    info = info.reshape(info_rows, pair_width).astype(jnp.bfloat16)
    packed = jnp.concatenate([keys, values], axis=1)
    packed = jnp.concatenate([packed, info], axis=0)
    gathered = ring_gather(packed, ring, "ctx")
    if tp_size == 4 and rows_ctx % (2 * tp_size) == 0:
        grad_rows = tp_scatter(grad_part, rows_mine, "tp").astype(jnp.bfloat16)
    else:
        grad_rows = lax.psum_scatter(grad_part, "tp", scatter_dimension=0, tiled=True)
    keys_all = gathered[:, :rows_ctx, :head_dim].reshape(total_rows, head_dim)
    values_all = gathered[:, :rows_ctx, head_dim:].reshape(total_rows, head_dim)
    info_all = gathered[:, rows_ctx:, :].reshape(ctx_size, info_rows * pair_width).astype(
        jnp.float32
    )
    key_doc = info_all[:, :rows_ctx].reshape(total_rows)
    key_place = (
        info_all[:, rows_ctx : 2 * rows_ctx] * PIECE + info_all[:, 2 * rows_ctx : 3 * rows_ctx]
    ).reshape(total_rows)

    allowed = (query_doc.astype(jnp.float32)[:, None] == key_doc[None, :]) & (
        key_place[None, :] <= query_place.astype(jnp.float32)[:, None]
    )
    allowed = jnp.broadcast_to(allowed[None], (heads, rows_mine, total_rows)).reshape(
        stacked, total_rows
    )

    raw_query = query_block.reshape(rows_mine, heads, head_dim)
    rotated = rotate(raw_query, cosine_mine[:, None, :], sine_mine[:, None, :]).astype(jnp.bfloat16)
    queries = jnp.transpose(rotated, (1, 0, 2)).reshape(stacked, head_dim)

    scores = against(queries, keys_all) * factor
    masked = jnp.where(allowed, scores, NEG)
    top = jnp.max(masked, axis=1)
    weights = jnp.where(allowed, jnp.exp(masked - top[:, None]), 0.0)
    total = jnp.sum(weights, axis=1)
    summed = jnp.dot(weights.astype(jnp.bfloat16), values_all, preferred_element_type=jnp.float32)
    attended = (summed / total[:, None]).astype(jnp.bfloat16)
    logsum = top + jnp.log(total)

    rows_attended = jnp.transpose(attended.reshape(heads, rows_mine, head_dim), (1, 0, 2)).reshape(
        rows_mine, heads_width
    )
    piece = lax.all_gather(rows_attended, "tp", axis=0, tiled=True)
    out = jnp.dot(piece, w_out, preferred_element_type=jnp.float32).astype(jnp.bfloat16)
    out_weight_grad = across(piece, grad_out)

    grad_stack = jnp.transpose(grad_rows.reshape(rows_mine, heads, head_dim), (1, 0, 2)).reshape(
        stacked, head_dim
    )
    delta = jnp.sum(grad_stack.astype(jnp.float32) * attended.astype(jnp.float32), axis=1)
    prob = jnp.where(allowed, jnp.exp(scores - logsum[:, None]), 0.0)
    dprob = against(grad_stack, values_all)
    dscore = (prob * (dprob - delta[:, None])).astype(jnp.bfloat16)
    query_sum = jnp.dot(dscore, keys_all, preferred_element_type=jnp.float32)
    key_part = across(dscore, queries) * factor
    value_part = across(prob.astype(jnp.bfloat16), grad_stack)
    pair_all = jnp.concatenate([key_part, value_part], axis=1)
    out_ring = Ring(out_weight_grad, ring, "ctx").advance(len(ring) // 2)
    pair_grad = butterfly_sum(ring_scatter_relative(pair_all, ring, "ctx"), "tp")
    out_ring.state, pair_grad = lax.optimization_barrier((out_ring.state, pair_grad))

    key_raw = rotate(pair_grad[:, :head_dim], cosine_all, -sine_all)
    query_grad = jnp.transpose((query_sum * factor).reshape(heads, rows_mine, head_dim), (1, 0, 2))
    query_raw = rotate(query_grad, cosine_mine[:, None, :], -sine_mine[:, None, :]).reshape(
        rows_mine, heads_width
    )
    query_rows = lax.all_gather(query_raw.astype(jnp.bfloat16), "tp", axis=0, tiled=True)
    d_qkv = jnp.concatenate(
        [query_rows, key_raw.astype(jnp.bfloat16), pair_grad[:, head_dim:].astype(jnp.bfloat16)],
        axis=1,
    )
    grad_x = jnp.dot(d_qkv, w_qkv, preferred_element_type=jnp.float32).astype(jnp.bfloat16)
    joint_weight = across(d_qkv, tokens)
    out_ring.advance(len(ring) - 1)
    out_ring.state, joint_weight = lax.optimization_barrier((out_ring.state, joint_weight))
    grad_w_qkv = ring_scatter(joint_weight, ring, "ctx")
    grad_w_out = out_ring.result()
    return (out, grad_x, grad_w_qkv, grad_w_out)


def solution(mesh):
    return jax.shard_map(
        functools.partial(shards, ring_of(mesh)),
        mesh=mesh,
        in_specs=(P("ctx", "tp"), P("ctx"), P("ctx"), P(None, "tp"), P(None, "tp"), P("ctx", "tp")),
        out_specs=(P("ctx", "tp"), P("ctx", "tp"), P("ctx", "tp"), P("ctx", "tp")),
        check_vma=False,
    )
```

```python
import functools
import math

import jax
import jax.numpy as jnp
from jax import lax
from jax.sharding import PartitionSpec as P

HD = 128
HQ = 8


THETA = 500000.0
NEG = -1e30
PIECE = 64


def angles(place, width):
    half = width // 2
    freq = THETA ** (-(jnp.arange(half, dtype=jnp.float32) * 2.0 / width))
    turn = place.astype(jnp.float32)[:, None] * freq[None, :]
    return (jnp.cos(turn), jnp.sin(turn))


def rotate(vector, cosine, sine):
    half = vector.shape[-1] // 2
    first = vector[..., :half]
    second = vector[..., half:]
    return jnp.concatenate(
        [first * cosine - second * sine, second * cosine + first * sine], axis=-1
    )


def against(left, right):
    return lax.dot_general(
        left, right, (((1,), (1,)), ((), ())), preferred_element_type=jnp.float32
    )


def across(left, right):
    return lax.dot_general(
        left, right, (((0,), (0,)), ((), ())), preferred_element_type=jnp.float32
    )


def ring_of(mesh):
    count = mesh.shape["ctx"]
    try:
        grid = mesh.devices.reshape(count, -1)
        coords = [tuple(grid[i, 0].coords) for i in range(count)]
    except Exception:
        return list(range(count))
    varying = [d for d in range(len(coords[0])) if len({c[d] for c in coords}) > 1]
    if len(varying) == 1:
        return sorted(range(count), key=lambda i: coords[i][varying[0]])
    if len(varying) != 2:
        return list(range(count))
    for short, long in (varying, varying[::-1]):
        levels = sorted({c[short] for c in coords})
        if len(levels) == 2:
            there = sorted(
                (i for i in range(count) if coords[i][short] == levels[0]),
                key=lambda i: coords[i][long],
            )
            back = sorted(
                (i for i in range(count) if coords[i][short] == levels[1]),
                key=lambda i: -coords[i][long],
            )
            return there + back
    return list(range(count))


def ring_scatter(partial, ring, axis):
    count = len(ring)
    where = [0] * count
    for spot, member in enumerate(ring):
        where[member] = spot
    spot = jnp.asarray(where, jnp.int32)[lax.axis_index(axis)]
    order = jnp.asarray(ring, jnp.int32)
    rows = partial.shape[0] // count
    half = partial.shape[1] // 2
    blocks = partial.reshape(count, rows, partial.shape[1])
    left = blocks[:, :, :half]
    right = blocks[:, :, half:]

    def block(side, offset):
        return lax.dynamic_index_in_dim(side, order[(spot + offset) % count], 0, keepdims=False)

    forward = [(ring[p], ring[(p + 1) % count]) for p in range(count)]
    backward = [(ring[p], ring[(p - 1) % count]) for p in range(count)]
    send_left = block(left, count - 1)
    send_right = block(right, 1)
    for step in range(count - 1):
        got_left = lax.ppermute(send_left.astype(jnp.bfloat16), axis, forward)
        got_right = lax.ppermute(send_right.astype(jnp.bfloat16), axis, backward)
        send_left = got_left.astype(jnp.float32) + block(left, 2 * count - step - 2)
        send_right = got_right.astype(jnp.float32) + block(right, step + 2)
    return jnp.concatenate([send_left, send_right], axis=1)


def ring_spot(ring, axis):
    where = [0] * len(ring)
    for spot, member in enumerate(ring):
        where[member] = spot
    return jnp.asarray(where, jnp.int32)[lax.axis_index(axis)]


def ring_gather(value, ring, axis):
    count = len(ring)
    forward = [(ring[p], ring[(p + 1) % count]) for p in range(count)]
    backward = [(ring[p], ring[(p - 1) % count]) for p in range(count)]
    ahead = count // 2
    behind = count - 1 - ahead
    got = [value] + [None] * (count - 1)
    from_left = value
    from_right = value
    for step in range(max(ahead, behind)):
        if step < ahead:
            from_left = lax.ppermute(from_left, axis, forward)
            got[count - step - 1] = from_left
        if step < behind:
            from_right = lax.ppermute(from_right, axis, backward)
            got[step + 1] = from_right
    return jnp.stack(got, axis=0)


def ring_scatter_relative(partial, ring, axis):
    count = len(ring)
    rows = partial.shape[0] // count
    half = partial.shape[1] // 2
    blocks = partial.reshape(count, rows, partial.shape[1])
    left = blocks[:, :, :half]
    right = blocks[:, :, half:]
    forward = [(ring[p], ring[(p + 1) % count]) for p in range(count)]
    backward = [(ring[p], ring[(p - 1) % count]) for p in range(count)]
    send_left = left[count - 1]
    send_right = right[1 % count]
    for step in range(count - 1):
        got_left = lax.ppermute(send_left.astype(jnp.bfloat16), axis, forward)
        got_right = lax.ppermute(send_right.astype(jnp.bfloat16), axis, backward)
        send_left = got_left.astype(jnp.float32) + left[(2 * count - step - 2) % count]
        send_right = got_right.astype(jnp.float32) + right[(step + 2) % count]
    return jnp.concatenate([send_left, send_right], axis=1)


class Ring:
    def __init__(self, partial, ring, axis):
        count = len(ring)
        self.count = count
        self.axis = axis
        self.spot = ring_spot(ring, axis)
        self.order = jnp.asarray(ring, jnp.int32)
        rows = partial.shape[0] // count
        half = partial.shape[1] // 2
        blocks = partial.reshape(count, rows, partial.shape[1])
        self.left = blocks[:, :, :half]
        self.right = blocks[:, :, half:]
        self.forward = [(ring[p], ring[(p + 1) % count]) for p in range(count)]
        self.backward = [(ring[p], ring[(p - 1) % count]) for p in range(count)]
        self.state = (self.block(self.left, count - 1), self.block(self.right, 1))
        self.done = 0

    def block(self, side, offset):
        index = self.order[(self.spot + offset) % self.count]
        return lax.dynamic_index_in_dim(side, index, 0, keepdims=False)

    def advance(self, upto):
        count = self.count
        send_left, send_right = self.state
        for step in range(self.done, min(upto, count - 1)):
            got_left = lax.ppermute(send_left.astype(jnp.bfloat16), self.axis, self.forward)
            got_right = lax.ppermute(send_right.astype(jnp.bfloat16), self.axis, self.backward)
            send_left = got_left.astype(jnp.float32) + self.block(self.left, 2 * count - step - 2)
            send_right = got_right.astype(jnp.float32) + self.block(self.right, step + 2)
            self.done = step + 1
        self.state = (send_left, send_right)
        return self

    def result(self):
        self.advance(self.count - 1)
        return jnp.concatenate(list(self.state), axis=1)


def tp_project(partial, rows_mine, split, axis):
    rank = lax.axis_index(axis)
    core = rank % 2
    near = [(i, i ^ 1) for i in range(4)]
    far = [(i, i ^ 2) for i in range(4)]
    chip = partial + lax.ppermute(partial, axis, near)
    head = chip[:, :split]
    tail = chip[:, split:]
    half_rows = tail.shape[0] // 2
    mine = lax.dynamic_slice_in_dim(head, rank * rows_mine, rows_mine, 0)
    theirs = lax.dynamic_slice_in_dim(head, (rank ^ 2) * rows_mine, rows_mine, 0)
    own_head = mine + lax.ppermute(theirs, axis, far)
    tail_half = lax.dynamic_slice_in_dim(tail, core * half_rows, half_rows, 0)
    tail_half = tail_half + lax.ppermute(tail_half, axis, far)
    other_half = lax.ppermute(tail_half, axis, near)
    first = jnp.where(core == 0, tail_half, other_half)
    second = jnp.where(core == 0, other_half, tail_half)
    return own_head, jnp.concatenate([first, second], axis=0)


def tp_scatter(partial, rows_mine, axis):
    rank = lax.axis_index(axis)
    far = [(i, i ^ 2) for i in range(4)]
    near = [(i, i ^ 1) for i in range(4)]
    pair_rows = 2 * rows_mine
    chip = rank // 2
    kept = lax.dynamic_slice_in_dim(partial, chip * pair_rows, pair_rows, 0)
    sent = lax.dynamic_slice_in_dim(partial, (1 - chip) * pair_rows, pair_rows, 0)
    kept = kept.astype(jnp.float32) + lax.ppermute(
        sent.astype(jnp.bfloat16), axis, far
    ).astype(jnp.float32)
    core = rank % 2
    mine = lax.dynamic_slice_in_dim(kept, core * rows_mine, rows_mine, 0)
    other = lax.dynamic_slice_in_dim(kept, (1 - core) * rows_mine, rows_mine, 0)
    return mine + lax.ppermute(other.astype(jnp.bfloat16), axis, near).astype(jnp.float32)


def butterfly_sum(value, axis):
    count = lax.axis_size(axis)
    stride = 1
    while stride < count:
        pairs = [(i, i ^ stride) for i in range(count)]
        value = value + lax.ppermute(value, axis, pairs)
        stride *= 2
    return value


def shards(ring, tokens, document, place, w_qkv, w_out, grad_out):
    rows_ctx, slice_width = tokens.shape
    ctx_size = lax.axis_size("ctx")
    tp_size = lax.axis_size("tp")
    rows_mine = rows_ctx // tp_size
    tp_rank = lax.axis_index("tp")
    head_dim = HD
    heads = HQ
    heads_width = heads * head_dim
    pair_width = 2 * head_dim
    factor = 1.0 / math.sqrt(head_dim)
    first_row = tp_rank * rows_mine
    stacked = heads * rows_mine
    total_rows = ctx_size * rows_ctx

    grad_part = against(grad_out, w_out).astype(jnp.bfloat16)

    cosine_all, sine_all = angles(place, head_dim)
    cosine_mine = lax.dynamic_slice_in_dim(cosine_all, first_row, rows_mine, 0)
    sine_mine = lax.dynamic_slice_in_dim(sine_all, first_row, rows_mine, 0)
    query_doc = lax.dynamic_slice_in_dim(document, first_row, rows_mine, 0)
    query_place = lax.dynamic_slice_in_dim(place, first_row, rows_mine, 0)

    projected = against(tokens, w_qkv)
    if tp_size == 4 and rows_ctx % (2 * tp_size) == 0:
        query_block, pair_rows = tp_project(projected, rows_mine, heads_width, "tp")
    else:
        qkv = lax.psum(projected, "tp")
        query_block = lax.dynamic_slice_in_dim(qkv[:, :heads_width], first_row, rows_mine, 0)
        pair_rows = qkv[:, heads_width:]
    keys = rotate(pair_rows[:, :head_dim], cosine_all, sine_all).astype(jnp.bfloat16)
    values = pair_rows[:, head_dim:].astype(jnp.bfloat16)

    info = jnp.concatenate(
        [document, place // PIECE, place % PIECE], axis=0
    ).astype(jnp.float32)
    info_rows = -(-info.shape[0] // pair_width)
    info = jnp.pad(info, (0, info_rows * pair_width - info.shape[0]))
    info = info.reshape(info_rows, pair_width).astype(jnp.bfloat16)
    packed = jnp.concatenate([keys, values], axis=1)
    packed = jnp.concatenate([packed, info], axis=0)
    gathered = ring_gather(packed, ring, "ctx")
    if tp_size == 4 and rows_ctx % (2 * tp_size) == 0:
        grad_rows = tp_scatter(grad_part, rows_mine, "tp").astype(jnp.bfloat16)
    else:
        grad_rows = lax.psum_scatter(grad_part, "tp", scatter_dimension=0, tiled=True)
    keys_all = gathered[:, :rows_ctx, :head_dim].reshape(total_rows, head_dim)
    values_all = gathered[:, :rows_ctx, head_dim:].reshape(total_rows, head_dim)
    info_all = gathered[:, rows_ctx:, :].reshape(ctx_size, info_rows * pair_width).astype(
        jnp.float32
    )
    key_doc = info_all[:, :rows_ctx].reshape(total_rows)
    key_place = (
        info_all[:, rows_ctx : 2 * rows_ctx] * PIECE + info_all[:, 2 * rows_ctx : 3 * rows_ctx]
    ).reshape(total_rows)

    allowed = (query_doc.astype(jnp.float32)[:, None] == key_doc[None, :]) & (
        key_place[None, :] <= query_place.astype(jnp.float32)[:, None]
    )
    allowed = jnp.broadcast_to(allowed[None], (heads, rows_mine, total_rows)).reshape(
        stacked, total_rows
    )

    raw_query = query_block.reshape(rows_mine, heads, head_dim)
    rotated = rotate(raw_query, cosine_mine[:, None, :], sine_mine[:, None, :]).astype(jnp.bfloat16)
    queries = jnp.transpose(rotated, (1, 0, 2)).reshape(stacked, head_dim)

    scores = against(queries, keys_all) * factor
    masked = jnp.where(allowed, scores, NEG)
    top = jnp.max(masked, axis=1)
    weights = jnp.where(allowed, jnp.exp(masked - top[:, None]), 0.0)
    total = jnp.sum(weights, axis=1)
    summed = jnp.dot(weights.astype(jnp.bfloat16), values_all, preferred_element_type=jnp.float32)
    attended = (summed / total[:, None]).astype(jnp.bfloat16)
    logsum = top + jnp.log(total)

    rows_attended = jnp.transpose(attended.reshape(heads, rows_mine, head_dim), (1, 0, 2)).reshape(
        rows_mine, heads_width
    )
    piece = lax.all_gather(rows_attended, "tp", axis=0, tiled=True)
    out = jnp.dot(piece, w_out, preferred_element_type=jnp.float32).astype(jnp.bfloat16)
    out_weight_grad = across(piece, grad_out)

    grad_stack = jnp.transpose(grad_rows.reshape(rows_mine, heads, head_dim), (1, 0, 2)).reshape(
        stacked, head_dim
    )
    delta = jnp.sum(grad_stack.astype(jnp.float32) * attended.astype(jnp.float32), axis=1)
    prob = jnp.where(allowed, jnp.exp(scores - logsum[:, None]), 0.0)
    dprob = against(grad_stack, values_all)
    dscore = (prob * (dprob - delta[:, None])).astype(jnp.bfloat16)
    query_sum = jnp.dot(dscore, keys_all, preferred_element_type=jnp.float32)
    key_part = across(dscore, queries) * factor
    value_part = across(prob.astype(jnp.bfloat16), grad_stack)
    pair_all = jnp.concatenate([key_part, value_part], axis=1)
    out_ring = Ring(out_weight_grad, ring, "ctx").advance(len(ring) // 2)
    pair_grad = butterfly_sum(ring_scatter_relative(pair_all, ring, "ctx"), "tp")
    out_ring.state, pair_grad = lax.optimization_barrier((out_ring.state, pair_grad))

    key_raw = rotate(pair_grad[:, :head_dim], cosine_all, -sine_all)
    query_grad = jnp.transpose((query_sum * factor).reshape(heads, rows_mine, head_dim), (1, 0, 2))
    query_raw = rotate(query_grad, cosine_mine[:, None, :], -sine_mine[:, None, :]).reshape(
        rows_mine, heads_width
    )
    query_rows = lax.all_gather(query_raw.astype(jnp.bfloat16), "tp", axis=0, tiled=True)
    d_qkv = jnp.concatenate(
        [query_rows, key_raw.astype(jnp.bfloat16), pair_grad[:, head_dim:].astype(jnp.bfloat16)],
        axis=1,
    )
    grad_x = jnp.dot(d_qkv, w_qkv, preferred_element_type=jnp.float32).astype(jnp.bfloat16)
    joint_weight = across(d_qkv, tokens)
    out_ring.advance(len(ring) - 1)
    out_ring.state, joint_weight = lax.optimization_barrier((out_ring.state, joint_weight))
    chunk = joint_weight.shape[1] // 2
    grad_w_qkv = jnp.concatenate(
        [
            ring_scatter(joint_weight[:, :chunk], ring, "ctx"),
            ring_scatter(joint_weight[:, chunk:], ring, "ctx"),
        ],
        axis=1,
    )
    grad_w_out = out_ring.result()
    return (out, grad_x, grad_w_qkv, grad_w_out)


def solution(mesh):
    return jax.shard_map(
        functools.partial(shards, ring_of(mesh)),
        mesh=mesh,
        in_specs=(P("ctx", "tp"), P("ctx"), P("ctx"), P(None, "tp"), P(None, "tp"), P("ctx", "tp")),
        out_specs=(P("ctx", "tp"), P("ctx", "tp"), P("ctx", "tp"), P("ctx", "tp")),
        check_vma=False,
    )
```

```python
import functools
import math

import jax
import jax.numpy as jnp
from jax import lax
from jax.sharding import PartitionSpec as P

HD = 128
HQ = 8


THETA = 500000.0
NEG = -1e30
PIECE = 64


def angles(place, width):
    half = width // 2
    freq = THETA ** (-(jnp.arange(half, dtype=jnp.float32) * 2.0 / width))
    turn = place.astype(jnp.float32)[:, None] * freq[None, :]
    return (jnp.cos(turn), jnp.sin(turn))


def rotate(vector, cosine, sine):
    half = vector.shape[-1] // 2
    first = vector[..., :half]
    second = vector[..., half:]
    return jnp.concatenate(
        [first * cosine - second * sine, second * cosine + first * sine], axis=-1
    )


def against(left, right):
    return lax.dot_general(
        left, right, (((1,), (1,)), ((), ())), preferred_element_type=jnp.float32
    )


def across(left, right):
    return lax.dot_general(
        left, right, (((0,), (0,)), ((), ())), preferred_element_type=jnp.float32
    )


def ring_of(mesh):
    count = mesh.shape["ctx"]
    try:
        grid = mesh.devices.reshape(count, -1)
        coords = [tuple(grid[i, 0].coords) for i in range(count)]
    except Exception:
        return list(range(count))
    varying = [d for d in range(len(coords[0])) if len({c[d] for c in coords}) > 1]
    if len(varying) == 1:
        return sorted(range(count), key=lambda i: coords[i][varying[0]])
    if len(varying) != 2:
        return list(range(count))
    for short, long in (varying, varying[::-1]):
        levels = sorted({c[short] for c in coords})
        if len(levels) == 2:
            there = sorted(
                (i for i in range(count) if coords[i][short] == levels[0]),
                key=lambda i: coords[i][long],
            )
            back = sorted(
                (i for i in range(count) if coords[i][short] == levels[1]),
                key=lambda i: -coords[i][long],
            )
            return there + back
    return list(range(count))


def ring_scatter(partial, ring, axis):
    count = len(ring)
    where = [0] * count
    for spot, member in enumerate(ring):
        where[member] = spot
    spot = jnp.asarray(where, jnp.int32)[lax.axis_index(axis)]
    order = jnp.asarray(ring, jnp.int32)
    rows = partial.shape[0] // count
    half = partial.shape[1] // 2
    blocks = partial.reshape(count, rows, partial.shape[1])
    left = blocks[:, :, :half]
    right = blocks[:, :, half:]

    def block(side, offset):
        return lax.dynamic_index_in_dim(side, order[(spot + offset) % count], 0, keepdims=False)

    forward = [(ring[p], ring[(p + 1) % count]) for p in range(count)]
    backward = [(ring[p], ring[(p - 1) % count]) for p in range(count)]
    send_left = block(left, count - 1)
    send_right = block(right, 1)
    for step in range(count - 1):
        got_left = lax.ppermute(send_left.astype(jnp.bfloat16), axis, forward)
        got_right = lax.ppermute(send_right.astype(jnp.bfloat16), axis, backward)
        send_left = got_left.astype(jnp.float32) + block(left, 2 * count - step - 2)
        send_right = got_right.astype(jnp.float32) + block(right, step + 2)
    return jnp.concatenate([send_left, send_right], axis=1)


def ring_spot(ring, axis):
    where = [0] * len(ring)
    for spot, member in enumerate(ring):
        where[member] = spot
    return jnp.asarray(where, jnp.int32)[lax.axis_index(axis)]


def ring_gather(value, ring, axis):
    count = len(ring)
    forward = [(ring[p], ring[(p + 1) % count]) for p in range(count)]
    backward = [(ring[p], ring[(p - 1) % count]) for p in range(count)]
    ahead = count // 2
    behind = count - 1 - ahead
    got = [value] + [None] * (count - 1)
    from_left = value
    from_right = value
    for step in range(max(ahead, behind)):
        if step < ahead:
            from_left = lax.ppermute(from_left, axis, forward)
            got[count - step - 1] = from_left
        if step < behind:
            from_right = lax.ppermute(from_right, axis, backward)
            got[step + 1] = from_right
    return jnp.stack(got, axis=0)


def ring_scatter_relative(partial, ring, axis):
    count = len(ring)
    rows = partial.shape[0] // count
    half = partial.shape[1] // 2
    blocks = partial.reshape(count, rows, partial.shape[1])
    left = blocks[:, :, :half]
    right = blocks[:, :, half:]
    forward = [(ring[p], ring[(p + 1) % count]) for p in range(count)]
    backward = [(ring[p], ring[(p - 1) % count]) for p in range(count)]
    send_left = left[count - 1]
    send_right = right[1 % count]
    for step in range(count - 1):
        got_left = lax.ppermute(send_left.astype(jnp.bfloat16), axis, forward)
        got_right = lax.ppermute(send_right.astype(jnp.bfloat16), axis, backward)
        send_left = got_left.astype(jnp.float32) + left[(2 * count - step - 2) % count]
        send_right = got_right.astype(jnp.float32) + right[(step + 2) % count]
    return jnp.concatenate([send_left, send_right], axis=1)


class Ring:
    def __init__(self, partial, ring, axis):
        count = len(ring)
        self.count = count
        self.axis = axis
        self.spot = ring_spot(ring, axis)
        self.order = jnp.asarray(ring, jnp.int32)
        rows = partial.shape[0] // count
        half = partial.shape[1] // 2
        blocks = partial.reshape(count, rows, partial.shape[1])
        self.left = blocks[:, :, :half]
        self.right = blocks[:, :, half:]
        self.forward = [(ring[p], ring[(p + 1) % count]) for p in range(count)]
        self.backward = [(ring[p], ring[(p - 1) % count]) for p in range(count)]
        self.state = (self.block(self.left, count - 1), self.block(self.right, 1))
        self.done = 0

    def block(self, side, offset):
        index = self.order[(self.spot + offset) % self.count]
        return lax.dynamic_index_in_dim(side, index, 0, keepdims=False)

    def advance(self, upto):
        count = self.count
        send_left, send_right = self.state
        for step in range(self.done, min(upto, count - 1)):
            got_left = lax.ppermute(send_left.astype(jnp.bfloat16), self.axis, self.forward)
            got_right = lax.ppermute(send_right.astype(jnp.bfloat16), self.axis, self.backward)
            send_left = got_left.astype(jnp.float32) + self.block(self.left, 2 * count - step - 2)
            send_right = got_right.astype(jnp.float32) + self.block(self.right, step + 2)
            self.done = step + 1
        self.state = (send_left, send_right)
        return self

    def result(self):
        self.advance(self.count - 1)
        return jnp.concatenate(list(self.state), axis=1)


def tp_project(partial, rows_mine, split, axis):
    rank = lax.axis_index(axis)
    core = rank % 2
    near = [(i, i ^ 1) for i in range(4)]
    far = [(i, i ^ 2) for i in range(4)]
    chip = partial + lax.ppermute(partial, axis, near)
    head = chip[:, :split]
    tail = chip[:, split:]
    half_rows = tail.shape[0] // 2
    mine = lax.dynamic_slice_in_dim(head, rank * rows_mine, rows_mine, 0)
    theirs = lax.dynamic_slice_in_dim(head, (rank ^ 2) * rows_mine, rows_mine, 0)
    own_head = mine + lax.ppermute(theirs, axis, far)
    tail_half = lax.dynamic_slice_in_dim(tail, core * half_rows, half_rows, 0)
    tail_half = tail_half + lax.ppermute(tail_half, axis, far)
    other_half = lax.ppermute(tail_half, axis, near)
    first = jnp.where(core == 0, tail_half, other_half)
    second = jnp.where(core == 0, other_half, tail_half)
    return own_head, jnp.concatenate([first, second], axis=0)


def tp_scatter(partial, rows_mine, axis):
    rank = lax.axis_index(axis)
    far = [(i, i ^ 2) for i in range(4)]
    near = [(i, i ^ 1) for i in range(4)]
    pair_rows = 2 * rows_mine
    chip = rank // 2
    kept = lax.dynamic_slice_in_dim(partial, chip * pair_rows, pair_rows, 0)
    sent = lax.dynamic_slice_in_dim(partial, (1 - chip) * pair_rows, pair_rows, 0)
    kept = kept.astype(jnp.float32) + lax.ppermute(
        sent.astype(jnp.bfloat16), axis, far
    ).astype(jnp.float32)
    core = rank % 2
    mine = lax.dynamic_slice_in_dim(kept, core * rows_mine, rows_mine, 0)
    other = lax.dynamic_slice_in_dim(kept, (1 - core) * rows_mine, rows_mine, 0)
    return mine + lax.ppermute(other.astype(jnp.bfloat16), axis, near).astype(jnp.float32)


def direct_gather(value, axis):
    count = lax.axis_size(axis)
    got = [value] + [None] * (count - 1)
    for shift in range(1, count):
        pairs = [(i, (i + shift) % count) for i in range(count)]
        got[count - shift] = lax.ppermute(value, axis, pairs)
    return jnp.stack(got, axis=0)


def direct_scatter(partial, axis):
    count = lax.axis_size(axis)
    rows = partial.shape[0] // count
    blocks = partial.reshape(count, rows, partial.shape[1])
    total = blocks[0]
    for shift in range(1, count):
        pairs = [(i, (i + shift) % count) for i in range(count)]
        total = total + lax.ppermute(blocks[shift].astype(jnp.bfloat16), axis, pairs).astype(
            jnp.float32
        )
    return total


def butterfly_sum(value, axis):
    count = lax.axis_size(axis)
    stride = 1
    while stride < count:
        pairs = [(i, i ^ stride) for i in range(count)]
        value = value + lax.ppermute(value, axis, pairs)
        stride *= 2
    return value


def shards(ring, tokens, document, place, w_qkv, w_out, grad_out):
    rows_ctx, slice_width = tokens.shape
    ctx_size = lax.axis_size("ctx")
    tp_size = lax.axis_size("tp")
    rows_mine = rows_ctx // tp_size
    tp_rank = lax.axis_index("tp")
    head_dim = HD
    heads = HQ
    heads_width = heads * head_dim
    pair_width = 2 * head_dim
    factor = 1.0 / math.sqrt(head_dim)
    first_row = tp_rank * rows_mine
    stacked = heads * rows_mine
    total_rows = ctx_size * rows_ctx

    grad_part = against(grad_out, w_out).astype(jnp.bfloat16)

    cosine_all, sine_all = angles(place, head_dim)
    cosine_mine = lax.dynamic_slice_in_dim(cosine_all, first_row, rows_mine, 0)
    sine_mine = lax.dynamic_slice_in_dim(sine_all, first_row, rows_mine, 0)
    query_doc = lax.dynamic_slice_in_dim(document, first_row, rows_mine, 0)
    query_place = lax.dynamic_slice_in_dim(place, first_row, rows_mine, 0)

    projected = against(tokens, w_qkv)
    if tp_size == 4 and rows_ctx % (2 * tp_size) == 0:
        query_block, pair_rows = tp_project(projected, rows_mine, heads_width, "tp")
    else:
        qkv = lax.psum(projected, "tp")
        query_block = lax.dynamic_slice_in_dim(qkv[:, :heads_width], first_row, rows_mine, 0)
        pair_rows = qkv[:, heads_width:]
    keys = rotate(pair_rows[:, :head_dim], cosine_all, sine_all).astype(jnp.bfloat16)
    values = pair_rows[:, head_dim:].astype(jnp.bfloat16)

    info = jnp.concatenate(
        [document, place // PIECE, place % PIECE], axis=0
    ).astype(jnp.float32)
    info_rows = -(-info.shape[0] // pair_width)
    info = jnp.pad(info, (0, info_rows * pair_width - info.shape[0]))
    info = info.reshape(info_rows, pair_width).astype(jnp.bfloat16)
    packed = jnp.concatenate([keys, values], axis=1)
    packed = jnp.concatenate([packed, info], axis=0)
    gathered = direct_gather(packed, "ctx")
    if tp_size == 4 and rows_ctx % (2 * tp_size) == 0:
        grad_rows = tp_scatter(grad_part, rows_mine, "tp").astype(jnp.bfloat16)
    else:
        grad_rows = lax.psum_scatter(grad_part, "tp", scatter_dimension=0, tiled=True)
    keys_all = gathered[:, :rows_ctx, :head_dim].reshape(total_rows, head_dim)
    values_all = gathered[:, :rows_ctx, head_dim:].reshape(total_rows, head_dim)
    info_all = gathered[:, rows_ctx:, :].reshape(ctx_size, info_rows * pair_width).astype(
        jnp.float32
    )
    key_doc = info_all[:, :rows_ctx].reshape(total_rows)
    key_place = (
        info_all[:, rows_ctx : 2 * rows_ctx] * PIECE + info_all[:, 2 * rows_ctx : 3 * rows_ctx]
    ).reshape(total_rows)

    allowed = (query_doc.astype(jnp.float32)[:, None] == key_doc[None, :]) & (
        key_place[None, :] <= query_place.astype(jnp.float32)[:, None]
    )
    allowed = jnp.broadcast_to(allowed[None], (heads, rows_mine, total_rows)).reshape(
        stacked, total_rows
    )

    raw_query = query_block.reshape(rows_mine, heads, head_dim)
    rotated = rotate(raw_query, cosine_mine[:, None, :], sine_mine[:, None, :]).astype(jnp.bfloat16)
    queries = jnp.transpose(rotated, (1, 0, 2)).reshape(stacked, head_dim)

    scores = against(queries, keys_all) * factor
    masked = jnp.where(allowed, scores, NEG)
    top = jnp.max(masked, axis=1)
    weights = jnp.where(allowed, jnp.exp(masked - top[:, None]), 0.0)
    total = jnp.sum(weights, axis=1)
    summed = jnp.dot(weights.astype(jnp.bfloat16), values_all, preferred_element_type=jnp.float32)
    attended = (summed / total[:, None]).astype(jnp.bfloat16)
    logsum = top + jnp.log(total)

    rows_attended = jnp.transpose(attended.reshape(heads, rows_mine, head_dim), (1, 0, 2)).reshape(
        rows_mine, heads_width
    )
    piece = lax.all_gather(rows_attended, "tp", axis=0, tiled=True)
    out = jnp.dot(piece, w_out, preferred_element_type=jnp.float32).astype(jnp.bfloat16)
    out_weight_grad = across(piece, grad_out)

    grad_stack = jnp.transpose(grad_rows.reshape(rows_mine, heads, head_dim), (1, 0, 2)).reshape(
        stacked, head_dim
    )
    delta = jnp.sum(grad_stack.astype(jnp.float32) * attended.astype(jnp.float32), axis=1)
    prob = jnp.where(allowed, jnp.exp(scores - logsum[:, None]), 0.0)
    dprob = against(grad_stack, values_all)
    dscore = (prob * (dprob - delta[:, None])).astype(jnp.bfloat16)
    query_sum = jnp.dot(dscore, keys_all, preferred_element_type=jnp.float32)
    key_part = across(dscore, queries) * factor
    value_part = across(prob.astype(jnp.bfloat16), grad_stack)
    pair_all = jnp.concatenate([key_part, value_part], axis=1)
    out_ring = Ring(out_weight_grad, ring, "ctx").advance(len(ring) // 2)
    pair_grad = butterfly_sum(direct_scatter(pair_all, "ctx"), "tp")
    out_ring.state, pair_grad = lax.optimization_barrier((out_ring.state, pair_grad))

    key_raw = rotate(pair_grad[:, :head_dim], cosine_all, -sine_all)
    query_grad = jnp.transpose((query_sum * factor).reshape(heads, rows_mine, head_dim), (1, 0, 2))
    query_raw = rotate(query_grad, cosine_mine[:, None, :], -sine_mine[:, None, :]).reshape(
        rows_mine, heads_width
    )
    query_rows = lax.all_gather(query_raw.astype(jnp.bfloat16), "tp", axis=0, tiled=True)
    d_qkv = jnp.concatenate(
        [query_rows, key_raw.astype(jnp.bfloat16), pair_grad[:, head_dim:].astype(jnp.bfloat16)],
        axis=1,
    )
    grad_x = jnp.dot(d_qkv, w_qkv, preferred_element_type=jnp.float32).astype(jnp.bfloat16)
    joint_weight = across(d_qkv, tokens)
    out_ring.advance(len(ring) - 1)
    out_ring.state, joint_weight = lax.optimization_barrier((out_ring.state, joint_weight))
    grad_w_qkv = ring_scatter(joint_weight, ring, "ctx")
    grad_w_out = out_ring.result()
    return (out, grad_x, grad_w_qkv, grad_w_out)


def solution(mesh):
    return jax.shard_map(
        functools.partial(shards, ring_of(mesh)),
        mesh=mesh,
        in_specs=(P("ctx", "tp"), P("ctx"), P("ctx"), P(None, "tp"), P(None, "tp"), P("ctx", "tp")),
        out_specs=(P("ctx", "tp"), P("ctx", "tp"), P("ctx", "tp"), P("ctx", "tp")),
        check_vma=False,
    )
```

```python
import functools
import math

import jax
import jax.numpy as jnp
from jax import lax
from jax.sharding import PartitionSpec as P

HD = 128
HQ = 8


THETA = 500000.0
NEG = -1e30
PIECE = 64


def angles(place, width):
    half = width // 2
    freq = THETA ** (-(jnp.arange(half, dtype=jnp.float32) * 2.0 / width))
    turn = place.astype(jnp.float32)[:, None] * freq[None, :]
    return (jnp.cos(turn), jnp.sin(turn))


def rotate(vector, cosine, sine):
    half = vector.shape[-1] // 2
    first = vector[..., :half]
    second = vector[..., half:]
    return jnp.concatenate(
        [first * cosine - second * sine, second * cosine + first * sine], axis=-1
    )


def against(left, right):
    return lax.dot_general(
        left, right, (((1,), (1,)), ((), ())), preferred_element_type=jnp.float32
    )


def across(left, right):
    return lax.dot_general(
        left, right, (((0,), (0,)), ((), ())), preferred_element_type=jnp.float32
    )


def ring_of(mesh):
    count = mesh.shape["ctx"]
    try:
        grid = mesh.devices.reshape(count, -1)
        coords = [tuple(grid[i, 0].coords) for i in range(count)]
    except Exception:
        return list(range(count))
    varying = [d for d in range(len(coords[0])) if len({c[d] for c in coords}) > 1]
    if len(varying) == 1:
        return sorted(range(count), key=lambda i: coords[i][varying[0]])
    if len(varying) != 2:
        return list(range(count))
    for short, long in (varying, varying[::-1]):
        levels = sorted({c[short] for c in coords})
        if len(levels) == 2:
            there = sorted(
                (i for i in range(count) if coords[i][short] == levels[0]),
                key=lambda i: coords[i][long],
            )
            back = sorted(
                (i for i in range(count) if coords[i][short] == levels[1]),
                key=lambda i: -coords[i][long],
            )
            return there + back
    return list(range(count))


def ring_scatter(partial, ring, axis):
    count = len(ring)
    where = [0] * count
    for spot, member in enumerate(ring):
        where[member] = spot
    spot = jnp.asarray(where, jnp.int32)[lax.axis_index(axis)]
    order = jnp.asarray(ring, jnp.int32)
    rows = partial.shape[0] // count
    half = partial.shape[1] // 2
    blocks = partial.reshape(count, rows, partial.shape[1])
    left = blocks[:, :, :half]
    right = blocks[:, :, half:]

    def block(side, offset):
        return lax.dynamic_index_in_dim(side, order[(spot + offset) % count], 0, keepdims=False)

    forward = [(ring[p], ring[(p + 1) % count]) for p in range(count)]
    backward = [(ring[p], ring[(p - 1) % count]) for p in range(count)]
    send_left = block(left, count - 1)
    send_right = block(right, 1)
    for step in range(count - 1):
        got_left = lax.ppermute(send_left.astype(jnp.bfloat16), axis, forward)
        got_right = lax.ppermute(send_right.astype(jnp.bfloat16), axis, backward)
        send_left = got_left.astype(jnp.float32) + block(left, 2 * count - step - 2)
        send_right = got_right.astype(jnp.float32) + block(right, step + 2)
    return jnp.concatenate([send_left, send_right], axis=1)


def ring_spot(ring, axis):
    where = [0] * len(ring)
    for spot, member in enumerate(ring):
        where[member] = spot
    return jnp.asarray(where, jnp.int32)[lax.axis_index(axis)]


def ring_gather(value, ring, axis):
    count = len(ring)
    forward = [(ring[p], ring[(p + 1) % count]) for p in range(count)]
    backward = [(ring[p], ring[(p - 1) % count]) for p in range(count)]
    ahead = count // 2
    behind = count - 1 - ahead
    got = [value] + [None] * (count - 1)
    from_left = value
    from_right = value
    for step in range(max(ahead, behind)):
        if step < ahead:
            from_left = lax.ppermute(from_left, axis, forward)
            got[count - step - 1] = from_left
        if step < behind:
            from_right = lax.ppermute(from_right, axis, backward)
            got[step + 1] = from_right
    return jnp.stack(got, axis=0)


def ring_scatter_relative(partial, ring, axis):
    count = len(ring)
    rows = partial.shape[0] // count
    half = partial.shape[1] // 2
    blocks = partial.reshape(count, rows, partial.shape[1])
    left = blocks[:, :, :half]
    right = blocks[:, :, half:]
    forward = [(ring[p], ring[(p + 1) % count]) for p in range(count)]
    backward = [(ring[p], ring[(p - 1) % count]) for p in range(count)]
    send_left = left[count - 1]
    send_right = right[1 % count]
    for step in range(count - 1):
        got_left = lax.ppermute(send_left.astype(jnp.bfloat16), axis, forward)
        got_right = lax.ppermute(send_right.astype(jnp.bfloat16), axis, backward)
        send_left = got_left.astype(jnp.float32) + left[(2 * count - step - 2) % count]
        send_right = got_right.astype(jnp.float32) + right[(step + 2) % count]
    return jnp.concatenate([send_left, send_right], axis=1)


class Ring:
    def __init__(self, partial, ring, axis):
        count = len(ring)
        self.count = count
        self.axis = axis
        self.spot = ring_spot(ring, axis)
        self.order = jnp.asarray(ring, jnp.int32)
        rows = partial.shape[0] // count
        half = partial.shape[1] // 2
        blocks = partial.reshape(count, rows, partial.shape[1])
        self.left = blocks[:, :, :half]
        self.right = blocks[:, :, half:]
        self.forward = [(ring[p], ring[(p + 1) % count]) for p in range(count)]
        self.backward = [(ring[p], ring[(p - 1) % count]) for p in range(count)]
        self.state = (self.block(self.left, count - 1), self.block(self.right, 1))
        self.done = 0

    def block(self, side, offset):
        index = self.order[(self.spot + offset) % self.count]
        return lax.dynamic_index_in_dim(side, index, 0, keepdims=False)

    def advance(self, upto):
        count = self.count
        send_left, send_right = self.state
        for step in range(self.done, min(upto, count - 1)):
            got_left = lax.ppermute(send_left.astype(jnp.bfloat16), self.axis, self.forward)
            got_right = lax.ppermute(send_right.astype(jnp.bfloat16), self.axis, self.backward)
            send_left = got_left.astype(jnp.float32) + self.block(self.left, 2 * count - step - 2)
            send_right = got_right.astype(jnp.float32) + self.block(self.right, step + 2)
            self.done = step + 1
        self.state = (send_left, send_right)
        return self

    def result(self):
        self.advance(self.count - 1)
        return jnp.concatenate(list(self.state), axis=1)


def tp_project(partial, rows_mine, split, axis):
    rank = lax.axis_index(axis)
    core = rank % 2
    near = [(i, i ^ 1) for i in range(4)]
    far = [(i, i ^ 2) for i in range(4)]
    chip = partial + lax.ppermute(partial, axis, near)
    head = chip[:, :split]
    tail = chip[:, split:]
    half_rows = tail.shape[0] // 2
    mine = lax.dynamic_slice_in_dim(head, rank * rows_mine, rows_mine, 0)
    theirs = lax.dynamic_slice_in_dim(head, (rank ^ 2) * rows_mine, rows_mine, 0)
    own_head = mine + lax.ppermute(theirs, axis, far)
    tail_half = lax.dynamic_slice_in_dim(tail, core * half_rows, half_rows, 0)
    tail_half = tail_half + lax.ppermute(tail_half, axis, far)
    other_half = lax.ppermute(tail_half, axis, near)
    first = jnp.where(core == 0, tail_half, other_half)
    second = jnp.where(core == 0, other_half, tail_half)
    return own_head, jnp.concatenate([first, second], axis=0)


def tp_scatter(partial, rows_mine, axis):
    rank = lax.axis_index(axis)
    far = [(i, i ^ 2) for i in range(4)]
    near = [(i, i ^ 1) for i in range(4)]
    pair_rows = 2 * rows_mine
    chip = rank // 2
    kept = lax.dynamic_slice_in_dim(partial, chip * pair_rows, pair_rows, 0)
    sent = lax.dynamic_slice_in_dim(partial, (1 - chip) * pair_rows, pair_rows, 0)
    kept = kept.astype(jnp.float32) + lax.ppermute(
        sent.astype(jnp.bfloat16), axis, far
    ).astype(jnp.float32)
    core = rank % 2
    mine = lax.dynamic_slice_in_dim(kept, core * rows_mine, rows_mine, 0)
    other = lax.dynamic_slice_in_dim(kept, (1 - core) * rows_mine, rows_mine, 0)
    return mine + lax.ppermute(other.astype(jnp.bfloat16), axis, near).astype(jnp.float32)


def direct_gather(value, axis):
    count = lax.axis_size(axis)
    got = [value] + [None] * (count - 1)
    for shift in range(1, count):
        pairs = [(i, (i + shift) % count) for i in range(count)]
        got[count - shift] = lax.ppermute(value, axis, pairs)
    return jnp.stack(got, axis=0)


def direct_scatter(partial, axis):
    count = lax.axis_size(axis)
    rows = partial.shape[0] // count
    blocks = partial.reshape(count, rows, partial.shape[1])
    total = blocks[0]
    for shift in range(1, count):
        pairs = [(i, (i + shift) % count) for i in range(count)]
        total = total + lax.ppermute(blocks[shift].astype(jnp.bfloat16), axis, pairs).astype(
            jnp.float32
        )
    return total


def ring_exchange(value, block_cols, ring, axis):
    count = len(ring)
    spot = ring_spot(ring, axis)
    order = jnp.asarray(ring, jnp.int32)
    got = [lax.dynamic_slice_in_dim(value, order[spot] * block_cols, block_cols, 1)]
    for offset in range(1, count):
        pairs = [(ring[p], ring[(p - offset) % count]) for p in range(count)]
        target = order[(spot - offset) % count]
        sent = lax.dynamic_slice_in_dim(value, target * block_cols, block_cols, 1)
        got.append(lax.ppermute(sent, axis, pairs))
    return jnp.concatenate(got, axis=0)


def butterfly_sum(value, axis):
    count = lax.axis_size(axis)
    stride = 1
    while stride < count:
        pairs = [(i, i ^ stride) for i in range(count)]
        value = value + lax.ppermute(value, axis, pairs)
        stride *= 2
    return value


def shards(ring, tokens, document, place, w_qkv, w_out, grad_out):
    rows_ctx, slice_width = tokens.shape
    ctx_size = lax.axis_size("ctx")
    tp_size = lax.axis_size("tp")
    rows_mine = rows_ctx // tp_size
    tp_rank = lax.axis_index("tp")
    head_dim = HD
    heads = HQ
    heads_width = heads * head_dim
    pair_width = 2 * head_dim
    factor = 1.0 / math.sqrt(head_dim)
    first_row = tp_rank * rows_mine
    stacked = heads * rows_mine
    total_rows = ctx_size * rows_ctx

    grad_part = against(grad_out, w_out).astype(jnp.bfloat16)

    cosine_all, sine_all = angles(place, head_dim)
    cosine_mine = lax.dynamic_slice_in_dim(cosine_all, first_row, rows_mine, 0)
    sine_mine = lax.dynamic_slice_in_dim(sine_all, first_row, rows_mine, 0)
    query_doc = lax.dynamic_slice_in_dim(document, first_row, rows_mine, 0)
    query_place = lax.dynamic_slice_in_dim(place, first_row, rows_mine, 0)

    projected = against(tokens, w_qkv)
    if tp_size == 4 and rows_ctx % (2 * tp_size) == 0:
        query_block, pair_rows = tp_project(projected, rows_mine, heads_width, "tp")
    else:
        qkv = lax.psum(projected, "tp")
        query_block = lax.dynamic_slice_in_dim(qkv[:, :heads_width], first_row, rows_mine, 0)
        pair_rows = qkv[:, heads_width:]
    keys = rotate(pair_rows[:, :head_dim], cosine_all, sine_all).astype(jnp.bfloat16)
    values = pair_rows[:, head_dim:].astype(jnp.bfloat16)

    info = jnp.concatenate(
        [document, place // PIECE, place % PIECE], axis=0
    ).astype(jnp.float32)
    info_rows = -(-info.shape[0] // pair_width)
    info = jnp.pad(info, (0, info_rows * pair_width - info.shape[0]))
    info = info.reshape(info_rows, pair_width).astype(jnp.bfloat16)
    packed = jnp.concatenate([keys, values], axis=1)
    packed = jnp.concatenate([packed, info], axis=0)
    gathered = direct_gather(packed, "ctx")
    if tp_size == 4 and rows_ctx % (2 * tp_size) == 0:
        grad_rows = tp_scatter(grad_part, rows_mine, "tp").astype(jnp.bfloat16)
    else:
        grad_rows = lax.psum_scatter(grad_part, "tp", scatter_dimension=0, tiled=True)
    keys_all = gathered[:, :rows_ctx, :head_dim].reshape(total_rows, head_dim)
    values_all = gathered[:, :rows_ctx, head_dim:].reshape(total_rows, head_dim)
    info_all = gathered[:, rows_ctx:, :].reshape(ctx_size, info_rows * pair_width).astype(
        jnp.float32
    )
    key_doc = info_all[:, :rows_ctx].reshape(total_rows)
    key_place = (
        info_all[:, rows_ctx : 2 * rows_ctx] * PIECE + info_all[:, 2 * rows_ctx : 3 * rows_ctx]
    ).reshape(total_rows)

    allowed = (query_doc.astype(jnp.float32)[:, None] == key_doc[None, :]) & (
        key_place[None, :] <= query_place.astype(jnp.float32)[:, None]
    )
    allowed = jnp.broadcast_to(allowed[None], (heads, rows_mine, total_rows)).reshape(
        stacked, total_rows
    )

    raw_query = query_block.reshape(rows_mine, heads, head_dim)
    rotated = rotate(raw_query, cosine_mine[:, None, :], sine_mine[:, None, :]).astype(jnp.bfloat16)
    queries = jnp.transpose(rotated, (1, 0, 2)).reshape(stacked, head_dim)

    scores = against(queries, keys_all) * factor
    masked = jnp.where(allowed, scores, NEG)
    top = jnp.max(masked, axis=1)
    weights = jnp.where(allowed, jnp.exp(masked - top[:, None]), 0.0)
    total = jnp.sum(weights, axis=1)
    summed = jnp.dot(weights.astype(jnp.bfloat16), values_all, preferred_element_type=jnp.float32)
    attended = (summed / total[:, None]).astype(jnp.bfloat16)
    logsum = top + jnp.log(total)

    rows_attended = jnp.transpose(attended.reshape(heads, rows_mine, head_dim), (1, 0, 2)).reshape(
        rows_mine, heads_width
    )
    piece = lax.all_gather(rows_attended, "tp", axis=0, tiled=True)
    out = jnp.dot(piece, w_out, preferred_element_type=jnp.float32).astype(jnp.bfloat16)
    out_weight_grad = across(piece, grad_out)

    tokens_all = ring_gather(tokens[:, : slice_width // 2], ring, "ctx")
    tokens_all = tokens_all.reshape(total_rows, slice_width // 2)
    tokens_all, grad_rows = lax.optimization_barrier((tokens_all, grad_rows))
    grad_stack = jnp.transpose(grad_rows.reshape(rows_mine, heads, head_dim), (1, 0, 2)).reshape(
        stacked, head_dim
    )
    delta = jnp.sum(grad_stack.astype(jnp.float32) * attended.astype(jnp.float32), axis=1)
    prob = jnp.where(allowed, jnp.exp(scores - logsum[:, None]), 0.0)
    dprob = against(grad_stack, values_all)
    dscore = (prob * (dprob - delta[:, None])).astype(jnp.bfloat16)
    query_sum = jnp.dot(dscore, keys_all, preferred_element_type=jnp.float32)
    key_part = across(dscore, queries) * factor
    value_part = across(prob.astype(jnp.bfloat16), grad_stack)
    pair_all = jnp.concatenate([key_part, value_part], axis=1)
    out_ring = Ring(out_weight_grad, ring, "ctx").advance(len(ring) // 2)
    pair_grad = butterfly_sum(direct_scatter(pair_all, "ctx"), "tp")
    out_ring.state, pair_grad = lax.optimization_barrier((out_ring.state, pair_grad))

    key_raw = rotate(pair_grad[:, :head_dim], cosine_all, -sine_all)
    query_grad = jnp.transpose((query_sum * factor).reshape(heads, rows_mine, head_dim), (1, 0, 2))
    query_raw = rotate(query_grad, cosine_mine[:, None, :], -sine_mine[:, None, :]).reshape(
        rows_mine, heads_width
    )
    query_rows = lax.all_gather(query_raw.astype(jnp.bfloat16), "tp", axis=0, tiled=True)
    d_qkv = jnp.concatenate(
        [query_rows, key_raw.astype(jnp.bfloat16), pair_grad[:, head_dim:].astype(jnp.bfloat16)],
        axis=1,
    )
    grad_x = jnp.dot(d_qkv, w_qkv, preferred_element_type=jnp.float32).astype(jnp.bfloat16)
    split = slice_width // 2
    joint_weight = across(d_qkv, tokens[:, split:])
    out_ring.advance(len(ring) - 1)
    out_ring.state, joint_weight = lax.optimization_barrier((out_ring.state, joint_weight))
    d_cols = ring_exchange(d_qkv, d_qkv.shape[1] // ctx_size, ring, "ctx")
    grad_w_qkv = jnp.concatenate(
        [across(d_cols, tokens_all), ring_scatter(joint_weight, ring, "ctx")], axis=1
    )
    grad_w_out = out_ring.result()
    return (out, grad_x, grad_w_qkv, grad_w_out)


def solution(mesh):
    return jax.shard_map(
        functools.partial(shards, ring_of(mesh)),
        mesh=mesh,
        in_specs=(P("ctx", "tp"), P("ctx"), P("ctx"), P(None, "tp"), P(None, "tp"), P("ctx", "tp")),
        out_specs=(P("ctx", "tp"), P("ctx", "tp"), P("ctx", "tp"), P("ctx", "tp")),
        check_vma=False,
    )
```

```python
import functools
import math

import jax
import jax.numpy as jnp
from jax import lax
from jax.sharding import PartitionSpec as P

HD = 128
HQ = 8


THETA = 500000.0
NEG = -1e30
PIECE = 64


def angles(place, width):
    half = width // 2
    freq = THETA ** (-(jnp.arange(half, dtype=jnp.float32) * 2.0 / width))
    turn = place.astype(jnp.float32)[:, None] * freq[None, :]
    return (jnp.cos(turn), jnp.sin(turn))


def rotate(vector, cosine, sine):
    half = vector.shape[-1] // 2
    first = vector[..., :half]
    second = vector[..., half:]
    return jnp.concatenate(
        [first * cosine - second * sine, second * cosine + first * sine], axis=-1
    )


def against(left, right):
    return lax.dot_general(
        left, right, (((1,), (1,)), ((), ())), preferred_element_type=jnp.float32
    )


def across(left, right):
    return lax.dot_general(
        left, right, (((0,), (0,)), ((), ())), preferred_element_type=jnp.float32
    )


def ring_of(mesh):
    count = mesh.shape["ctx"]
    try:
        grid = mesh.devices.reshape(count, -1)
        coords = [tuple(grid[i, 0].coords) for i in range(count)]
    except Exception:
        return list(range(count))
    varying = [d for d in range(len(coords[0])) if len({c[d] for c in coords}) > 1]
    if len(varying) == 1:
        return sorted(range(count), key=lambda i: coords[i][varying[0]])
    if len(varying) != 2:
        return list(range(count))
    for short, long in (varying, varying[::-1]):
        levels = sorted({c[short] for c in coords})
        if len(levels) == 2:
            there = sorted(
                (i for i in range(count) if coords[i][short] == levels[0]),
                key=lambda i: coords[i][long],
            )
            back = sorted(
                (i for i in range(count) if coords[i][short] == levels[1]),
                key=lambda i: -coords[i][long],
            )
            return there + back
    return list(range(count))


def ring_scatter(partial, ring, axis, by_offset=False):
    count = len(ring)
    where = [0] * count
    for spot, member in enumerate(ring):
        where[member] = spot
    rank = lax.axis_index(axis)
    spot = jnp.asarray(where, jnp.int32)[rank]
    order = jnp.asarray(ring, jnp.int32)
    if by_offset:
        order = (order - rank) % count
    rows = partial.shape[0] // count
    half = partial.shape[1] // 2
    blocks = partial.reshape(count, rows, partial.shape[1])
    left = blocks[:, :, :half]
    right = blocks[:, :, half:]

    def block(side, offset):
        return lax.dynamic_index_in_dim(side, order[(spot + offset) % count], 0, keepdims=False)

    forward = [(ring[p], ring[(p + 1) % count]) for p in range(count)]
    backward = [(ring[p], ring[(p - 1) % count]) for p in range(count)]
    send_left = block(left, count - 1)
    send_right = block(right, 1)
    for step in range(count - 1):
        got_left = lax.ppermute(send_left.astype(jnp.bfloat16), axis, forward)
        got_right = lax.ppermute(send_right.astype(jnp.bfloat16), axis, backward)
        send_left = got_left.astype(jnp.float32) + block(left, 2 * count - step - 2)
        send_right = got_right.astype(jnp.float32) + block(right, step + 2)
    return jnp.concatenate([send_left, send_right], axis=1)


def ring_spot(ring, axis):
    where = [0] * len(ring)
    for spot, member in enumerate(ring):
        where[member] = spot
    return jnp.asarray(where, jnp.int32)[lax.axis_index(axis)]


def ring_gather(value, ring, axis):
    count = len(ring)
    forward = [(ring[p], ring[(p + 1) % count]) for p in range(count)]
    backward = [(ring[p], ring[(p - 1) % count]) for p in range(count)]
    ahead = count // 2
    behind = count - 1 - ahead
    got = [value] + [None] * (count - 1)
    from_left = value
    from_right = value
    for step in range(max(ahead, behind)):
        if step < ahead:
            from_left = lax.ppermute(from_left, axis, forward)
            got[count - step - 1] = from_left
        if step < behind:
            from_right = lax.ppermute(from_right, axis, backward)
            got[step + 1] = from_right
    return jnp.stack(got, axis=0)


def ring_scatter_relative(partial, ring, axis):
    count = len(ring)
    rows = partial.shape[0] // count
    half = partial.shape[1] // 2
    blocks = partial.reshape(count, rows, partial.shape[1])
    left = blocks[:, :, :half]
    right = blocks[:, :, half:]
    forward = [(ring[p], ring[(p + 1) % count]) for p in range(count)]
    backward = [(ring[p], ring[(p - 1) % count]) for p in range(count)]
    send_left = left[count - 1]
    send_right = right[1 % count]
    for step in range(count - 1):
        got_left = lax.ppermute(send_left.astype(jnp.bfloat16), axis, forward)
        got_right = lax.ppermute(send_right.astype(jnp.bfloat16), axis, backward)
        send_left = got_left.astype(jnp.float32) + left[(2 * count - step - 2) % count]
        send_right = got_right.astype(jnp.float32) + right[(step + 2) % count]
    return jnp.concatenate([send_left, send_right], axis=1)


class Ring:
    def __init__(self, partial, ring, axis):
        count = len(ring)
        self.count = count
        self.axis = axis
        self.spot = ring_spot(ring, axis)
        self.order = jnp.asarray(ring, jnp.int32)
        rows = partial.shape[0] // count
        half = partial.shape[1] // 2
        blocks = partial.reshape(count, rows, partial.shape[1])
        self.left = blocks[:, :, :half]
        self.right = blocks[:, :, half:]
        self.forward = [(ring[p], ring[(p + 1) % count]) for p in range(count)]
        self.backward = [(ring[p], ring[(p - 1) % count]) for p in range(count)]
        self.state = (self.block(self.left, count - 1), self.block(self.right, 1))
        self.done = 0

    def block(self, side, offset):
        index = self.order[(self.spot + offset) % self.count]
        return lax.dynamic_index_in_dim(side, index, 0, keepdims=False)

    def advance(self, upto):
        count = self.count
        send_left, send_right = self.state
        for step in range(self.done, min(upto, count - 1)):
            got_left = lax.ppermute(send_left.astype(jnp.bfloat16), self.axis, self.forward)
            got_right = lax.ppermute(send_right.astype(jnp.bfloat16), self.axis, self.backward)
            send_left = got_left.astype(jnp.float32) + self.block(self.left, 2 * count - step - 2)
            send_right = got_right.astype(jnp.float32) + self.block(self.right, step + 2)
            self.done = step + 1
        self.state = (send_left, send_right)
        return self

    def result(self):
        self.advance(self.count - 1)
        return jnp.concatenate(list(self.state), axis=1)


def tp_project(partial, rows_mine, split, axis):
    rank = lax.axis_index(axis)
    core = rank % 2
    near = [(i, i ^ 1) for i in range(4)]
    far = [(i, i ^ 2) for i in range(4)]
    chip = partial + lax.ppermute(partial, axis, near)
    head = chip[:, :split]
    tail = chip[:, split:]
    half_rows = tail.shape[0] // 2
    mine = lax.dynamic_slice_in_dim(head, rank * rows_mine, rows_mine, 0)
    theirs = lax.dynamic_slice_in_dim(head, (rank ^ 2) * rows_mine, rows_mine, 0)
    own_head = mine + lax.ppermute(theirs, axis, far)
    tail_half = lax.dynamic_slice_in_dim(tail, core * half_rows, half_rows, 0)
    tail_half = tail_half + lax.ppermute(tail_half, axis, far)
    other_half = lax.ppermute(tail_half, axis, near)
    first = jnp.where(core == 0, tail_half, other_half)
    second = jnp.where(core == 0, other_half, tail_half)
    return own_head, jnp.concatenate([first, second], axis=0)


def tp_scatter(partial, rows_mine, axis):
    rank = lax.axis_index(axis)
    far = [(i, i ^ 2) for i in range(4)]
    near = [(i, i ^ 1) for i in range(4)]
    pair_rows = 2 * rows_mine
    chip = rank // 2
    kept = lax.dynamic_slice_in_dim(partial, chip * pair_rows, pair_rows, 0)
    sent = lax.dynamic_slice_in_dim(partial, (1 - chip) * pair_rows, pair_rows, 0)
    kept = kept.astype(jnp.float32) + lax.ppermute(
        sent.astype(jnp.bfloat16), axis, far
    ).astype(jnp.float32)
    core = rank % 2
    mine = lax.dynamic_slice_in_dim(kept, core * rows_mine, rows_mine, 0)
    other = lax.dynamic_slice_in_dim(kept, (1 - core) * rows_mine, rows_mine, 0)
    return mine + lax.ppermute(other.astype(jnp.bfloat16), axis, near).astype(jnp.float32)


def direct_gather(value, axis):
    count = lax.axis_size(axis)
    got = [value] + [None] * (count - 1)
    for shift in range(1, count):
        pairs = [(i, (i + shift) % count) for i in range(count)]
        got[count - shift] = lax.ppermute(value, axis, pairs)
    return jnp.stack(got, axis=0)


def direct_scatter(partial, axis):
    count = lax.axis_size(axis)
    rows = partial.shape[0] // count
    blocks = partial.reshape(count, rows, partial.shape[1])
    total = blocks[0]
    for shift in range(1, count):
        pairs = [(i, (i + shift) % count) for i in range(count)]
        total = total + lax.ppermute(blocks[shift].astype(jnp.bfloat16), axis, pairs).astype(
            jnp.float32
        )
    return total


def butterfly_sum(value, axis):
    count = lax.axis_size(axis)
    stride = 1
    while stride < count:
        pairs = [(i, i ^ stride) for i in range(count)]
        value = value + lax.ppermute(value, axis, pairs)
        stride *= 2
    return value


def shards(ring, tokens, document, place, w_qkv, w_out, grad_out):
    rows_ctx, slice_width = tokens.shape
    ctx_size = lax.axis_size("ctx")
    tp_size = lax.axis_size("tp")
    rows_mine = rows_ctx // tp_size
    tp_rank = lax.axis_index("tp")
    head_dim = HD
    heads = HQ
    heads_width = heads * head_dim
    pair_width = 2 * head_dim
    factor = 1.0 / math.sqrt(head_dim)
    first_row = tp_rank * rows_mine
    stacked = heads * rows_mine
    total_rows = ctx_size * rows_ctx

    grad_part = against(grad_out, w_out).astype(jnp.bfloat16)

    cosine_all, sine_all = angles(place, head_dim)
    cosine_mine = lax.dynamic_slice_in_dim(cosine_all, first_row, rows_mine, 0)
    sine_mine = lax.dynamic_slice_in_dim(sine_all, first_row, rows_mine, 0)
    query_doc = lax.dynamic_slice_in_dim(document, first_row, rows_mine, 0)
    query_place = lax.dynamic_slice_in_dim(place, first_row, rows_mine, 0)

    projected = against(tokens, w_qkv)
    if tp_size == 4 and rows_ctx % (2 * tp_size) == 0:
        query_block, pair_rows = tp_project(projected, rows_mine, heads_width, "tp")
    else:
        qkv = lax.psum(projected, "tp")
        query_block = lax.dynamic_slice_in_dim(qkv[:, :heads_width], first_row, rows_mine, 0)
        pair_rows = qkv[:, heads_width:]
    keys = rotate(pair_rows[:, :head_dim], cosine_all, sine_all).astype(jnp.bfloat16)
    values = pair_rows[:, head_dim:].astype(jnp.bfloat16)

    info = jnp.concatenate(
        [document, place // PIECE, place % PIECE], axis=0
    ).astype(jnp.float32)
    info_rows = -(-info.shape[0] // pair_width)
    info = jnp.pad(info, (0, info_rows * pair_width - info.shape[0]))
    info = info.reshape(info_rows, pair_width).astype(jnp.bfloat16)
    packed = jnp.concatenate([keys, values], axis=1)
    packed = jnp.concatenate([packed, info], axis=0)
    gathered = direct_gather(packed, "ctx")
    if tp_size == 4 and rows_ctx % (2 * tp_size) == 0:
        grad_rows = tp_scatter(grad_part, rows_mine, "tp").astype(jnp.bfloat16)
    else:
        grad_rows = lax.psum_scatter(grad_part, "tp", scatter_dimension=0, tiled=True)
    keys_all = gathered[:, :rows_ctx, :head_dim].reshape(total_rows, head_dim)
    values_all = gathered[:, :rows_ctx, head_dim:].reshape(total_rows, head_dim)
    info_all = gathered[:, rows_ctx:, :].reshape(ctx_size, info_rows * pair_width).astype(
        jnp.float32
    )
    key_doc = info_all[:, :rows_ctx].reshape(total_rows)
    key_place = (
        info_all[:, rows_ctx : 2 * rows_ctx] * PIECE + info_all[:, 2 * rows_ctx : 3 * rows_ctx]
    ).reshape(total_rows)

    allowed = (query_doc.astype(jnp.float32)[:, None] == key_doc[None, :]) & (
        key_place[None, :] <= query_place.astype(jnp.float32)[:, None]
    )
    allowed = jnp.broadcast_to(allowed[None], (heads, rows_mine, total_rows)).reshape(
        stacked, total_rows
    )

    raw_query = query_block.reshape(rows_mine, heads, head_dim)
    rotated = rotate(raw_query, cosine_mine[:, None, :], sine_mine[:, None, :]).astype(jnp.bfloat16)
    queries = jnp.transpose(rotated, (1, 0, 2)).reshape(stacked, head_dim)

    scores = against(queries, keys_all) * factor
    masked = jnp.where(allowed, scores, NEG)
    top = jnp.max(masked, axis=1)
    weights = jnp.where(allowed, jnp.exp(masked - top[:, None]), 0.0)
    total = jnp.sum(weights, axis=1)
    summed = jnp.dot(weights.astype(jnp.bfloat16), values_all, preferred_element_type=jnp.float32)
    attended = (summed / total[:, None]).astype(jnp.bfloat16)
    logsum = top + jnp.log(total)

    rows_attended = jnp.transpose(attended.reshape(heads, rows_mine, head_dim), (1, 0, 2)).reshape(
        rows_mine, heads_width
    )
    piece = lax.all_gather(rows_attended, "tp", axis=0, tiled=True)
    out = jnp.dot(piece, w_out, preferred_element_type=jnp.float32).astype(jnp.bfloat16)
    out_weight_grad = across(piece, grad_out)

    grad_stack = jnp.transpose(grad_rows.reshape(rows_mine, heads, head_dim), (1, 0, 2)).reshape(
        stacked, head_dim
    )
    delta = jnp.sum(grad_stack.astype(jnp.float32) * attended.astype(jnp.float32), axis=1)
    prob = jnp.where(allowed, jnp.exp(scores - logsum[:, None]), 0.0)
    dprob = against(grad_stack, values_all)
    dscore = (prob * (dprob - delta[:, None])).astype(jnp.bfloat16)
    query_sum = jnp.dot(dscore, keys_all, preferred_element_type=jnp.float32)
    key_part = across(dscore, queries) * factor
    value_part = across(prob.astype(jnp.bfloat16), grad_stack)
    pair_all = jnp.concatenate([key_part, value_part], axis=1)
    out_ring = Ring(out_weight_grad, ring, "ctx").advance(len(ring) // 2)
    pair_grad = butterfly_sum(ring_scatter(pair_all, ring, "ctx", by_offset=True), "tp")
    out_ring.state, pair_grad = lax.optimization_barrier((out_ring.state, pair_grad))

    key_raw = rotate(pair_grad[:, :head_dim], cosine_all, -sine_all)
    query_grad = jnp.transpose((query_sum * factor).reshape(heads, rows_mine, head_dim), (1, 0, 2))
    query_raw = rotate(query_grad, cosine_mine[:, None, :], -sine_mine[:, None, :]).reshape(
        rows_mine, heads_width
    )
    query_rows = lax.all_gather(query_raw.astype(jnp.bfloat16), "tp", axis=0, tiled=True)
    d_qkv = jnp.concatenate(
        [query_rows, key_raw.astype(jnp.bfloat16), pair_grad[:, head_dim:].astype(jnp.bfloat16)],
        axis=1,
    )
    grad_x = jnp.dot(d_qkv, w_qkv, preferred_element_type=jnp.float32).astype(jnp.bfloat16)
    joint_weight = across(d_qkv, tokens)
    out_ring.advance(len(ring) - 1)
    out_ring.state, joint_weight = lax.optimization_barrier((out_ring.state, joint_weight))
    grad_w_qkv = ring_scatter(joint_weight, ring, "ctx")
    grad_w_out = out_ring.result()
    return (out, grad_x, grad_w_qkv, grad_w_out)


def solution(mesh):
    return jax.shard_map(
        functools.partial(shards, ring_of(mesh)),
        mesh=mesh,
        in_specs=(P("ctx", "tp"), P("ctx"), P("ctx"), P(None, "tp"), P(None, "tp"), P("ctx", "tp")),
        out_specs=(P("ctx", "tp"), P("ctx", "tp"), P("ctx", "tp"), P("ctx", "tp")),
        check_vma=False,
    )
```

```python
import functools
import math

import jax
import jax.numpy as jnp
from jax import lax
from jax.sharding import PartitionSpec as P

HD = 128
HQ = 8


THETA = 500000.0
NEG = -1e30
PIECE = 64


def angles(place, width):
    half = width // 2
    freq = THETA ** (-(jnp.arange(half, dtype=jnp.float32) * 2.0 / width))
    turn = place.astype(jnp.float32)[:, None] * freq[None, :]
    return (jnp.cos(turn), jnp.sin(turn))


def rotate(vector, cosine, sine):
    half = vector.shape[-1] // 2
    first = vector[..., :half]
    second = vector[..., half:]
    return jnp.concatenate(
        [first * cosine - second * sine, second * cosine + first * sine], axis=-1
    )


def against(left, right):
    return lax.dot_general(
        left, right, (((1,), (1,)), ((), ())), preferred_element_type=jnp.float32
    )


def across(left, right):
    return lax.dot_general(
        left, right, (((0,), (0,)), ((), ())), preferred_element_type=jnp.float32
    )


def ring_of(mesh):
    count = mesh.shape["ctx"]
    try:
        grid = mesh.devices.reshape(count, -1)
        coords = [tuple(grid[i, 0].coords) for i in range(count)]
    except Exception:
        return list(range(count))
    varying = [d for d in range(len(coords[0])) if len({c[d] for c in coords}) > 1]
    if len(varying) == 1:
        return sorted(range(count), key=lambda i: coords[i][varying[0]])
    if len(varying) != 2:
        return list(range(count))
    for short, long in (varying, varying[::-1]):
        levels = sorted({c[short] for c in coords})
        if len(levels) == 2:
            there = sorted(
                (i for i in range(count) if coords[i][short] == levels[0]),
                key=lambda i: coords[i][long],
            )
            back = sorted(
                (i for i in range(count) if coords[i][short] == levels[1]),
                key=lambda i: -coords[i][long],
            )
            return there + back
    return list(range(count))


def ring_scatter(partial, ring, axis):
    count = len(ring)
    where = [0] * count
    for spot, member in enumerate(ring):
        where[member] = spot
    spot = jnp.asarray(where, jnp.int32)[lax.axis_index(axis)]
    order = jnp.asarray(ring, jnp.int32)
    rows = partial.shape[0] // count
    half = partial.shape[1] // 2
    blocks = partial.reshape(count, rows, partial.shape[1])
    left = blocks[:, :, :half]
    right = blocks[:, :, half:]

    def block(side, offset):
        return lax.dynamic_index_in_dim(side, order[(spot + offset) % count], 0, keepdims=False)

    forward = [(ring[p], ring[(p + 1) % count]) for p in range(count)]
    backward = [(ring[p], ring[(p - 1) % count]) for p in range(count)]
    send_left = block(left, count - 1)
    send_right = block(right, 1)
    for step in range(count - 1):
        got_left = lax.ppermute(send_left.astype(jnp.bfloat16), axis, forward)
        got_right = lax.ppermute(send_right.astype(jnp.bfloat16), axis, backward)
        send_left = got_left.astype(jnp.float32) + block(left, 2 * count - step - 2)
        send_right = got_right.astype(jnp.float32) + block(right, step + 2)
    return jnp.concatenate([send_left, send_right], axis=1)


def ring_spot(ring, axis):
    where = [0] * len(ring)
    for spot, member in enumerate(ring):
        where[member] = spot
    return jnp.asarray(where, jnp.int32)[lax.axis_index(axis)]


def ring_gather(value, ring, axis):
    count = len(ring)
    forward = [(ring[p], ring[(p + 1) % count]) for p in range(count)]
    backward = [(ring[p], ring[(p - 1) % count]) for p in range(count)]
    ahead = count // 2
    behind = count - 1 - ahead
    got = [value] + [None] * (count - 1)
    from_left = value
    from_right = value
    for step in range(max(ahead, behind)):
        if step < ahead:
            from_left = lax.ppermute(from_left, axis, forward)
            got[count - step - 1] = from_left
        if step < behind:
            from_right = lax.ppermute(from_right, axis, backward)
            got[step + 1] = from_right
    return jnp.stack(got, axis=0)


def ring_scatter_relative(partial, ring, axis):
    count = len(ring)
    rows = partial.shape[0] // count
    half = partial.shape[1] // 2
    blocks = partial.reshape(count, rows, partial.shape[1])
    left = blocks[:, :, :half]
    right = blocks[:, :, half:]
    forward = [(ring[p], ring[(p + 1) % count]) for p in range(count)]
    backward = [(ring[p], ring[(p - 1) % count]) for p in range(count)]
    send_left = left[count - 1]
    send_right = right[1 % count]
    for step in range(count - 1):
        got_left = lax.ppermute(send_left.astype(jnp.bfloat16), axis, forward)
        got_right = lax.ppermute(send_right.astype(jnp.bfloat16), axis, backward)
        send_left = got_left.astype(jnp.float32) + left[(2 * count - step - 2) % count]
        send_right = got_right.astype(jnp.float32) + right[(step + 2) % count]
    return jnp.concatenate([send_left, send_right], axis=1)


class Ring:
    def __init__(self, partial, ring, axis):
        count = len(ring)
        self.count = count
        self.axis = axis
        self.spot = ring_spot(ring, axis)
        self.order = jnp.asarray(ring, jnp.int32)
        rows = partial.shape[0] // count
        half = partial.shape[1] // 2
        blocks = partial.reshape(count, rows, partial.shape[1])
        self.left = blocks[:, :, :half]
        self.right = blocks[:, :, half:]
        self.forward = [(ring[p], ring[(p + 1) % count]) for p in range(count)]
        self.backward = [(ring[p], ring[(p - 1) % count]) for p in range(count)]
        self.state = (self.block(self.left, count - 1), self.block(self.right, 1))
        self.done = 0

    def block(self, side, offset):
        index = self.order[(self.spot + offset) % self.count]
        return lax.dynamic_index_in_dim(side, index, 0, keepdims=False)

    def advance(self, upto):
        count = self.count
        send_left, send_right = self.state
        for step in range(self.done, min(upto, count - 1)):
            got_left = lax.ppermute(send_left.astype(jnp.bfloat16), self.axis, self.forward)
            got_right = lax.ppermute(send_right.astype(jnp.bfloat16), self.axis, self.backward)
            send_left = got_left.astype(jnp.float32) + self.block(self.left, 2 * count - step - 2)
            send_right = got_right.astype(jnp.float32) + self.block(self.right, step + 2)
            self.done = step + 1
        self.state = (send_left, send_right)
        return self

    def result(self):
        self.advance(self.count - 1)
        return jnp.concatenate(list(self.state), axis=1)


def tp_project(partial, rows_mine, split, axis):
    rank = lax.axis_index(axis)
    core = rank % 2
    near = [(i, i ^ 1) for i in range(4)]
    far = [(i, i ^ 2) for i in range(4)]
    chip = partial + lax.ppermute(partial, axis, near)
    head = chip[:, :split]
    tail = chip[:, split:]
    half_rows = tail.shape[0] // 2
    mine = lax.dynamic_slice_in_dim(head, rank * rows_mine, rows_mine, 0)
    theirs = lax.dynamic_slice_in_dim(head, (rank ^ 2) * rows_mine, rows_mine, 0)
    own_head = mine + lax.ppermute(theirs, axis, far)
    tail_half = lax.dynamic_slice_in_dim(tail, core * half_rows, half_rows, 0)
    tail_half = tail_half + lax.ppermute(tail_half, axis, far)
    other_half = lax.ppermute(tail_half, axis, near)
    first = jnp.where(core == 0, tail_half, other_half)
    second = jnp.where(core == 0, other_half, tail_half)
    return own_head, jnp.concatenate([first, second], axis=0)


def tp_scatter(partial, rows_mine, axis):
    rank = lax.axis_index(axis)
    far = [(i, i ^ 2) for i in range(4)]
    near = [(i, i ^ 1) for i in range(4)]
    pair_rows = 2 * rows_mine
    chip = rank // 2
    kept = lax.dynamic_slice_in_dim(partial, chip * pair_rows, pair_rows, 0)
    sent = lax.dynamic_slice_in_dim(partial, (1 - chip) * pair_rows, pair_rows, 0)
    kept = kept.astype(jnp.float32) + lax.ppermute(
        sent.astype(jnp.bfloat16), axis, far
    ).astype(jnp.float32)
    core = rank % 2
    mine = lax.dynamic_slice_in_dim(kept, core * rows_mine, rows_mine, 0)
    other = lax.dynamic_slice_in_dim(kept, (1 - core) * rows_mine, rows_mine, 0)
    return mine + lax.ppermute(other.astype(jnp.bfloat16), axis, near).astype(jnp.float32)


def direct_gather(value, axis):
    count = lax.axis_size(axis)
    got = [value] + [None] * (count - 1)
    for shift in range(1, count):
        pairs = [(i, (i + shift) % count) for i in range(count)]
        got[count - shift] = lax.ppermute(value, axis, pairs)
    return jnp.stack(got, axis=0)


def direct_scatter(partial, axis):
    count = lax.axis_size(axis)
    rows = partial.shape[0] // count
    blocks = partial.reshape(count, rows, partial.shape[1])
    total = blocks[0]
    for shift in range(1, count):
        pairs = [(i, (i + shift) % count) for i in range(count)]
        total = total + lax.ppermute(blocks[shift].astype(jnp.bfloat16), axis, pairs).astype(
            jnp.float32
        )
    return total


def butterfly_sum(value, axis):
    count = lax.axis_size(axis)
    stride = 1
    while stride < count:
        pairs = [(i, i ^ stride) for i in range(count)]
        value = value + lax.ppermute(value, axis, pairs)
        stride *= 2
    return value


def shards(ring, tokens, document, place, w_qkv, w_out, grad_out):
    rows_ctx, slice_width = tokens.shape
    ctx_size = lax.axis_size("ctx")
    tp_size = lax.axis_size("tp")
    rows_mine = rows_ctx // tp_size
    tp_rank = lax.axis_index("tp")
    head_dim = HD
    heads = HQ
    heads_width = heads * head_dim
    pair_width = 2 * head_dim
    factor = 1.0 / math.sqrt(head_dim)
    first_row = tp_rank * rows_mine
    stacked = heads * rows_mine
    total_rows = ctx_size * rows_ctx

    grad_part = against(grad_out, w_out).astype(jnp.bfloat16)

    cosine_all, sine_all = angles(place, head_dim)
    cosine_mine = lax.dynamic_slice_in_dim(cosine_all, first_row, rows_mine, 0)
    sine_mine = lax.dynamic_slice_in_dim(sine_all, first_row, rows_mine, 0)
    query_doc = lax.dynamic_slice_in_dim(document, first_row, rows_mine, 0)
    query_place = lax.dynamic_slice_in_dim(place, first_row, rows_mine, 0)

    projected = against(tokens, w_qkv)
    if tp_size == 4 and rows_ctx % (2 * tp_size) == 0:
        query_block, pair_rows = tp_project(projected, rows_mine, heads_width, "tp")
    else:
        qkv = lax.psum(projected, "tp")
        query_block = lax.dynamic_slice_in_dim(qkv[:, :heads_width], first_row, rows_mine, 0)
        pair_rows = qkv[:, heads_width:]
    keys = rotate(pair_rows[:, :head_dim], cosine_all, sine_all).astype(jnp.bfloat16)
    values = pair_rows[:, head_dim:].astype(jnp.bfloat16)

    info = jnp.concatenate(
        [document, place // PIECE, place % PIECE], axis=0
    ).astype(jnp.float32)
    info_rows = -(-info.shape[0] // pair_width)
    info = jnp.pad(info, (0, info_rows * pair_width - info.shape[0]))
    info = info.reshape(info_rows, pair_width).astype(jnp.bfloat16)
    packed = jnp.concatenate([keys, values], axis=1)
    packed = jnp.concatenate([packed, info], axis=0)
    gathered = direct_gather(packed, "ctx")
    if tp_size == 4 and rows_ctx % (2 * tp_size) == 0:
        grad_rows = tp_scatter(grad_part, rows_mine, "tp").astype(jnp.bfloat16)
    else:
        grad_rows = lax.psum_scatter(grad_part, "tp", scatter_dimension=0, tiled=True)
    keys_all = gathered[:, :rows_ctx, :head_dim].reshape(total_rows, head_dim)
    values_all = gathered[:, :rows_ctx, head_dim:].reshape(total_rows, head_dim)
    info_all = gathered[:, rows_ctx:, :].reshape(ctx_size, info_rows * pair_width).astype(
        jnp.float32
    )
    key_doc = info_all[:, :rows_ctx].reshape(total_rows)
    key_place = (
        info_all[:, rows_ctx : 2 * rows_ctx] * PIECE + info_all[:, 2 * rows_ctx : 3 * rows_ctx]
    ).reshape(total_rows)

    allowed = (query_doc.astype(jnp.float32)[:, None] == key_doc[None, :]) & (
        key_place[None, :] <= query_place.astype(jnp.float32)[:, None]
    )
    allowed = jnp.broadcast_to(allowed[None], (heads, rows_mine, total_rows)).reshape(
        stacked, total_rows
    )

    raw_query = query_block.reshape(rows_mine, heads, head_dim)
    rotated = rotate(raw_query, cosine_mine[:, None, :], sine_mine[:, None, :]).astype(jnp.bfloat16)
    queries = jnp.transpose(rotated, (1, 0, 2)).reshape(stacked, head_dim)

    scores = against(queries, keys_all) * factor
    masked = jnp.where(allowed, scores, NEG)
    top = jnp.max(masked, axis=1)
    weights = jnp.where(allowed, jnp.exp(masked - top[:, None]), 0.0)
    total = jnp.sum(weights, axis=1)
    summed = jnp.dot(weights.astype(jnp.bfloat16), values_all, preferred_element_type=jnp.float32)
    attended = (summed / total[:, None]).astype(jnp.bfloat16)
    logsum = top + jnp.log(total)

    rows_attended = jnp.transpose(attended.reshape(heads, rows_mine, head_dim), (1, 0, 2)).reshape(
        rows_mine, heads_width
    )
    piece = lax.all_gather(rows_attended, "tp", axis=0, tiled=True)
    out = jnp.dot(piece, w_out, preferred_element_type=jnp.float32).astype(jnp.bfloat16)
    out_weight_grad = across(piece, grad_out)

    out, grad_rows = lax.optimization_barrier((out, grad_rows))
    grad_stack = jnp.transpose(grad_rows.reshape(rows_mine, heads, head_dim), (1, 0, 2)).reshape(
        stacked, head_dim
    )
    delta = jnp.sum(grad_stack.astype(jnp.float32) * attended.astype(jnp.float32), axis=1)
    prob = jnp.where(allowed, jnp.exp(scores - logsum[:, None]), 0.0)
    dprob = against(grad_stack, values_all)
    dscore = (prob * (dprob - delta[:, None])).astype(jnp.bfloat16)
    query_sum = jnp.dot(dscore, keys_all, preferred_element_type=jnp.float32)
    key_part = across(dscore, queries) * factor
    value_part = across(prob.astype(jnp.bfloat16), grad_stack)
    pair_all = jnp.concatenate([key_part, value_part], axis=1)
    out_ring = Ring(out_weight_grad, ring, "ctx").advance(len(ring) // 2)
    pair_grad = butterfly_sum(direct_scatter(pair_all, "ctx"), "tp")
    out_ring.state, pair_grad = lax.optimization_barrier((out_ring.state, pair_grad))

    key_raw = rotate(pair_grad[:, :head_dim], cosine_all, -sine_all)
    query_grad = jnp.transpose((query_sum * factor).reshape(heads, rows_mine, head_dim), (1, 0, 2))
    query_raw = rotate(query_grad, cosine_mine[:, None, :], -sine_mine[:, None, :]).reshape(
        rows_mine, heads_width
    )
    query_rows = lax.all_gather(query_raw.astype(jnp.bfloat16), "tp", axis=0, tiled=True)
    d_qkv = jnp.concatenate(
        [query_rows, key_raw.astype(jnp.bfloat16), pair_grad[:, head_dim:].astype(jnp.bfloat16)],
        axis=1,
    )
    grad_x = jnp.dot(d_qkv, w_qkv, preferred_element_type=jnp.float32).astype(jnp.bfloat16)
    joint_weight = across(d_qkv, tokens)
    out_ring.advance(len(ring) - 1)
    out_ring.state, joint_weight, grad_x = lax.optimization_barrier(
        (out_ring.state, joint_weight, grad_x)
    )
    grad_w_qkv = ring_scatter(joint_weight, ring, "ctx")
    grad_w_out = out_ring.result()
    return (out, grad_x, grad_w_qkv, grad_w_out)


def solution(mesh):
    return jax.shard_map(
        functools.partial(shards, ring_of(mesh)),
        mesh=mesh,
        in_specs=(P("ctx", "tp"), P("ctx"), P("ctx"), P(None, "tp"), P(None, "tp"), P("ctx", "tp")),
        out_specs=(P("ctx", "tp"), P("ctx", "tp"), P("ctx", "tp"), P("ctx", "tp")),
        check_vma=False,
    )
```

```python
import functools
import math

import jax
import jax.numpy as jnp
from jax import lax
from jax.sharding import PartitionSpec as P

HD = 128
HQ = 8


THETA = 500000.0
NEG = -1e30
PIECE = 64


def angles(place, width):
    half = width // 2
    freq = THETA ** (-(jnp.arange(half, dtype=jnp.float32) * 2.0 / width))
    turn = place.astype(jnp.float32)[:, None] * freq[None, :]
    return (jnp.cos(turn), jnp.sin(turn))


def rotate(vector, cosine, sine):
    half = vector.shape[-1] // 2
    first = vector[..., :half]
    second = vector[..., half:]
    return jnp.concatenate(
        [first * cosine - second * sine, second * cosine + first * sine], axis=-1
    )


def against(left, right):
    return lax.dot_general(
        left, right, (((1,), (1,)), ((), ())), preferred_element_type=jnp.float32
    )


def across(left, right):
    return lax.dot_general(
        left, right, (((0,), (0,)), ((), ())), preferred_element_type=jnp.float32
    )


def ring_of(mesh):
    count = mesh.shape["ctx"]
    try:
        grid = mesh.devices.reshape(count, -1)
        coords = [tuple(grid[i, 0].coords) for i in range(count)]
    except Exception:
        return list(range(count))
    varying = [d for d in range(len(coords[0])) if len({c[d] for c in coords}) > 1]
    if len(varying) == 1:
        return sorted(range(count), key=lambda i: coords[i][varying[0]])
    if len(varying) != 2:
        return list(range(count))
    for short, long in (varying, varying[::-1]):
        levels = sorted({c[short] for c in coords})
        if len(levels) == 2:
            there = sorted(
                (i for i in range(count) if coords[i][short] == levels[0]),
                key=lambda i: coords[i][long],
            )
            back = sorted(
                (i for i in range(count) if coords[i][short] == levels[1]),
                key=lambda i: -coords[i][long],
            )
            return there + back
    return list(range(count))


def ring_scatter(partial, ring, axis):
    count = len(ring)
    where = [0] * count
    for spot, member in enumerate(ring):
        where[member] = spot
    spot = jnp.asarray(where, jnp.int32)[lax.axis_index(axis)]
    order = jnp.asarray(ring, jnp.int32)
    rows = partial.shape[0] // count
    half = partial.shape[1] // 2
    blocks = partial.reshape(count, rows, partial.shape[1])
    left = blocks[:, :, :half]
    right = blocks[:, :, half:]

    def block(side, offset):
        return lax.dynamic_index_in_dim(side, order[(spot + offset) % count], 0, keepdims=False)

    forward = [(ring[p], ring[(p + 1) % count]) for p in range(count)]
    backward = [(ring[p], ring[(p - 1) % count]) for p in range(count)]
    send_left = block(left, count - 1)
    send_right = block(right, 1)
    for step in range(count - 1):
        got_left = lax.ppermute(send_left.astype(jnp.bfloat16), axis, forward)
        got_right = lax.ppermute(send_right.astype(jnp.bfloat16), axis, backward)
        send_left = got_left.astype(jnp.float32) + block(left, 2 * count - step - 2)
        send_right = got_right.astype(jnp.float32) + block(right, step + 2)
    return jnp.concatenate([send_left, send_right], axis=1)


def ring_spot(ring, axis):
    where = [0] * len(ring)
    for spot, member in enumerate(ring):
        where[member] = spot
    return jnp.asarray(where, jnp.int32)[lax.axis_index(axis)]


def ring_gather(value, ring, axis):
    count = len(ring)
    forward = [(ring[p], ring[(p + 1) % count]) for p in range(count)]
    backward = [(ring[p], ring[(p - 1) % count]) for p in range(count)]
    ahead = count // 2
    behind = count - 1 - ahead
    got = [value] + [None] * (count - 1)
    from_left = value
    from_right = value
    for step in range(max(ahead, behind)):
        if step < ahead:
            from_left = lax.ppermute(from_left, axis, forward)
            got[count - step - 1] = from_left
        if step < behind:
            from_right = lax.ppermute(from_right, axis, backward)
            got[step + 1] = from_right
    return jnp.stack(got, axis=0)


def ring_scatter_relative(partial, ring, axis):
    count = len(ring)
    rows = partial.shape[0] // count
    half = partial.shape[1] // 2
    blocks = partial.reshape(count, rows, partial.shape[1])
    left = blocks[:, :, :half]
    right = blocks[:, :, half:]
    forward = [(ring[p], ring[(p + 1) % count]) for p in range(count)]
    backward = [(ring[p], ring[(p - 1) % count]) for p in range(count)]
    send_left = left[count - 1]
    send_right = right[1 % count]
    for step in range(count - 1):
        got_left = lax.ppermute(send_left.astype(jnp.bfloat16), axis, forward)
        got_right = lax.ppermute(send_right.astype(jnp.bfloat16), axis, backward)
        send_left = got_left.astype(jnp.float32) + left[(2 * count - step - 2) % count]
        send_right = got_right.astype(jnp.float32) + right[(step + 2) % count]
    return jnp.concatenate([send_left, send_right], axis=1)


class Ring:
    def __init__(self, partial, ring, axis):
        count = len(ring)
        self.count = count
        self.axis = axis
        self.spot = ring_spot(ring, axis)
        self.order = jnp.asarray(ring, jnp.int32)
        rows = partial.shape[0] // count
        half = partial.shape[1] // 2
        blocks = partial.reshape(count, rows, partial.shape[1])
        self.left = blocks[:, :, :half]
        self.right = blocks[:, :, half:]
        self.forward = [(ring[p], ring[(p + 1) % count]) for p in range(count)]
        self.backward = [(ring[p], ring[(p - 1) % count]) for p in range(count)]
        self.state = (self.block(self.left, count - 1), self.block(self.right, 1))
        self.done = 0

    def block(self, side, offset):
        index = self.order[(self.spot + offset) % self.count]
        return lax.dynamic_index_in_dim(side, index, 0, keepdims=False)

    def advance(self, upto):
        count = self.count
        send_left, send_right = self.state
        for step in range(self.done, min(upto, count - 1)):
            got_left = lax.ppermute(send_left.astype(jnp.bfloat16), self.axis, self.forward)
            got_right = lax.ppermute(send_right.astype(jnp.bfloat16), self.axis, self.backward)
            send_left = got_left.astype(jnp.float32) + self.block(self.left, 2 * count - step - 2)
            send_right = got_right.astype(jnp.float32) + self.block(self.right, step + 2)
            self.done = step + 1
        self.state = (send_left, send_right)
        return self

    def result(self):
        self.advance(self.count - 1)
        return jnp.concatenate(list(self.state), axis=1)


def tp_project(partial, rows_mine, split, axis):
    rank = lax.axis_index(axis)
    core = rank % 2
    near = [(i, i ^ 1) for i in range(4)]
    far = [(i, i ^ 2) for i in range(4)]
    chip = partial + lax.ppermute(partial, axis, near)
    head = chip[:, :split]
    tail = chip[:, split:]
    half_rows = tail.shape[0] // 2
    mine = lax.dynamic_slice_in_dim(head, rank * rows_mine, rows_mine, 0)
    theirs = lax.dynamic_slice_in_dim(head, (rank ^ 2) * rows_mine, rows_mine, 0)
    own_head = mine + lax.ppermute(theirs, axis, far)
    tail_half = lax.dynamic_slice_in_dim(tail, core * half_rows, half_rows, 0)
    tail_half = tail_half + lax.ppermute(tail_half, axis, far)
    other_half = lax.ppermute(tail_half, axis, near)
    first = jnp.where(core == 0, tail_half, other_half)
    second = jnp.where(core == 0, other_half, tail_half)
    return own_head, jnp.concatenate([first, second], axis=0)


def tp_scatter(partial, rows_mine, axis):
    rank = lax.axis_index(axis)
    far = [(i, i ^ 2) for i in range(4)]
    near = [(i, i ^ 1) for i in range(4)]
    pair_rows = 2 * rows_mine
    chip = rank // 2
    kept = lax.dynamic_slice_in_dim(partial, chip * pair_rows, pair_rows, 0)
    sent = lax.dynamic_slice_in_dim(partial, (1 - chip) * pair_rows, pair_rows, 0)
    kept = kept.astype(jnp.float32) + lax.ppermute(
        sent.astype(jnp.bfloat16), axis, far
    ).astype(jnp.float32)
    core = rank % 2
    mine = lax.dynamic_slice_in_dim(kept, core * rows_mine, rows_mine, 0)
    other = lax.dynamic_slice_in_dim(kept, (1 - core) * rows_mine, rows_mine, 0)
    return mine + lax.ppermute(other.astype(jnp.bfloat16), axis, near).astype(jnp.float32)


def direct_gather(value, axis):
    count = lax.axis_size(axis)
    got = [value] + [None] * (count - 1)
    for shift in range(1, count):
        pairs = [(i, (i + shift) % count) for i in range(count)]
        got[count - shift] = lax.ppermute(value, axis, pairs)
    return jnp.stack(got, axis=0)


def direct_scatter(partial, axis):
    count = lax.axis_size(axis)
    rows = partial.shape[0] // count
    blocks = partial.reshape(count, rows, partial.shape[1])
    total = blocks[0]
    for shift in range(1, count):
        pairs = [(i, (i + shift) % count) for i in range(count)]
        total = total + lax.ppermute(blocks[shift].astype(jnp.bfloat16), axis, pairs).astype(
            jnp.float32
        )
    return total


def butterfly_sum(value, axis):
    count = lax.axis_size(axis)
    stride = 1
    while stride < count:
        pairs = [(i, i ^ stride) for i in range(count)]
        value = value + lax.ppermute(value, axis, pairs)
        stride *= 2
    return value


def shards(ring, tokens, document, place, w_qkv, w_out, grad_out):
    rows_ctx, slice_width = tokens.shape
    ctx_size = lax.axis_size("ctx")
    tp_size = lax.axis_size("tp")
    rows_mine = rows_ctx // tp_size
    tp_rank = lax.axis_index("tp")
    head_dim = HD
    heads = HQ
    heads_width = heads * head_dim
    pair_width = 2 * head_dim
    factor = 1.0 / math.sqrt(head_dim)
    first_row = tp_rank * rows_mine
    stacked = heads * rows_mine
    total_rows = ctx_size * rows_ctx

    grad_part = against(grad_out, w_out).astype(jnp.bfloat16)

    cosine_all, sine_all = angles(place, head_dim)
    cosine_mine = lax.dynamic_slice_in_dim(cosine_all, first_row, rows_mine, 0)
    sine_mine = lax.dynamic_slice_in_dim(sine_all, first_row, rows_mine, 0)
    query_doc = lax.dynamic_slice_in_dim(document, first_row, rows_mine, 0)
    query_place = lax.dynamic_slice_in_dim(place, first_row, rows_mine, 0)

    projected = against(tokens, w_qkv)
    if tp_size == 4 and rows_ctx % (2 * tp_size) == 0:
        query_block, pair_rows = tp_project(projected, rows_mine, heads_width, "tp")
    else:
        qkv = lax.psum(projected, "tp")
        query_block = lax.dynamic_slice_in_dim(qkv[:, :heads_width], first_row, rows_mine, 0)
        pair_rows = qkv[:, heads_width:]
    keys = rotate(pair_rows[:, :head_dim], cosine_all, sine_all).astype(jnp.bfloat16)
    values = pair_rows[:, head_dim:].astype(jnp.bfloat16)

    info = jnp.concatenate(
        [document, place // PIECE, place % PIECE], axis=0
    ).astype(jnp.float32)
    info_rows = -(-info.shape[0] // pair_width)
    info = jnp.pad(info, (0, info_rows * pair_width - info.shape[0]))
    info = info.reshape(info_rows, pair_width).astype(jnp.bfloat16)
    packed = jnp.concatenate([keys, values], axis=1)
    packed = jnp.concatenate([packed, info], axis=0)
    gathered = direct_gather(packed, "ctx")
    if tp_size == 4 and rows_ctx % (2 * tp_size) == 0:
        grad_rows = tp_scatter(grad_part, rows_mine, "tp").astype(jnp.bfloat16)
    else:
        grad_rows = lax.psum_scatter(grad_part, "tp", scatter_dimension=0, tiled=True)
    keys_all = gathered[:, :rows_ctx, :head_dim].reshape(total_rows, head_dim)
    values_all = gathered[:, :rows_ctx, head_dim:].reshape(total_rows, head_dim)
    info_all = gathered[:, rows_ctx:, :].reshape(ctx_size, info_rows * pair_width).astype(
        jnp.float32
    )
    key_doc = info_all[:, :rows_ctx].reshape(total_rows)
    key_place = (
        info_all[:, rows_ctx : 2 * rows_ctx] * PIECE + info_all[:, 2 * rows_ctx : 3 * rows_ctx]
    ).reshape(total_rows)

    allowed = (query_doc.astype(jnp.float32)[:, None] == key_doc[None, :]) & (
        key_place[None, :] <= query_place.astype(jnp.float32)[:, None]
    )
    allowed = jnp.broadcast_to(allowed[None], (heads, rows_mine, total_rows)).reshape(
        stacked, total_rows
    )

    raw_query = query_block.reshape(rows_mine, heads, head_dim)
    rotated = rotate(raw_query, cosine_mine[:, None, :], sine_mine[:, None, :]).astype(jnp.bfloat16)
    queries = jnp.transpose(rotated, (1, 0, 2)).reshape(stacked, head_dim)

    scores = against(queries, keys_all) * factor
    masked = jnp.where(allowed, scores, NEG)
    top = jnp.max(masked, axis=1)
    weights = jnp.where(allowed, jnp.exp(masked - top[:, None]), 0.0)
    total = jnp.sum(weights, axis=1)
    summed = jnp.dot(weights.astype(jnp.bfloat16), values_all, preferred_element_type=jnp.float32)
    attended = (summed / total[:, None]).astype(jnp.bfloat16)
    logsum = top + jnp.log(total)

    rows_attended = jnp.transpose(attended.reshape(heads, rows_mine, head_dim), (1, 0, 2)).reshape(
        rows_mine, heads_width
    )
    piece = lax.all_gather(rows_attended, "tp", axis=0, tiled=True)
    out = jnp.dot(piece, w_out, preferred_element_type=jnp.float32).astype(jnp.bfloat16)
    out_weight_grad = across(piece, grad_out)

    grad_stack = jnp.transpose(grad_rows.reshape(rows_mine, heads, head_dim), (1, 0, 2)).reshape(
        stacked, head_dim
    )
    delta = jnp.sum(grad_stack.astype(jnp.float32) * attended.astype(jnp.float32), axis=1)
    prob = jnp.where(allowed, jnp.exp(scores - logsum[:, None]), 0.0)
    dprob = against(grad_stack, values_all)
    dscore = (prob * (dprob - delta[:, None])).astype(jnp.bfloat16)
    query_sum = jnp.dot(dscore, keys_all, preferred_element_type=jnp.float32)
    key_part = across(dscore, queries) * factor
    value_part = across(prob.astype(jnp.bfloat16), grad_stack)
    pair_all = jnp.concatenate([key_part, value_part], axis=1)
    out_ring = Ring(out_weight_grad, ring, "ctx").advance(len(ring) // 4)
    pair_grad = butterfly_sum(direct_scatter(pair_all, "ctx"), "tp")
    out_ring.state, pair_grad = lax.optimization_barrier((out_ring.state, pair_grad))

    key_raw = rotate(pair_grad[:, :head_dim], cosine_all, -sine_all)
    query_grad = jnp.transpose((query_sum * factor).reshape(heads, rows_mine, head_dim), (1, 0, 2))
    query_raw = rotate(query_grad, cosine_mine[:, None, :], -sine_mine[:, None, :]).reshape(
        rows_mine, heads_width
    )
    query_rows = lax.all_gather(query_raw.astype(jnp.bfloat16), "tp", axis=0, tiled=True)
    d_qkv = jnp.concatenate(
        [query_rows, key_raw.astype(jnp.bfloat16), pair_grad[:, head_dim:].astype(jnp.bfloat16)],
        axis=1,
    )
    grad_x = jnp.dot(d_qkv, w_qkv, preferred_element_type=jnp.float32).astype(jnp.bfloat16)
    joint_weight = across(d_qkv, tokens)
    out_ring.advance(len(ring) - 1)
    out_ring.state, joint_weight = lax.optimization_barrier((out_ring.state, joint_weight))
    grad_w_qkv = ring_scatter(joint_weight, ring, "ctx")
    grad_w_out = out_ring.result()
    return (out, grad_x, grad_w_qkv, grad_w_out)


def solution(mesh):
    return jax.shard_map(
        functools.partial(shards, ring_of(mesh)),
        mesh=mesh,
        in_specs=(P("ctx", "tp"), P("ctx"), P("ctx"), P(None, "tp"), P(None, "tp"), P("ctx", "tp")),
        out_specs=(P("ctx", "tp"), P("ctx", "tp"), P("ctx", "tp"), P("ctx", "tp")),
        check_vma=False,
    )
```

```python
import functools
import math

import jax
import jax.numpy as jnp
from jax import lax
from jax.sharding import PartitionSpec as P

HD = 128
HQ = 8


THETA = 500000.0
NEG = -1e30
PIECE = 64


def angles(place, width):
    half = width // 2
    freq = THETA ** (-(jnp.arange(half, dtype=jnp.float32) * 2.0 / width))
    turn = place.astype(jnp.float32)[:, None] * freq[None, :]
    return (jnp.cos(turn), jnp.sin(turn))


def rotate(vector, cosine, sine):
    half = vector.shape[-1] // 2
    first = vector[..., :half]
    second = vector[..., half:]
    return jnp.concatenate(
        [first * cosine - second * sine, second * cosine + first * sine], axis=-1
    )


def against(left, right):
    return lax.dot_general(
        left, right, (((1,), (1,)), ((), ())), preferred_element_type=jnp.float32
    )


def across(left, right):
    return lax.dot_general(
        left, right, (((0,), (0,)), ((), ())), preferred_element_type=jnp.float32
    )


def ring_of(mesh):
    count = mesh.shape["ctx"]
    try:
        grid = mesh.devices.reshape(count, -1)
        coords = [tuple(grid[i, 0].coords) for i in range(count)]
    except Exception:
        return list(range(count))
    varying = [d for d in range(len(coords[0])) if len({c[d] for c in coords}) > 1]
    if len(varying) == 1:
        return sorted(range(count), key=lambda i: coords[i][varying[0]])
    if len(varying) != 2:
        return list(range(count))
    for short, long in (varying, varying[::-1]):
        levels = sorted({c[short] for c in coords})
        if len(levels) == 2:
            there = sorted(
                (i for i in range(count) if coords[i][short] == levels[0]),
                key=lambda i: coords[i][long],
            )
            back = sorted(
                (i for i in range(count) if coords[i][short] == levels[1]),
                key=lambda i: -coords[i][long],
            )
            return there + back
    return list(range(count))


def ring_scatter(partial, ring, axis):
    count = len(ring)
    where = [0] * count
    for spot, member in enumerate(ring):
        where[member] = spot
    spot = jnp.asarray(where, jnp.int32)[lax.axis_index(axis)]
    order = jnp.asarray(ring, jnp.int32)
    rows = partial.shape[0] // count
    half = partial.shape[1] // 2
    blocks = partial.reshape(count, rows, partial.shape[1])
    left = blocks[:, :, :half]
    right = blocks[:, :, half:]

    def block(side, offset):
        return lax.dynamic_index_in_dim(side, order[(spot + offset) % count], 0, keepdims=False)

    forward = [(ring[p], ring[(p + 1) % count]) for p in range(count)]
    backward = [(ring[p], ring[(p - 1) % count]) for p in range(count)]
    send_left = block(left, count - 1)
    send_right = block(right, 1)
    for step in range(count - 1):
        got_left = lax.ppermute(send_left.astype(jnp.bfloat16), axis, forward)
        got_right = lax.ppermute(send_right.astype(jnp.bfloat16), axis, backward)
        send_left = got_left.astype(jnp.float32) + block(left, 2 * count - step - 2)
        send_right = got_right.astype(jnp.float32) + block(right, step + 2)
    return jnp.concatenate([send_left, send_right], axis=1)


def ring_spot(ring, axis):
    where = [0] * len(ring)
    for spot, member in enumerate(ring):
        where[member] = spot
    return jnp.asarray(where, jnp.int32)[lax.axis_index(axis)]


def ring_gather(value, ring, axis):
    count = len(ring)
    forward = [(ring[p], ring[(p + 1) % count]) for p in range(count)]
    backward = [(ring[p], ring[(p - 1) % count]) for p in range(count)]
    ahead = count // 2
    behind = count - 1 - ahead
    got = [value] + [None] * (count - 1)
    from_left = value
    from_right = value
    for step in range(max(ahead, behind)):
        if step < ahead:
            from_left = lax.ppermute(from_left, axis, forward)
            got[count - step - 1] = from_left
        if step < behind:
            from_right = lax.ppermute(from_right, axis, backward)
            got[step + 1] = from_right
    return jnp.stack(got, axis=0)


def ring_scatter_relative(partial, ring, axis):
    count = len(ring)
    rows = partial.shape[0] // count
    half = partial.shape[1] // 2
    blocks = partial.reshape(count, rows, partial.shape[1])
    left = blocks[:, :, :half]
    right = blocks[:, :, half:]
    forward = [(ring[p], ring[(p + 1) % count]) for p in range(count)]
    backward = [(ring[p], ring[(p - 1) % count]) for p in range(count)]
    send_left = left[count - 1]
    send_right = right[1 % count]
    for step in range(count - 1):
        got_left = lax.ppermute(send_left.astype(jnp.bfloat16), axis, forward)
        got_right = lax.ppermute(send_right.astype(jnp.bfloat16), axis, backward)
        send_left = got_left.astype(jnp.float32) + left[(2 * count - step - 2) % count]
        send_right = got_right.astype(jnp.float32) + right[(step + 2) % count]
    return jnp.concatenate([send_left, send_right], axis=1)


class Ring:
    def __init__(self, partial, ring, axis):
        count = len(ring)
        self.count = count
        self.axis = axis
        self.spot = ring_spot(ring, axis)
        self.order = jnp.asarray(ring, jnp.int32)
        rows = partial.shape[0] // count
        half = partial.shape[1] // 2
        blocks = partial.reshape(count, rows, partial.shape[1])
        self.left = blocks[:, :, :half]
        self.right = blocks[:, :, half:]
        self.forward = [(ring[p], ring[(p + 1) % count]) for p in range(count)]
        self.backward = [(ring[p], ring[(p - 1) % count]) for p in range(count)]
        self.state = (self.block(self.left, count - 1), self.block(self.right, 1))
        self.done = 0

    def block(self, side, offset):
        index = self.order[(self.spot + offset) % self.count]
        return lax.dynamic_index_in_dim(side, index, 0, keepdims=False)

    def advance(self, upto):
        count = self.count
        send_left, send_right = self.state
        for step in range(self.done, min(upto, count - 1)):
            got_left = lax.ppermute(send_left.astype(jnp.bfloat16), self.axis, self.forward)
            got_right = lax.ppermute(send_right.astype(jnp.bfloat16), self.axis, self.backward)
            send_left = got_left.astype(jnp.float32) + self.block(self.left, 2 * count - step - 2)
            send_right = got_right.astype(jnp.float32) + self.block(self.right, step + 2)
            self.done = step + 1
        self.state = (send_left, send_right)
        return self

    def result(self):
        self.advance(self.count - 1)
        return jnp.concatenate(list(self.state), axis=1)


def tp_project(partial, rows_mine, split, axis):
    rank = lax.axis_index(axis)
    core = rank % 2
    near = [(i, i ^ 1) for i in range(4)]
    far = [(i, i ^ 2) for i in range(4)]
    chip = partial + lax.ppermute(partial, axis, near)
    head = chip[:, :split]
    tail = chip[:, split:]
    half_rows = tail.shape[0] // 2
    mine = lax.dynamic_slice_in_dim(head, rank * rows_mine, rows_mine, 0)
    theirs = lax.dynamic_slice_in_dim(head, (rank ^ 2) * rows_mine, rows_mine, 0)
    own_head = mine + lax.ppermute(theirs, axis, far)
    tail_half = lax.dynamic_slice_in_dim(tail, core * half_rows, half_rows, 0)
    tail_half = tail_half + lax.ppermute(tail_half, axis, far)
    other_half = lax.ppermute(tail_half, axis, near)
    first = jnp.where(core == 0, tail_half, other_half)
    second = jnp.where(core == 0, other_half, tail_half)
    return own_head, jnp.concatenate([first, second], axis=0)


def tp_scatter(partial, rows_mine, axis):
    rank = lax.axis_index(axis)
    far = [(i, i ^ 2) for i in range(4)]
    near = [(i, i ^ 1) for i in range(4)]
    pair_rows = 2 * rows_mine
    chip = rank // 2
    kept = lax.dynamic_slice_in_dim(partial, chip * pair_rows, pair_rows, 0)
    sent = lax.dynamic_slice_in_dim(partial, (1 - chip) * pair_rows, pair_rows, 0)
    kept = kept.astype(jnp.float32) + lax.ppermute(
        sent.astype(jnp.bfloat16), axis, far
    ).astype(jnp.float32)
    core = rank % 2
    mine = lax.dynamic_slice_in_dim(kept, core * rows_mine, rows_mine, 0)
    other = lax.dynamic_slice_in_dim(kept, (1 - core) * rows_mine, rows_mine, 0)
    return mine + lax.ppermute(other.astype(jnp.bfloat16), axis, near).astype(jnp.float32)


def direct_gather(value, axis):
    count = lax.axis_size(axis)
    got = [value] + [None] * (count - 1)
    for shift in range(1, count):
        pairs = [(i, (i + shift) % count) for i in range(count)]
        got[count - shift] = lax.ppermute(value, axis, pairs)
    return jnp.stack(got, axis=0)


def direct_scatter(partial, axis):
    count = lax.axis_size(axis)
    rows = partial.shape[0] // count
    blocks = partial.reshape(count, rows, partial.shape[1])
    total = blocks[0]
    for shift in range(1, count):
        pairs = [(i, (i + shift) % count) for i in range(count)]
        total = total + lax.ppermute(blocks[shift].astype(jnp.bfloat16), axis, pairs).astype(
            jnp.float32
        )
    return total


def butterfly_sum(value, axis):
    count = lax.axis_size(axis)
    stride = 1
    while stride < count:
        pairs = [(i, i ^ stride) for i in range(count)]
        value = value + lax.ppermute(value, axis, pairs)
        stride *= 2
    return value


def shards(ring, tokens, document, place, w_qkv, w_out, grad_out):
    rows_ctx, slice_width = tokens.shape
    ctx_size = lax.axis_size("ctx")
    tp_size = lax.axis_size("tp")
    rows_mine = rows_ctx // tp_size
    tp_rank = lax.axis_index("tp")
    head_dim = HD
    heads = HQ
    heads_width = heads * head_dim
    pair_width = 2 * head_dim
    factor = 1.0 / math.sqrt(head_dim)
    first_row = tp_rank * rows_mine
    stacked = heads * rows_mine
    total_rows = ctx_size * rows_ctx

    grad_part = against(grad_out, w_out).astype(jnp.bfloat16)

    cosine_all, sine_all = angles(place, head_dim)
    cosine_mine = lax.dynamic_slice_in_dim(cosine_all, first_row, rows_mine, 0)
    sine_mine = lax.dynamic_slice_in_dim(sine_all, first_row, rows_mine, 0)
    query_doc = lax.dynamic_slice_in_dim(document, first_row, rows_mine, 0)
    query_place = lax.dynamic_slice_in_dim(place, first_row, rows_mine, 0)

    projected = against(tokens, w_qkv)
    if tp_size == 4 and rows_ctx % (2 * tp_size) == 0:
        query_block, pair_rows = tp_project(projected, rows_mine, heads_width, "tp")
    else:
        qkv = lax.psum(projected, "tp")
        query_block = lax.dynamic_slice_in_dim(qkv[:, :heads_width], first_row, rows_mine, 0)
        pair_rows = qkv[:, heads_width:]
    keys = rotate(pair_rows[:, :head_dim], cosine_all, sine_all).astype(jnp.bfloat16)
    values = pair_rows[:, head_dim:].astype(jnp.bfloat16)

    info = jnp.concatenate(
        [document, place // PIECE, place % PIECE], axis=0
    ).astype(jnp.float32)
    info_rows = -(-info.shape[0] // pair_width)
    info = jnp.pad(info, (0, info_rows * pair_width - info.shape[0]))
    info = info.reshape(info_rows, pair_width).astype(jnp.bfloat16)
    packed = jnp.concatenate([keys, values], axis=1)
    packed = jnp.concatenate([packed, info], axis=0)
    gathered = direct_gather(packed, "ctx")
    if tp_size == 4 and rows_ctx % (2 * tp_size) == 0:
        grad_rows = tp_scatter(grad_part, rows_mine, "tp").astype(jnp.bfloat16)
    else:
        grad_rows = lax.psum_scatter(grad_part, "tp", scatter_dimension=0, tiled=True)
    keys_all = gathered[:, :rows_ctx, :head_dim].reshape(total_rows, head_dim)
    values_all = gathered[:, :rows_ctx, head_dim:].reshape(total_rows, head_dim)
    info_all = gathered[:, rows_ctx:, :].reshape(ctx_size, info_rows * pair_width).astype(
        jnp.float32
    )
    key_doc = info_all[:, :rows_ctx].reshape(total_rows)
    key_place = (
        info_all[:, rows_ctx : 2 * rows_ctx] * PIECE + info_all[:, 2 * rows_ctx : 3 * rows_ctx]
    ).reshape(total_rows)

    allowed = (query_doc.astype(jnp.float32)[:, None] == key_doc[None, :]) & (
        key_place[None, :] <= query_place.astype(jnp.float32)[:, None]
    )
    allowed = jnp.broadcast_to(allowed[None], (heads, rows_mine, total_rows)).reshape(
        stacked, total_rows
    )

    raw_query = query_block.reshape(rows_mine, heads, head_dim)
    rotated = rotate(raw_query, cosine_mine[:, None, :], sine_mine[:, None, :]).astype(jnp.bfloat16)
    queries = jnp.transpose(rotated, (1, 0, 2)).reshape(stacked, head_dim)

    scores = against(queries, keys_all) * factor
    masked = jnp.where(allowed, scores, NEG)
    top = jnp.max(masked, axis=1)
    weights = jnp.where(allowed, jnp.exp(masked - top[:, None]), 0.0)
    total = jnp.sum(weights, axis=1)
    summed = jnp.dot(weights.astype(jnp.bfloat16), values_all, preferred_element_type=jnp.float32)
    attended = (summed / total[:, None]).astype(jnp.bfloat16)
    logsum = top + jnp.log(total)

    rows_attended = jnp.transpose(attended.reshape(heads, rows_mine, head_dim), (1, 0, 2)).reshape(
        rows_mine, heads_width
    )
    piece = lax.all_gather(rows_attended, "tp", axis=0, tiled=True)
    out = jnp.dot(piece, w_out, preferred_element_type=jnp.float32).astype(jnp.bfloat16)
    out_weight_grad = across(piece, grad_out)

    grad_stack = jnp.transpose(grad_rows.reshape(rows_mine, heads, head_dim), (1, 0, 2)).reshape(
        stacked, head_dim
    )
    delta = jnp.sum(grad_stack.astype(jnp.float32) * attended.astype(jnp.float32), axis=1)
    prob = jnp.where(allowed, jnp.exp(scores - logsum[:, None]), 0.0)
    dprob = against(grad_stack, values_all)
    dscore = (prob * (dprob - delta[:, None])).astype(jnp.bfloat16)
    query_sum = jnp.dot(dscore, keys_all, preferred_element_type=jnp.float32)
    key_part = across(dscore, queries) * factor
    value_part = across(prob.astype(jnp.bfloat16), grad_stack)
    pair_all = jnp.concatenate([key_part, value_part], axis=1)
    out_ring = Ring(out_weight_grad, ring, "ctx").advance(len(ring) // 8)
    pair_grad = butterfly_sum(direct_scatter(pair_all, "ctx"), "tp")
    out_ring.state, pair_grad = lax.optimization_barrier((out_ring.state, pair_grad))

    key_raw = rotate(pair_grad[:, :head_dim], cosine_all, -sine_all)
    query_grad = jnp.transpose((query_sum * factor).reshape(heads, rows_mine, head_dim), (1, 0, 2))
    query_raw = rotate(query_grad, cosine_mine[:, None, :], -sine_mine[:, None, :]).reshape(
        rows_mine, heads_width
    )
    query_rows = lax.all_gather(query_raw.astype(jnp.bfloat16), "tp", axis=0, tiled=True)
    d_qkv = jnp.concatenate(
        [query_rows, key_raw.astype(jnp.bfloat16), pair_grad[:, head_dim:].astype(jnp.bfloat16)],
        axis=1,
    )
    grad_x = jnp.dot(d_qkv, w_qkv, preferred_element_type=jnp.float32).astype(jnp.bfloat16)
    joint_weight = across(d_qkv, tokens)
    out_ring.advance(len(ring) - 1)
    out_ring.state, joint_weight = lax.optimization_barrier((out_ring.state, joint_weight))
    grad_w_qkv = ring_scatter(joint_weight, ring, "ctx")
    grad_w_out = out_ring.result()
    return (out, grad_x, grad_w_qkv, grad_w_out)


def solution(mesh):
    return jax.shard_map(
        functools.partial(shards, ring_of(mesh)),
        mesh=mesh,
        in_specs=(P("ctx", "tp"), P("ctx"), P("ctx"), P(None, "tp"), P(None, "tp"), P("ctx", "tp")),
        out_specs=(P("ctx", "tp"), P("ctx", "tp"), P("ctx", "tp"), P("ctx", "tp")),
        check_vma=False,
    )
```

```python
import functools
import math

import jax
import jax.numpy as jnp
from jax import lax
from jax.sharding import PartitionSpec as P

HD = 128
HQ = 8


THETA = 500000.0
NEG = -1e30
PIECE = 64


def angles(place, width):
    half = width // 2
    freq = THETA ** (-(jnp.arange(half, dtype=jnp.float32) * 2.0 / width))
    turn = place.astype(jnp.float32)[:, None] * freq[None, :]
    return (jnp.cos(turn), jnp.sin(turn))


def rotate(vector, cosine, sine):
    half = vector.shape[-1] // 2
    first = vector[..., :half]
    second = vector[..., half:]
    return jnp.concatenate(
        [first * cosine - second * sine, second * cosine + first * sine], axis=-1
    )


def against(left, right):
    return lax.dot_general(
        left, right, (((1,), (1,)), ((), ())), preferred_element_type=jnp.float32
    )


def across(left, right):
    return lax.dot_general(
        left, right, (((0,), (0,)), ((), ())), preferred_element_type=jnp.float32
    )


def ring_of(mesh):
    count = mesh.shape["ctx"]
    try:
        grid = mesh.devices.reshape(count, -1)
        coords = [tuple(grid[i, 0].coords) for i in range(count)]
    except Exception:
        return list(range(count))
    varying = [d for d in range(len(coords[0])) if len({c[d] for c in coords}) > 1]
    if len(varying) == 1:
        return sorted(range(count), key=lambda i: coords[i][varying[0]])
    if len(varying) != 2:
        return list(range(count))
    for short, long in (varying, varying[::-1]):
        levels = sorted({c[short] for c in coords})
        if len(levels) == 2:
            there = sorted(
                (i for i in range(count) if coords[i][short] == levels[0]),
                key=lambda i: coords[i][long],
            )
            back = sorted(
                (i for i in range(count) if coords[i][short] == levels[1]),
                key=lambda i: -coords[i][long],
            )
            return there + back
    return list(range(count))


def ring_scatter(partial, ring, axis):
    count = len(ring)
    where = [0] * count
    for spot, member in enumerate(ring):
        where[member] = spot
    spot = jnp.asarray(where, jnp.int32)[lax.axis_index(axis)]
    order = jnp.asarray(ring, jnp.int32)
    rows = partial.shape[0] // count
    half = partial.shape[1] // 2
    blocks = partial.reshape(count, rows, partial.shape[1])
    left = blocks[:, :, :half]
    right = blocks[:, :, half:]

    def block(side, offset):
        return lax.dynamic_index_in_dim(side, order[(spot + offset) % count], 0, keepdims=False)

    forward = [(ring[p], ring[(p + 1) % count]) for p in range(count)]
    backward = [(ring[p], ring[(p - 1) % count]) for p in range(count)]
    send_left = block(left, count - 1)
    send_right = block(right, 1)
    for step in range(count - 1):
        got_left = lax.ppermute(send_left.astype(jnp.bfloat16), axis, forward)
        got_right = lax.ppermute(send_right.astype(jnp.bfloat16), axis, backward)
        send_left = got_left.astype(jnp.float32) + block(left, 2 * count - step - 2)
        send_right = got_right.astype(jnp.float32) + block(right, step + 2)
    return jnp.concatenate([send_left, send_right], axis=1)


def ring_spot(ring, axis):
    where = [0] * len(ring)
    for spot, member in enumerate(ring):
        where[member] = spot
    return jnp.asarray(where, jnp.int32)[lax.axis_index(axis)]


def ring_gather(value, ring, axis):
    count = len(ring)
    forward = [(ring[p], ring[(p + 1) % count]) for p in range(count)]
    backward = [(ring[p], ring[(p - 1) % count]) for p in range(count)]
    ahead = count // 2
    behind = count - 1 - ahead
    got = [value] + [None] * (count - 1)
    from_left = value
    from_right = value
    for step in range(max(ahead, behind)):
        if step < ahead:
            from_left = lax.ppermute(from_left, axis, forward)
            got[count - step - 1] = from_left
        if step < behind:
            from_right = lax.ppermute(from_right, axis, backward)
            got[step + 1] = from_right
    return jnp.stack(got, axis=0)


def ring_scatter_relative(partial, ring, axis):
    count = len(ring)
    rows = partial.shape[0] // count
    half = partial.shape[1] // 2
    blocks = partial.reshape(count, rows, partial.shape[1])
    left = blocks[:, :, :half]
    right = blocks[:, :, half:]
    forward = [(ring[p], ring[(p + 1) % count]) for p in range(count)]
    backward = [(ring[p], ring[(p - 1) % count]) for p in range(count)]
    send_left = left[count - 1]
    send_right = right[1 % count]
    for step in range(count - 1):
        got_left = lax.ppermute(send_left.astype(jnp.bfloat16), axis, forward)
        got_right = lax.ppermute(send_right.astype(jnp.bfloat16), axis, backward)
        send_left = got_left.astype(jnp.float32) + left[(2 * count - step - 2) % count]
        send_right = got_right.astype(jnp.float32) + right[(step + 2) % count]
    return jnp.concatenate([send_left, send_right], axis=1)


class Ring:
    def __init__(self, partial, ring, axis):
        count = len(ring)
        self.count = count
        self.axis = axis
        self.spot = ring_spot(ring, axis)
        self.order = jnp.asarray(ring, jnp.int32)
        rows = partial.shape[0] // count
        half = partial.shape[1] // 2
        blocks = partial.reshape(count, rows, partial.shape[1])
        self.left = blocks[:, :, :half]
        self.right = blocks[:, :, half:]
        self.forward = [(ring[p], ring[(p + 1) % count]) for p in range(count)]
        self.backward = [(ring[p], ring[(p - 1) % count]) for p in range(count)]
        self.state = (self.block(self.left, count - 1), self.block(self.right, 1))
        self.done = 0

    def block(self, side, offset):
        index = self.order[(self.spot + offset) % self.count]
        return lax.dynamic_index_in_dim(side, index, 0, keepdims=False)

    def advance(self, upto):
        count = self.count
        send_left, send_right = self.state
        for step in range(self.done, min(upto, count - 1)):
            got_left = lax.ppermute(send_left.astype(jnp.bfloat16), self.axis, self.forward)
            got_right = lax.ppermute(send_right.astype(jnp.bfloat16), self.axis, self.backward)
            send_left = got_left.astype(jnp.float32) + self.block(self.left, 2 * count - step - 2)
            send_right = got_right.astype(jnp.float32) + self.block(self.right, step + 2)
            self.done = step + 1
        self.state = (send_left, send_right)
        return self

    def result(self):
        self.advance(self.count - 1)
        return jnp.concatenate(list(self.state), axis=1)


def tp_project(partial, rows_mine, split, axis):
    rank = lax.axis_index(axis)
    core = rank % 2
    near = [(i, i ^ 1) for i in range(4)]
    far = [(i, i ^ 2) for i in range(4)]
    chip = partial + lax.ppermute(partial, axis, near)
    head = chip[:, :split]
    tail = chip[:, split:]
    half_rows = tail.shape[0] // 2
    mine = lax.dynamic_slice_in_dim(head, rank * rows_mine, rows_mine, 0)
    theirs = lax.dynamic_slice_in_dim(head, (rank ^ 2) * rows_mine, rows_mine, 0)
    own_head = mine + lax.ppermute(theirs, axis, far)
    tail_half = lax.dynamic_slice_in_dim(tail, core * half_rows, half_rows, 0)
    tail_half = tail_half + lax.ppermute(tail_half, axis, far)
    other_half = lax.ppermute(tail_half, axis, near)
    first = jnp.where(core == 0, tail_half, other_half)
    second = jnp.where(core == 0, other_half, tail_half)
    return own_head, jnp.concatenate([first, second], axis=0)


def tp_scatter(partial, rows_mine, axis):
    rank = lax.axis_index(axis)
    far = [(i, i ^ 2) for i in range(4)]
    near = [(i, i ^ 1) for i in range(4)]
    pair_rows = 2 * rows_mine
    chip = rank // 2
    kept = lax.dynamic_slice_in_dim(partial, chip * pair_rows, pair_rows, 0)
    sent = lax.dynamic_slice_in_dim(partial, (1 - chip) * pair_rows, pair_rows, 0)
    kept = kept.astype(jnp.float32) + lax.ppermute(
        sent.astype(jnp.bfloat16), axis, far
    ).astype(jnp.float32)
    core = rank % 2
    mine = lax.dynamic_slice_in_dim(kept, core * rows_mine, rows_mine, 0)
    other = lax.dynamic_slice_in_dim(kept, (1 - core) * rows_mine, rows_mine, 0)
    return mine + lax.ppermute(other.astype(jnp.bfloat16), axis, near).astype(jnp.float32)


def direct_gather(value, axis):
    count = lax.axis_size(axis)
    got = [value] + [None] * (count - 1)
    for shift in range(1, count):
        pairs = [(i, (i + shift) % count) for i in range(count)]
        got[count - shift] = lax.ppermute(value, axis, pairs)
    return jnp.stack(got, axis=0)


def direct_scatter(partial, axis):
    count = lax.axis_size(axis)
    rows = partial.shape[0] // count
    blocks = partial.reshape(count, rows, partial.shape[1])
    total = blocks[0]
    for shift in range(1, count):
        pairs = [(i, (i + shift) % count) for i in range(count)]
        total = total + lax.ppermute(blocks[shift].astype(jnp.bfloat16), axis, pairs).astype(
            jnp.float32
        )
    return total


def butterfly_sum(value, axis):
    count = lax.axis_size(axis)
    stride = 1
    while stride < count:
        pairs = [(i, i ^ stride) for i in range(count)]
        value = value + lax.ppermute(value, axis, pairs)
        stride *= 2
    return value


def shards(ring, tokens, document, place, w_qkv, w_out, grad_out):
    rows_ctx, slice_width = tokens.shape
    ctx_size = lax.axis_size("ctx")
    tp_size = lax.axis_size("tp")
    rows_mine = rows_ctx // tp_size
    tp_rank = lax.axis_index("tp")
    head_dim = HD
    heads = HQ
    heads_width = heads * head_dim
    pair_width = 2 * head_dim
    factor = 1.0 / math.sqrt(head_dim)
    first_row = tp_rank * rows_mine
    stacked = heads * rows_mine
    total_rows = ctx_size * rows_ctx

    grad_part = against(grad_out, w_out).astype(jnp.bfloat16)

    cosine_all, sine_all = angles(place, head_dim)
    cosine_mine = lax.dynamic_slice_in_dim(cosine_all, first_row, rows_mine, 0)
    sine_mine = lax.dynamic_slice_in_dim(sine_all, first_row, rows_mine, 0)
    query_doc = lax.dynamic_slice_in_dim(document, first_row, rows_mine, 0)
    query_place = lax.dynamic_slice_in_dim(place, first_row, rows_mine, 0)

    projected = against(tokens, w_qkv)
    if tp_size == 4 and rows_ctx % (2 * tp_size) == 0:
        query_block, pair_rows = tp_project(projected, rows_mine, heads_width, "tp")
    else:
        qkv = lax.psum(projected, "tp")
        query_block = lax.dynamic_slice_in_dim(qkv[:, :heads_width], first_row, rows_mine, 0)
        pair_rows = qkv[:, heads_width:]
    keys = rotate(pair_rows[:, :head_dim], cosine_all, sine_all).astype(jnp.bfloat16)
    values = pair_rows[:, head_dim:].astype(jnp.bfloat16)

    info = jnp.concatenate(
        [document, place // PIECE, place % PIECE], axis=0
    ).astype(jnp.float32)
    info_rows = -(-info.shape[0] // pair_width)
    info = jnp.pad(info, (0, info_rows * pair_width - info.shape[0]))
    info = info.reshape(info_rows, pair_width).astype(jnp.bfloat16)
    packed = jnp.concatenate([keys, values], axis=1)
    packed = jnp.concatenate([packed, info], axis=0)
    gathered = direct_gather(packed, "ctx")
    if tp_size == 4 and rows_ctx % (2 * tp_size) == 0:
        grad_rows = tp_scatter(grad_part, rows_mine, "tp").astype(jnp.bfloat16)
    else:
        grad_rows = lax.psum_scatter(grad_part, "tp", scatter_dimension=0, tiled=True)
    keys_all = gathered[:, :rows_ctx, :head_dim].reshape(total_rows, head_dim)
    values_all = gathered[:, :rows_ctx, head_dim:].reshape(total_rows, head_dim)
    info_all = gathered[:, rows_ctx:, :].reshape(ctx_size, info_rows * pair_width).astype(
        jnp.float32
    )
    key_doc = info_all[:, :rows_ctx].reshape(total_rows)
    key_place = (
        info_all[:, rows_ctx : 2 * rows_ctx] * PIECE + info_all[:, 2 * rows_ctx : 3 * rows_ctx]
    ).reshape(total_rows)

    allowed = (query_doc.astype(jnp.float32)[:, None] == key_doc[None, :]) & (
        key_place[None, :] <= query_place.astype(jnp.float32)[:, None]
    )
    allowed = jnp.broadcast_to(allowed[None], (heads, rows_mine, total_rows)).reshape(
        stacked, total_rows
    )

    raw_query = query_block.reshape(rows_mine, heads, head_dim)
    rotated = rotate(raw_query, cosine_mine[:, None, :], sine_mine[:, None, :]).astype(jnp.bfloat16)
    queries = jnp.transpose(rotated, (1, 0, 2)).reshape(stacked, head_dim)

    scores = against(queries, keys_all) * factor
    masked = jnp.where(allowed, scores, NEG)
    top = jnp.max(masked, axis=1)
    weights = jnp.where(allowed, jnp.exp(masked - top[:, None]), 0.0)
    total = jnp.sum(weights, axis=1)
    summed = jnp.dot(weights.astype(jnp.bfloat16), values_all, preferred_element_type=jnp.float32)
    attended = (summed / total[:, None]).astype(jnp.bfloat16)
    logsum = top + jnp.log(total)

    rows_attended = jnp.transpose(attended.reshape(heads, rows_mine, head_dim), (1, 0, 2)).reshape(
        rows_mine, heads_width
    )
    piece = lax.all_gather(rows_attended, "tp", axis=0, tiled=True)
    out = jnp.dot(piece, w_out, preferred_element_type=jnp.float32).astype(jnp.bfloat16)
    out_weight_grad = across(piece, grad_out)

    grad_stack = jnp.transpose(grad_rows.reshape(rows_mine, heads, head_dim), (1, 0, 2)).reshape(
        stacked, head_dim
    )
    delta = jnp.sum(grad_stack.astype(jnp.float32) * attended.astype(jnp.float32), axis=1)
    prob = jnp.where(allowed, jnp.exp(scores - logsum[:, None]), 0.0)
    dprob = against(grad_stack, values_all)
    dscore = (prob * (dprob - delta[:, None])).astype(jnp.bfloat16)
    query_sum = jnp.dot(dscore, keys_all, preferred_element_type=jnp.float32)
    key_part = across(dscore, queries) * factor
    value_part = across(prob.astype(jnp.bfloat16), grad_stack)
    pair_all = jnp.concatenate([key_part, value_part], axis=1)
    out_ring = Ring(out_weight_grad, ring, "ctx").advance(3 * len(ring) // 8)
    pair_grad = butterfly_sum(direct_scatter(pair_all, "ctx"), "tp")
    out_ring.state, pair_grad = lax.optimization_barrier((out_ring.state, pair_grad))

    key_raw = rotate(pair_grad[:, :head_dim], cosine_all, -sine_all)
    query_grad = jnp.transpose((query_sum * factor).reshape(heads, rows_mine, head_dim), (1, 0, 2))
    query_raw = rotate(query_grad, cosine_mine[:, None, :], -sine_mine[:, None, :]).reshape(
        rows_mine, heads_width
    )
    query_rows = lax.all_gather(query_raw.astype(jnp.bfloat16), "tp", axis=0, tiled=True)
    d_qkv = jnp.concatenate(
        [query_rows, key_raw.astype(jnp.bfloat16), pair_grad[:, head_dim:].astype(jnp.bfloat16)],
        axis=1,
    )
    grad_x = jnp.dot(d_qkv, w_qkv, preferred_element_type=jnp.float32).astype(jnp.bfloat16)
    joint_weight = across(d_qkv, tokens)
    out_ring.advance(len(ring) - 1)
    out_ring.state, joint_weight = lax.optimization_barrier((out_ring.state, joint_weight))
    grad_w_qkv = ring_scatter(joint_weight, ring, "ctx")
    grad_w_out = out_ring.result()
    return (out, grad_x, grad_w_qkv, grad_w_out)


def solution(mesh):
    return jax.shard_map(
        functools.partial(shards, ring_of(mesh)),
        mesh=mesh,
        in_specs=(P("ctx", "tp"), P("ctx"), P("ctx"), P(None, "tp"), P(None, "tp"), P("ctx", "tp")),
        out_specs=(P("ctx", "tp"), P("ctx", "tp"), P("ctx", "tp"), P("ctx", "tp")),
        check_vma=False,
    )
```

```python
import functools
import math

import jax
import jax.numpy as jnp
from jax import lax
from jax.sharding import PartitionSpec as P

HD = 128
HQ = 8


THETA = 500000.0
NEG = -1e30
PIECE = 64


def angles(place, width):
    half = width // 2
    freq = THETA ** (-(jnp.arange(half, dtype=jnp.float32) * 2.0 / width))
    turn = place.astype(jnp.float32)[:, None] * freq[None, :]
    return (jnp.cos(turn), jnp.sin(turn))


def rotate(vector, cosine, sine):
    half = vector.shape[-1] // 2
    first = vector[..., :half]
    second = vector[..., half:]
    return jnp.concatenate(
        [first * cosine - second * sine, second * cosine + first * sine], axis=-1
    )


def against(left, right):
    return lax.dot_general(
        left, right, (((1,), (1,)), ((), ())), preferred_element_type=jnp.float32
    )


def across(left, right):
    return lax.dot_general(
        left, right, (((0,), (0,)), ((), ())), preferred_element_type=jnp.float32
    )


def ring_of(mesh):
    count = mesh.shape["ctx"]
    try:
        grid = mesh.devices.reshape(count, -1)
        coords = [tuple(grid[i, 0].coords) for i in range(count)]
    except Exception:
        return list(range(count))
    varying = [d for d in range(len(coords[0])) if len({c[d] for c in coords}) > 1]
    if len(varying) == 1:
        return sorted(range(count), key=lambda i: coords[i][varying[0]])
    if len(varying) != 2:
        return list(range(count))
    for short, long in (varying, varying[::-1]):
        levels = sorted({c[short] for c in coords})
        if len(levels) == 2:
            there = sorted(
                (i for i in range(count) if coords[i][short] == levels[0]),
                key=lambda i: coords[i][long],
            )
            back = sorted(
                (i for i in range(count) if coords[i][short] == levels[1]),
                key=lambda i: -coords[i][long],
            )
            return there + back
    return list(range(count))


def ring_scatter(partial, ring, axis):
    count = len(ring)
    where = [0] * count
    for spot, member in enumerate(ring):
        where[member] = spot
    spot = jnp.asarray(where, jnp.int32)[lax.axis_index(axis)]
    order = jnp.asarray(ring, jnp.int32)
    rows = partial.shape[0] // count
    half = partial.shape[1] // 2
    blocks = partial.reshape(count, rows, partial.shape[1])
    left = blocks[:, :, :half]
    right = blocks[:, :, half:]

    def block(side, offset):
        return lax.dynamic_index_in_dim(side, order[(spot + offset) % count], 0, keepdims=False)

    forward = [(ring[p], ring[(p + 1) % count]) for p in range(count)]
    backward = [(ring[p], ring[(p - 1) % count]) for p in range(count)]
    send_left = block(left, count - 1)
    send_right = block(right, 1)
    for step in range(count - 1):
        got_left = lax.ppermute(send_left.astype(jnp.bfloat16), axis, forward)
        got_right = lax.ppermute(send_right.astype(jnp.bfloat16), axis, backward)
        send_left = got_left.astype(jnp.float32) + block(left, 2 * count - step - 2)
        send_right = got_right.astype(jnp.float32) + block(right, step + 2)
    return jnp.concatenate([send_left, send_right], axis=1)


def ring_spot(ring, axis):
    where = [0] * len(ring)
    for spot, member in enumerate(ring):
        where[member] = spot
    return jnp.asarray(where, jnp.int32)[lax.axis_index(axis)]


def ring_gather(value, ring, axis):
    count = len(ring)
    forward = [(ring[p], ring[(p + 1) % count]) for p in range(count)]
    backward = [(ring[p], ring[(p - 1) % count]) for p in range(count)]
    ahead = count // 2
    behind = count - 1 - ahead
    got = [value] + [None] * (count - 1)
    from_left = value
    from_right = value
    for step in range(max(ahead, behind)):
        if step < ahead:
            from_left = lax.ppermute(from_left, axis, forward)
            got[count - step - 1] = from_left
        if step < behind:
            from_right = lax.ppermute(from_right, axis, backward)
            got[step + 1] = from_right
    return jnp.stack(got, axis=0)


def ring_scatter_relative(partial, ring, axis):
    count = len(ring)
    rows = partial.shape[0] // count
    half = partial.shape[1] // 2
    blocks = partial.reshape(count, rows, partial.shape[1])
    left = blocks[:, :, :half]
    right = blocks[:, :, half:]
    forward = [(ring[p], ring[(p + 1) % count]) for p in range(count)]
    backward = [(ring[p], ring[(p - 1) % count]) for p in range(count)]
    send_left = left[count - 1]
    send_right = right[1 % count]
    for step in range(count - 1):
        got_left = lax.ppermute(send_left.astype(jnp.bfloat16), axis, forward)
        got_right = lax.ppermute(send_right.astype(jnp.bfloat16), axis, backward)
        send_left = got_left.astype(jnp.float32) + left[(2 * count - step - 2) % count]
        send_right = got_right.astype(jnp.float32) + right[(step + 2) % count]
    return jnp.concatenate([send_left, send_right], axis=1)


class Ring:
    def __init__(self, partial, ring, axis):
        count = len(ring)
        self.count = count
        self.axis = axis
        self.spot = ring_spot(ring, axis)
        self.order = jnp.asarray(ring, jnp.int32)
        rows = partial.shape[0] // count
        half = partial.shape[1] // 2
        blocks = partial.reshape(count, rows, partial.shape[1])
        self.left = blocks[:, :, :half]
        self.right = blocks[:, :, half:]
        self.forward = [(ring[p], ring[(p + 1) % count]) for p in range(count)]
        self.backward = [(ring[p], ring[(p - 1) % count]) for p in range(count)]
        self.state = (self.block(self.left, count - 1), self.block(self.right, 1))
        self.done = 0

    def block(self, side, offset):
        index = self.order[(self.spot + offset) % self.count]
        return lax.dynamic_index_in_dim(side, index, 0, keepdims=False)

    def advance(self, upto):
        count = self.count
        send_left, send_right = self.state
        for step in range(self.done, min(upto, count - 1)):
            got_left = lax.ppermute(send_left.astype(jnp.bfloat16), self.axis, self.forward)
            got_right = lax.ppermute(send_right.astype(jnp.bfloat16), self.axis, self.backward)
            send_left = got_left.astype(jnp.float32) + self.block(self.left, 2 * count - step - 2)
            send_right = got_right.astype(jnp.float32) + self.block(self.right, step + 2)
            self.done = step + 1
        self.state = (send_left, send_right)
        return self

    def result(self):
        self.advance(self.count - 1)
        return jnp.concatenate(list(self.state), axis=1)


def tp_project(partial, rows_mine, split, axis):
    rank = lax.axis_index(axis)
    core = rank % 2
    near = [(i, i ^ 1) for i in range(4)]
    far = [(i, i ^ 2) for i in range(4)]
    chip = partial + lax.ppermute(partial, axis, near)
    head = chip[:, :split]
    tail = chip[:, split:]
    half_rows = tail.shape[0] // 2
    mine = lax.dynamic_slice_in_dim(head, rank * rows_mine, rows_mine, 0)
    theirs = lax.dynamic_slice_in_dim(head, (rank ^ 2) * rows_mine, rows_mine, 0)
    own_head = mine + lax.ppermute(theirs, axis, far)
    tail_half = lax.dynamic_slice_in_dim(tail, core * half_rows, half_rows, 0)
    tail_half = tail_half + lax.ppermute(tail_half, axis, far)
    other_half = lax.ppermute(tail_half, axis, near)
    first = jnp.where(core == 0, tail_half, other_half)
    second = jnp.where(core == 0, other_half, tail_half)
    return own_head, jnp.concatenate([first, second], axis=0)


def tp_scatter(partial, rows_mine, axis):
    rank = lax.axis_index(axis)
    far = [(i, i ^ 2) for i in range(4)]
    near = [(i, i ^ 1) for i in range(4)]
    pair_rows = 2 * rows_mine
    chip = rank // 2
    kept = lax.dynamic_slice_in_dim(partial, chip * pair_rows, pair_rows, 0)
    sent = lax.dynamic_slice_in_dim(partial, (1 - chip) * pair_rows, pair_rows, 0)
    kept = kept.astype(jnp.float32) + lax.ppermute(
        sent.astype(jnp.bfloat16), axis, far
    ).astype(jnp.float32)
    core = rank % 2
    mine = lax.dynamic_slice_in_dim(kept, core * rows_mine, rows_mine, 0)
    other = lax.dynamic_slice_in_dim(kept, (1 - core) * rows_mine, rows_mine, 0)
    return mine + lax.ppermute(other.astype(jnp.bfloat16), axis, near).astype(jnp.float32)


def direct_gather(value, axis):
    count = lax.axis_size(axis)
    got = [value] + [None] * (count - 1)
    for shift in range(1, count):
        pairs = [(i, (i + shift) % count) for i in range(count)]
        got[count - shift] = lax.ppermute(value, axis, pairs)
    return jnp.stack(got, axis=0)


def direct_scatter(partial, axis):
    count = lax.axis_size(axis)
    rows = partial.shape[0] // count
    blocks = partial.reshape(count, rows, partial.shape[1])
    total = blocks[0]
    for shift in range(1, count):
        pairs = [(i, (i + shift) % count) for i in range(count)]
        total = total + lax.ppermute(blocks[shift].astype(jnp.bfloat16), axis, pairs).astype(
            jnp.float32
        )
    return total


def butterfly_sum(value, axis):
    count = lax.axis_size(axis)
    stride = 1
    while stride < count:
        pairs = [(i, i ^ stride) for i in range(count)]
        value = value + lax.ppermute(value, axis, pairs)
        stride *= 2
    return value


def shards(ring, tokens, document, place, w_qkv, w_out, grad_out):
    rows_ctx, slice_width = tokens.shape
    ctx_size = lax.axis_size("ctx")
    tp_size = lax.axis_size("tp")
    rows_mine = rows_ctx // tp_size
    tp_rank = lax.axis_index("tp")
    head_dim = HD
    heads = HQ
    heads_width = heads * head_dim
    pair_width = 2 * head_dim
    factor = 1.0 / math.sqrt(head_dim)
    first_row = tp_rank * rows_mine
    stacked = heads * rows_mine
    total_rows = ctx_size * rows_ctx

    grad_part = against(grad_out, w_out).astype(jnp.bfloat16)

    cosine_all, sine_all = angles(place, head_dim)
    cosine_mine = lax.dynamic_slice_in_dim(cosine_all, first_row, rows_mine, 0)
    sine_mine = lax.dynamic_slice_in_dim(sine_all, first_row, rows_mine, 0)
    query_doc = lax.dynamic_slice_in_dim(document, first_row, rows_mine, 0)
    query_place = lax.dynamic_slice_in_dim(place, first_row, rows_mine, 0)

    projected = against(tokens, w_qkv)
    if tp_size == 4 and rows_ctx % (2 * tp_size) == 0:
        query_block, pair_rows = tp_project(projected, rows_mine, heads_width, "tp")
    else:
        qkv = lax.psum(projected, "tp")
        query_block = lax.dynamic_slice_in_dim(qkv[:, :heads_width], first_row, rows_mine, 0)
        pair_rows = qkv[:, heads_width:]
    keys = rotate(pair_rows[:, :head_dim], cosine_all, sine_all).astype(jnp.bfloat16)
    values = pair_rows[:, head_dim:].astype(jnp.bfloat16)

    info = jnp.concatenate(
        [document, place // PIECE, place % PIECE], axis=0
    ).astype(jnp.float32)
    info_rows = -(-info.shape[0] // pair_width)
    info = jnp.pad(info, (0, info_rows * pair_width - info.shape[0]))
    info = info.reshape(info_rows, pair_width).astype(jnp.bfloat16)
    packed = jnp.concatenate([keys, values], axis=1)
    packed = jnp.concatenate([packed, info], axis=0)
    gathered = direct_gather(packed, "ctx")
    if tp_size == 4 and rows_ctx % (2 * tp_size) == 0:
        grad_rows = tp_scatter(grad_part, rows_mine, "tp").astype(jnp.bfloat16)
    else:
        grad_rows = lax.psum_scatter(grad_part, "tp", scatter_dimension=0, tiled=True)
    keys_all = gathered[:, :rows_ctx, :head_dim].reshape(total_rows, head_dim)
    values_all = gathered[:, :rows_ctx, head_dim:].reshape(total_rows, head_dim)
    info_all = gathered[:, rows_ctx:, :].reshape(ctx_size, info_rows * pair_width).astype(
        jnp.float32
    )
    key_doc = info_all[:, :rows_ctx].reshape(total_rows)
    key_place = (
        info_all[:, rows_ctx : 2 * rows_ctx] * PIECE + info_all[:, 2 * rows_ctx : 3 * rows_ctx]
    ).reshape(total_rows)

    allowed = (query_doc.astype(jnp.float32)[:, None] == key_doc[None, :]) & (
        key_place[None, :] <= query_place.astype(jnp.float32)[:, None]
    )
    allowed = jnp.broadcast_to(allowed[None], (heads, rows_mine, total_rows)).reshape(
        stacked, total_rows
    )

    raw_query = query_block.reshape(rows_mine, heads, head_dim)
    rotated = rotate(raw_query, cosine_mine[:, None, :], sine_mine[:, None, :]).astype(jnp.bfloat16)
    queries = jnp.transpose(rotated, (1, 0, 2)).reshape(stacked, head_dim)

    scores = against(queries, keys_all) * factor
    masked = jnp.where(allowed, scores, NEG)
    top = jnp.max(masked, axis=1)
    weights = jnp.where(allowed, jnp.exp(masked - top[:, None]), 0.0)
    total = jnp.sum(weights, axis=1)
    summed = jnp.dot(weights.astype(jnp.bfloat16), values_all, preferred_element_type=jnp.float32)
    attended = (summed / total[:, None]).astype(jnp.bfloat16)
    logsum = top + jnp.log(total)

    rows_attended = jnp.transpose(attended.reshape(heads, rows_mine, head_dim), (1, 0, 2)).reshape(
        rows_mine, heads_width
    )
    piece = lax.all_gather(rows_attended, "tp", axis=0, tiled=True)
    out = jnp.dot(piece, w_out, preferred_element_type=jnp.float32).astype(jnp.bfloat16)
    out_weight_grad = across(piece, grad_out)

    grad_stack = jnp.transpose(grad_rows.reshape(rows_mine, heads, head_dim), (1, 0, 2)).reshape(
        stacked, head_dim
    )
    delta = jnp.sum(grad_stack.astype(jnp.float32) * attended.astype(jnp.float32), axis=1)
    prob = jnp.where(allowed, jnp.exp(scores - logsum[:, None]), 0.0)
    dprob = against(grad_stack, values_all)
    dscore = (prob * (dprob - delta[:, None])).astype(jnp.bfloat16)
    query_sum = jnp.dot(dscore, keys_all, preferred_element_type=jnp.float32)
    key_part = across(dscore, queries) * factor
    value_part = across(prob.astype(jnp.bfloat16), grad_stack)
    pair_all = jnp.concatenate([key_part, value_part], axis=1)
    out_ring = Ring(out_weight_grad, ring, "ctx").advance(len(ring) // 4)
    pair_grad = butterfly_sum(direct_scatter(pair_all, "ctx"), "tp")
    out_ring.state, pair_grad = lax.optimization_barrier((out_ring.state, pair_grad))

    key_raw = rotate(pair_grad[:, :head_dim], cosine_all, -sine_all)
    query_grad = jnp.transpose((query_sum * factor).reshape(heads, rows_mine, head_dim), (1, 0, 2))
    query_raw = rotate(query_grad, cosine_mine[:, None, :], -sine_mine[:, None, :]).reshape(
        rows_mine, heads_width
    )
    query_rows = lax.all_gather(query_raw.astype(jnp.bfloat16), "tp", axis=0, tiled=True)
    d_qkv = jnp.concatenate(
        [query_rows, key_raw.astype(jnp.bfloat16), pair_grad[:, head_dim:].astype(jnp.bfloat16)],
        axis=1,
    )
    grad_x = jnp.dot(d_qkv, w_qkv, preferred_element_type=jnp.float32).astype(jnp.bfloat16)
    joint_weight = across(d_qkv, tokens)
    grad_w_qkv = ring_scatter(joint_weight, ring, "ctx")
    grad_w_out = out_ring.result()
    return (out, grad_x, grad_w_qkv, grad_w_out)


def solution(mesh):
    return jax.shard_map(
        functools.partial(shards, ring_of(mesh)),
        mesh=mesh,
        in_specs=(P("ctx", "tp"), P("ctx"), P("ctx"), P(None, "tp"), P(None, "tp"), P("ctx", "tp")),
        out_specs=(P("ctx", "tp"), P("ctx", "tp"), P("ctx", "tp"), P("ctx", "tp")),
        check_vma=False,
    )
```

```python
import functools
import math

import jax
import jax.numpy as jnp
from jax import lax
from jax.sharding import PartitionSpec as P

HD = 128
HQ = 8


THETA = 500000.0
NEG = -1e30
PIECE = 64


def angles(place, width):
    half = width // 2
    freq = THETA ** (-(jnp.arange(half, dtype=jnp.float32) * 2.0 / width))
    turn = place.astype(jnp.float32)[:, None] * freq[None, :]
    return (jnp.cos(turn), jnp.sin(turn))


def rotate(vector, cosine, sine):
    half = vector.shape[-1] // 2
    first = vector[..., :half]
    second = vector[..., half:]
    return jnp.concatenate(
        [first * cosine - second * sine, second * cosine + first * sine], axis=-1
    )


def against(left, right):
    return lax.dot_general(
        left, right, (((1,), (1,)), ((), ())), preferred_element_type=jnp.float32
    )


def across(left, right):
    return lax.dot_general(
        left, right, (((0,), (0,)), ((), ())), preferred_element_type=jnp.float32
    )


def ring_of(mesh):
    count = mesh.shape["ctx"]
    try:
        grid = mesh.devices.reshape(count, -1)
        coords = [tuple(grid[i, 0].coords) for i in range(count)]
    except Exception:
        return list(range(count))
    varying = [d for d in range(len(coords[0])) if len({c[d] for c in coords}) > 1]
    if len(varying) == 1:
        return sorted(range(count), key=lambda i: coords[i][varying[0]])
    if len(varying) != 2:
        return list(range(count))
    for short, long in (varying, varying[::-1]):
        levels = sorted({c[short] for c in coords})
        if len(levels) == 2:
            there = sorted(
                (i for i in range(count) if coords[i][short] == levels[0]),
                key=lambda i: coords[i][long],
            )
            back = sorted(
                (i for i in range(count) if coords[i][short] == levels[1]),
                key=lambda i: -coords[i][long],
            )
            return there + back
    return list(range(count))


def ring_scatter(partial, ring, axis):
    count = len(ring)
    where = [0] * count
    for spot, member in enumerate(ring):
        where[member] = spot
    spot = jnp.asarray(where, jnp.int32)[lax.axis_index(axis)]
    order = jnp.asarray(ring, jnp.int32)
    rows = partial.shape[0] // count
    half = partial.shape[1] // 2
    blocks = partial.reshape(count, rows, partial.shape[1])
    left = blocks[:, :, :half]
    right = blocks[:, :, half:]

    def block(side, offset):
        return lax.dynamic_index_in_dim(side, order[(spot + offset) % count], 0, keepdims=False)

    forward = [(ring[p], ring[(p + 1) % count]) for p in range(count)]
    backward = [(ring[p], ring[(p - 1) % count]) for p in range(count)]
    send_left = block(left, count - 1)
    send_right = block(right, 1)
    for step in range(count - 1):
        got_left = lax.ppermute(send_left.astype(jnp.bfloat16), axis, forward)
        got_right = lax.ppermute(send_right.astype(jnp.bfloat16), axis, backward)
        send_left = got_left.astype(jnp.float32) + block(left, 2 * count - step - 2)
        send_right = got_right.astype(jnp.float32) + block(right, step + 2)
    return jnp.concatenate([send_left, send_right], axis=1)


def ring_spot(ring, axis):
    where = [0] * len(ring)
    for spot, member in enumerate(ring):
        where[member] = spot
    return jnp.asarray(where, jnp.int32)[lax.axis_index(axis)]


def ring_gather(value, ring, axis):
    count = len(ring)
    forward = [(ring[p], ring[(p + 1) % count]) for p in range(count)]
    backward = [(ring[p], ring[(p - 1) % count]) for p in range(count)]
    ahead = count // 2
    behind = count - 1 - ahead
    got = [value] + [None] * (count - 1)
    from_left = value
    from_right = value
    for step in range(max(ahead, behind)):
        if step < ahead:
            from_left = lax.ppermute(from_left, axis, forward)
            got[count - step - 1] = from_left
        if step < behind:
            from_right = lax.ppermute(from_right, axis, backward)
            got[step + 1] = from_right
    return jnp.stack(got, axis=0)


def ring_scatter_relative(partial, ring, axis):
    count = len(ring)
    rows = partial.shape[0] // count
    half = partial.shape[1] // 2
    blocks = partial.reshape(count, rows, partial.shape[1])
    left = blocks[:, :, :half]
    right = blocks[:, :, half:]
    forward = [(ring[p], ring[(p + 1) % count]) for p in range(count)]
    backward = [(ring[p], ring[(p - 1) % count]) for p in range(count)]
    send_left = left[count - 1]
    send_right = right[1 % count]
    for step in range(count - 1):
        got_left = lax.ppermute(send_left.astype(jnp.bfloat16), axis, forward)
        got_right = lax.ppermute(send_right.astype(jnp.bfloat16), axis, backward)
        send_left = got_left.astype(jnp.float32) + left[(2 * count - step - 2) % count]
        send_right = got_right.astype(jnp.float32) + right[(step + 2) % count]
    return jnp.concatenate([send_left, send_right], axis=1)


class Ring:
    def __init__(self, partial, ring, axis):
        count = len(ring)
        self.count = count
        self.axis = axis
        self.spot = ring_spot(ring, axis)
        self.order = jnp.asarray(ring, jnp.int32)
        rows = partial.shape[0] // count
        half = partial.shape[1] // 2
        blocks = partial.reshape(count, rows, partial.shape[1])
        self.left = blocks[:, :, :half]
        self.right = blocks[:, :, half:]
        self.forward = [(ring[p], ring[(p + 1) % count]) for p in range(count)]
        self.backward = [(ring[p], ring[(p - 1) % count]) for p in range(count)]
        self.state = (self.block(self.left, count - 1), self.block(self.right, 1))
        self.done = 0

    def block(self, side, offset):
        index = self.order[(self.spot + offset) % self.count]
        return lax.dynamic_index_in_dim(side, index, 0, keepdims=False)

    def advance(self, upto):
        count = self.count
        send_left, send_right = self.state
        for step in range(self.done, min(upto, count - 1)):
            got_left = lax.ppermute(send_left.astype(jnp.bfloat16), self.axis, self.forward)
            got_right = lax.ppermute(send_right.astype(jnp.bfloat16), self.axis, self.backward)
            send_left = got_left.astype(jnp.float32) + self.block(self.left, 2 * count - step - 2)
            send_right = got_right.astype(jnp.float32) + self.block(self.right, step + 2)
            self.done = step + 1
        self.state = (send_left, send_right)
        return self

    def result(self):
        self.advance(self.count - 1)
        return jnp.concatenate(list(self.state), axis=1)


def tp_project(partial, rows_mine, split, axis):
    rank = lax.axis_index(axis)
    core = rank % 2
    near = [(i, i ^ 1) for i in range(4)]
    far = [(i, i ^ 2) for i in range(4)]
    chip = partial + lax.ppermute(partial, axis, near)
    head = chip[:, :split]
    tail = chip[:, split:]
    half_rows = tail.shape[0] // 2
    mine = lax.dynamic_slice_in_dim(head, rank * rows_mine, rows_mine, 0)
    theirs = lax.dynamic_slice_in_dim(head, (rank ^ 2) * rows_mine, rows_mine, 0)
    own_head = mine + lax.ppermute(theirs, axis, far)
    tail_half = lax.dynamic_slice_in_dim(tail, core * half_rows, half_rows, 0)
    tail_half = tail_half + lax.ppermute(tail_half, axis, far)
    other_half = lax.ppermute(tail_half, axis, near)
    first = jnp.where(core == 0, tail_half, other_half)
    second = jnp.where(core == 0, other_half, tail_half)
    return own_head, jnp.concatenate([first, second], axis=0)


def tp_scatter(partial, rows_mine, axis):
    rank = lax.axis_index(axis)
    far = [(i, i ^ 2) for i in range(4)]
    near = [(i, i ^ 1) for i in range(4)]
    pair_rows = 2 * rows_mine
    chip = rank // 2
    kept = lax.dynamic_slice_in_dim(partial, chip * pair_rows, pair_rows, 0)
    sent = lax.dynamic_slice_in_dim(partial, (1 - chip) * pair_rows, pair_rows, 0)
    kept = kept.astype(jnp.float32) + lax.ppermute(
        sent.astype(jnp.bfloat16), axis, far
    ).astype(jnp.float32)
    core = rank % 2
    mine = lax.dynamic_slice_in_dim(kept, core * rows_mine, rows_mine, 0)
    other = lax.dynamic_slice_in_dim(kept, (1 - core) * rows_mine, rows_mine, 0)
    return mine + lax.ppermute(other.astype(jnp.bfloat16), axis, near).astype(jnp.float32)


def direct_gather(value, axis):
    count = lax.axis_size(axis)
    got = [value] + [None] * (count - 1)
    for shift in range(1, count):
        pairs = [(i, (i + shift) % count) for i in range(count)]
        got[count - shift] = lax.ppermute(value, axis, pairs)
    return jnp.stack(got, axis=0)


def direct_scatter(partial, axis):
    count = lax.axis_size(axis)
    rows = partial.shape[0] // count
    blocks = partial.reshape(count, rows, partial.shape[1])
    total = blocks[0]
    for shift in range(1, count):
        pairs = [(i, (i + shift) % count) for i in range(count)]
        total = total + lax.ppermute(blocks[shift].astype(jnp.bfloat16), axis, pairs).astype(
            jnp.float32
        )
    return total


def butterfly_sum(value, axis):
    count = lax.axis_size(axis)
    stride = 1
    while stride < count:
        pairs = [(i, i ^ stride) for i in range(count)]
        value = value + lax.ppermute(value, axis, pairs)
        stride *= 2
    return value


def shards(ring, tokens, document, place, w_qkv, w_out, grad_out):
    rows_ctx, slice_width = tokens.shape
    ctx_size = lax.axis_size("ctx")
    tp_size = lax.axis_size("tp")
    rows_mine = rows_ctx // tp_size
    tp_rank = lax.axis_index("tp")
    head_dim = HD
    heads = HQ
    heads_width = heads * head_dim
    pair_width = 2 * head_dim
    factor = 1.0 / math.sqrt(head_dim)
    first_row = tp_rank * rows_mine
    stacked = heads * rows_mine
    total_rows = ctx_size * rows_ctx

    grad_part = against(grad_out, w_out).astype(jnp.bfloat16)

    cosine_all, sine_all = angles(place, head_dim)
    cosine_mine = lax.dynamic_slice_in_dim(cosine_all, first_row, rows_mine, 0)
    sine_mine = lax.dynamic_slice_in_dim(sine_all, first_row, rows_mine, 0)
    query_doc = lax.dynamic_slice_in_dim(document, first_row, rows_mine, 0)
    query_place = lax.dynamic_slice_in_dim(place, first_row, rows_mine, 0)

    projected = against(tokens, w_qkv)
    if tp_size == 4 and rows_ctx % (2 * tp_size) == 0:
        query_block, pair_rows = tp_project(projected, rows_mine, heads_width, "tp")
    else:
        qkv = lax.psum(projected, "tp")
        query_block = lax.dynamic_slice_in_dim(qkv[:, :heads_width], first_row, rows_mine, 0)
        pair_rows = qkv[:, heads_width:]
    keys = rotate(pair_rows[:, :head_dim], cosine_all, sine_all).astype(jnp.bfloat16)
    values = pair_rows[:, head_dim:].astype(jnp.bfloat16)

    info = jnp.concatenate(
        [document, place // PIECE, place % PIECE], axis=0
    ).astype(jnp.float32)
    info_rows = -(-info.shape[0] // pair_width)
    info = jnp.pad(info, (0, info_rows * pair_width - info.shape[0]))
    info = info.reshape(info_rows, pair_width).astype(jnp.bfloat16)
    packed = jnp.concatenate([keys, values], axis=1)
    packed = jnp.concatenate([packed, info], axis=0)
    gathered = ring_gather(packed, ring, "ctx")
    if tp_size == 4 and rows_ctx % (2 * tp_size) == 0:
        grad_rows = tp_scatter(grad_part, rows_mine, "tp").astype(jnp.bfloat16)
    else:
        grad_rows = lax.psum_scatter(grad_part, "tp", scatter_dimension=0, tiled=True)
    keys_all = gathered[:, :rows_ctx, :head_dim].reshape(total_rows, head_dim)
    values_all = gathered[:, :rows_ctx, head_dim:].reshape(total_rows, head_dim)
    info_all = gathered[:, rows_ctx:, :].reshape(ctx_size, info_rows * pair_width).astype(
        jnp.float32
    )
    key_doc = info_all[:, :rows_ctx].reshape(total_rows)
    key_place = (
        info_all[:, rows_ctx : 2 * rows_ctx] * PIECE + info_all[:, 2 * rows_ctx : 3 * rows_ctx]
    ).reshape(total_rows)

    allowed = (query_doc.astype(jnp.float32)[:, None] == key_doc[None, :]) & (
        key_place[None, :] <= query_place.astype(jnp.float32)[:, None]
    )
    allowed = jnp.broadcast_to(allowed[None], (heads, rows_mine, total_rows)).reshape(
        stacked, total_rows
    )

    raw_query = query_block.reshape(rows_mine, heads, head_dim)
    rotated = rotate(raw_query, cosine_mine[:, None, :], sine_mine[:, None, :]).astype(jnp.bfloat16)
    queries = jnp.transpose(rotated, (1, 0, 2)).reshape(stacked, head_dim)

    scores = against(queries, keys_all) * factor
    masked = jnp.where(allowed, scores, NEG)
    top = jnp.max(masked, axis=1)
    weights = jnp.where(allowed, jnp.exp(masked - top[:, None]), 0.0)
    total = jnp.sum(weights, axis=1)
    summed = jnp.dot(weights.astype(jnp.bfloat16), values_all, preferred_element_type=jnp.float32)
    attended = (summed / total[:, None]).astype(jnp.bfloat16)
    logsum = top + jnp.log(total)

    rows_attended = jnp.transpose(attended.reshape(heads, rows_mine, head_dim), (1, 0, 2)).reshape(
        rows_mine, heads_width
    )
    piece = lax.all_gather(rows_attended, "tp", axis=0, tiled=True)
    out = jnp.dot(piece, w_out, preferred_element_type=jnp.float32).astype(jnp.bfloat16)
    out_weight_grad = across(piece, grad_out)

    grad_stack = jnp.transpose(grad_rows.reshape(rows_mine, heads, head_dim), (1, 0, 2)).reshape(
        stacked, head_dim
    )
    delta = jnp.sum(grad_stack.astype(jnp.float32) * attended.astype(jnp.float32), axis=1)
    prob = jnp.where(allowed, jnp.exp(scores - logsum[:, None]), 0.0)
    dprob = against(grad_stack, values_all)
    dscore = (prob * (dprob - delta[:, None])).astype(jnp.bfloat16)
    query_sum = jnp.dot(dscore, keys_all, preferred_element_type=jnp.float32)
    key_part = across(dscore, queries) * factor
    value_part = across(prob.astype(jnp.bfloat16), grad_stack)
    pair_all = jnp.concatenate([key_part, value_part], axis=1)
    out_ring = Ring(out_weight_grad, ring, "ctx").advance(len(ring) // 4)
    pair_grad = butterfly_sum(ring_scatter_relative(pair_all, ring, "ctx"), "tp")
    out_ring.state, pair_grad = lax.optimization_barrier((out_ring.state, pair_grad))

    key_raw = rotate(pair_grad[:, :head_dim], cosine_all, -sine_all)
    query_grad = jnp.transpose((query_sum * factor).reshape(heads, rows_mine, head_dim), (1, 0, 2))
    query_raw = rotate(query_grad, cosine_mine[:, None, :], -sine_mine[:, None, :]).reshape(
        rows_mine, heads_width
    )
    query_rows = lax.all_gather(query_raw.astype(jnp.bfloat16), "tp", axis=0, tiled=True)
    d_qkv = jnp.concatenate(
        [query_rows, key_raw.astype(jnp.bfloat16), pair_grad[:, head_dim:].astype(jnp.bfloat16)],
        axis=1,
    )
    grad_x = jnp.dot(d_qkv, w_qkv, preferred_element_type=jnp.float32).astype(jnp.bfloat16)
    joint_weight = across(d_qkv, tokens)
    out_ring.advance(len(ring) - 1)
    out_ring.state, joint_weight = lax.optimization_barrier((out_ring.state, joint_weight))
    grad_w_qkv = ring_scatter(joint_weight, ring, "ctx")
    grad_w_out = out_ring.result()
    return (out, grad_x, grad_w_qkv, grad_w_out)


def solution(mesh):
    return jax.shard_map(
        functools.partial(shards, ring_of(mesh)),
        mesh=mesh,
        in_specs=(P("ctx", "tp"), P("ctx"), P("ctx"), P(None, "tp"), P(None, "tp"), P("ctx", "tp")),
        out_specs=(P("ctx", "tp"), P("ctx", "tp"), P("ctx", "tp"), P("ctx", "tp")),
        check_vma=False,
    )
```

```python
import functools
import math

import jax
import jax.numpy as jnp
from jax import lax
from jax.sharding import PartitionSpec as P

HD = 128
HQ = 8


THETA = 500000.0
NEG = -1e30
PIECE = 64


def angles(place, width):
    half = width // 2
    freq = THETA ** (-(jnp.arange(half, dtype=jnp.float32) * 2.0 / width))
    turn = place.astype(jnp.float32)[:, None] * freq[None, :]
    return (jnp.cos(turn), jnp.sin(turn))


def rotate(vector, cosine, sine):
    half = vector.shape[-1] // 2
    first = vector[..., :half]
    second = vector[..., half:]
    return jnp.concatenate(
        [first * cosine - second * sine, second * cosine + first * sine], axis=-1
    )


def against(left, right):
    return lax.dot_general(
        left, right, (((1,), (1,)), ((), ())), preferred_element_type=jnp.float32
    )


def across(left, right):
    return lax.dot_general(
        left, right, (((0,), (0,)), ((), ())), preferred_element_type=jnp.float32
    )


def ring_of(mesh):
    count = mesh.shape["ctx"]
    try:
        grid = mesh.devices.reshape(count, -1)
        coords = [tuple(grid[i, 0].coords) for i in range(count)]
    except Exception:
        return list(range(count))
    varying = [d for d in range(len(coords[0])) if len({c[d] for c in coords}) > 1]
    if len(varying) == 1:
        return sorted(range(count), key=lambda i: coords[i][varying[0]])
    if len(varying) != 2:
        return list(range(count))
    for short, long in (varying, varying[::-1]):
        levels = sorted({c[short] for c in coords})
        if len(levels) == 2:
            there = sorted(
                (i for i in range(count) if coords[i][short] == levels[0]),
                key=lambda i: coords[i][long],
            )
            back = sorted(
                (i for i in range(count) if coords[i][short] == levels[1]),
                key=lambda i: -coords[i][long],
            )
            return there + back
    return list(range(count))


def ring_scatter(partial, ring, axis):
    count = len(ring)
    where = [0] * count
    for spot, member in enumerate(ring):
        where[member] = spot
    spot = jnp.asarray(where, jnp.int32)[lax.axis_index(axis)]
    order = jnp.asarray(ring, jnp.int32)
    rows = partial.shape[0] // count
    half = partial.shape[1] // 2
    blocks = partial.reshape(count, rows, partial.shape[1])
    left = blocks[:, :, :half]
    right = blocks[:, :, half:]

    def block(side, offset):
        return lax.dynamic_index_in_dim(side, order[(spot + offset) % count], 0, keepdims=False)

    forward = [(ring[p], ring[(p + 1) % count]) for p in range(count)]
    backward = [(ring[p], ring[(p - 1) % count]) for p in range(count)]
    send_left = block(left, count - 1)
    send_right = block(right, 1)
    for step in range(count - 1):
        got_left = lax.ppermute(send_left.astype(jnp.bfloat16), axis, forward)
        got_right = lax.ppermute(send_right.astype(jnp.bfloat16), axis, backward)
        send_left = got_left.astype(jnp.float32) + block(left, 2 * count - step - 2)
        send_right = got_right.astype(jnp.float32) + block(right, step + 2)
    return jnp.concatenate([send_left, send_right], axis=1)


def ring_spot(ring, axis):
    where = [0] * len(ring)
    for spot, member in enumerate(ring):
        where[member] = spot
    return jnp.asarray(where, jnp.int32)[lax.axis_index(axis)]


def ring_gather(value, ring, axis):
    count = len(ring)
    forward = [(ring[p], ring[(p + 1) % count]) for p in range(count)]
    backward = [(ring[p], ring[(p - 1) % count]) for p in range(count)]
    ahead = count // 2
    behind = count - 1 - ahead
    got = [value] + [None] * (count - 1)
    from_left = value
    from_right = value
    for step in range(max(ahead, behind)):
        if step < ahead:
            from_left = lax.ppermute(from_left, axis, forward)
            got[count - step - 1] = from_left
        if step < behind:
            from_right = lax.ppermute(from_right, axis, backward)
            got[step + 1] = from_right
    return jnp.stack(got, axis=0)


def ring_scatter_relative(partial, ring, axis):
    count = len(ring)
    rows = partial.shape[0] // count
    half = partial.shape[1] // 2
    blocks = partial.reshape(count, rows, partial.shape[1])
    left = blocks[:, :, :half]
    right = blocks[:, :, half:]
    forward = [(ring[p], ring[(p + 1) % count]) for p in range(count)]
    backward = [(ring[p], ring[(p - 1) % count]) for p in range(count)]
    send_left = left[count - 1]
    send_right = right[1 % count]
    for step in range(count - 1):
        got_left = lax.ppermute(send_left.astype(jnp.bfloat16), axis, forward)
        got_right = lax.ppermute(send_right.astype(jnp.bfloat16), axis, backward)
        send_left = got_left.astype(jnp.float32) + left[(2 * count - step - 2) % count]
        send_right = got_right.astype(jnp.float32) + right[(step + 2) % count]
    return jnp.concatenate([send_left, send_right], axis=1)


class Ring:
    def __init__(self, partial, ring, axis):
        count = len(ring)
        self.count = count
        self.axis = axis
        self.spot = ring_spot(ring, axis)
        self.order = jnp.asarray(ring, jnp.int32)
        rows = partial.shape[0] // count
        half = partial.shape[1] // 2
        blocks = partial.reshape(count, rows, partial.shape[1])
        self.left = blocks[:, :, :half]
        self.right = blocks[:, :, half:]
        self.forward = [(ring[p], ring[(p + 1) % count]) for p in range(count)]
        self.backward = [(ring[p], ring[(p - 1) % count]) for p in range(count)]
        self.state = (self.block(self.left, count - 1), self.block(self.right, 1))
        self.done = 0

    def block(self, side, offset):
        index = self.order[(self.spot + offset) % self.count]
        return lax.dynamic_index_in_dim(side, index, 0, keepdims=False)

    def advance(self, upto):
        count = self.count
        send_left, send_right = self.state
        for step in range(self.done, min(upto, count - 1)):
            got_left = lax.ppermute(send_left.astype(jnp.bfloat16), self.axis, self.forward)
            got_right = lax.ppermute(send_right.astype(jnp.bfloat16), self.axis, self.backward)
            send_left = got_left.astype(jnp.float32) + self.block(self.left, 2 * count - step - 2)
            send_right = got_right.astype(jnp.float32) + self.block(self.right, step + 2)
            self.done = step + 1
        self.state = (send_left, send_right)
        return self

    def result(self):
        self.advance(self.count - 1)
        return jnp.concatenate(list(self.state), axis=1)


def tp_project(partial, rows_mine, split, axis):
    rank = lax.axis_index(axis)
    core = rank % 2
    near = [(i, i ^ 1) for i in range(4)]
    far = [(i, i ^ 2) for i in range(4)]
    chip = partial + lax.ppermute(partial, axis, near)
    head = chip[:, :split]
    tail = chip[:, split:]
    half_rows = tail.shape[0] // 2
    mine = lax.dynamic_slice_in_dim(head, rank * rows_mine, rows_mine, 0)
    theirs = lax.dynamic_slice_in_dim(head, (rank ^ 2) * rows_mine, rows_mine, 0)
    own_head = mine + lax.ppermute(theirs, axis, far)
    tail_half = lax.dynamic_slice_in_dim(tail, core * half_rows, half_rows, 0)
    tail_half = tail_half + lax.ppermute(tail_half, axis, far)
    other_half = lax.ppermute(tail_half, axis, near)
    first = jnp.where(core == 0, tail_half, other_half)
    second = jnp.where(core == 0, other_half, tail_half)
    return own_head, jnp.concatenate([first, second], axis=0)


def tp_scatter(partial, rows_mine, axis):
    rank = lax.axis_index(axis)
    far = [(i, i ^ 2) for i in range(4)]
    near = [(i, i ^ 1) for i in range(4)]
    pair_rows = 2 * rows_mine
    chip = rank // 2
    kept = lax.dynamic_slice_in_dim(partial, chip * pair_rows, pair_rows, 0)
    sent = lax.dynamic_slice_in_dim(partial, (1 - chip) * pair_rows, pair_rows, 0)
    kept = kept.astype(jnp.float32) + lax.ppermute(
        sent.astype(jnp.bfloat16), axis, far
    ).astype(jnp.float32)
    core = rank % 2
    mine = lax.dynamic_slice_in_dim(kept, core * rows_mine, rows_mine, 0)
    other = lax.dynamic_slice_in_dim(kept, (1 - core) * rows_mine, rows_mine, 0)
    return mine + lax.ppermute(other.astype(jnp.bfloat16), axis, near).astype(jnp.float32)


def direct_gather(value, axis):
    count = lax.axis_size(axis)
    got = [value] + [None] * (count - 1)
    for shift in range(1, count):
        pairs = [(i, (i + shift) % count) for i in range(count)]
        got[count - shift] = lax.ppermute(value, axis, pairs)
    return jnp.stack(got, axis=0)


def direct_scatter(partial, axis):
    count = lax.axis_size(axis)
    rows = partial.shape[0] // count
    blocks = partial.reshape(count, rows, partial.shape[1])
    total = blocks[0]
    for shift in range(1, count):
        pairs = [(i, (i + shift) % count) for i in range(count)]
        total = total + lax.ppermute(blocks[shift].astype(jnp.bfloat16), axis, pairs).astype(
            jnp.float32
        )
    return total


def butterfly_sum(value, axis):
    count = lax.axis_size(axis)
    stride = 1
    while stride < count:
        pairs = [(i, i ^ stride) for i in range(count)]
        value = value + lax.ppermute(value, axis, pairs)
        stride *= 2
    return value


def shards(ring, tokens, document, place, w_qkv, w_out, grad_out):
    rows_ctx, slice_width = tokens.shape
    ctx_size = lax.axis_size("ctx")
    tp_size = lax.axis_size("tp")
    rows_mine = rows_ctx // tp_size
    tp_rank = lax.axis_index("tp")
    head_dim = HD
    heads = HQ
    heads_width = heads * head_dim
    pair_width = 2 * head_dim
    factor = 1.0 / math.sqrt(head_dim)
    first_row = tp_rank * rows_mine
    stacked = heads * rows_mine
    total_rows = ctx_size * rows_ctx

    grad_part = against(grad_out, w_out).astype(jnp.bfloat16)

    cosine_all, sine_all = angles(place, head_dim)
    cosine_mine = lax.dynamic_slice_in_dim(cosine_all, first_row, rows_mine, 0)
    sine_mine = lax.dynamic_slice_in_dim(sine_all, first_row, rows_mine, 0)
    query_doc = lax.dynamic_slice_in_dim(document, first_row, rows_mine, 0)
    query_place = lax.dynamic_slice_in_dim(place, first_row, rows_mine, 0)

    projected = against(tokens, w_qkv)
    if tp_size == 4 and rows_ctx % (2 * tp_size) == 0:
        query_block, pair_rows = tp_project(projected, rows_mine, heads_width, "tp")
    else:
        qkv = lax.psum(projected, "tp")
        query_block = lax.dynamic_slice_in_dim(qkv[:, :heads_width], first_row, rows_mine, 0)
        pair_rows = qkv[:, heads_width:]
    keys = rotate(pair_rows[:, :head_dim], cosine_all, sine_all).astype(jnp.bfloat16)
    values = pair_rows[:, head_dim:].astype(jnp.bfloat16)

    info = jnp.concatenate(
        [document, place // PIECE, place % PIECE], axis=0
    ).astype(jnp.float32)
    info_rows = -(-info.shape[0] // pair_width)
    info = jnp.pad(info, (0, info_rows * pair_width - info.shape[0]))
    info = info.reshape(info_rows, pair_width).astype(jnp.bfloat16)
    packed = jnp.concatenate([keys, values], axis=1)
    packed = jnp.concatenate([packed, info], axis=0)
    gathered = direct_gather(packed, "ctx")
    if tp_size == 4 and rows_ctx % (2 * tp_size) == 0:
        grad_rows = tp_scatter(grad_part, rows_mine, "tp").astype(jnp.bfloat16)
    else:
        grad_rows = lax.psum_scatter(grad_part, "tp", scatter_dimension=0, tiled=True)
    keys_all = gathered[:, :rows_ctx, :head_dim].reshape(total_rows, head_dim)
    values_all = gathered[:, :rows_ctx, head_dim:].reshape(total_rows, head_dim)
    info_all = gathered[:, rows_ctx:, :].reshape(ctx_size, info_rows * pair_width).astype(
        jnp.float32
    )
    key_doc = info_all[:, :rows_ctx].reshape(total_rows)
    key_place = (
        info_all[:, rows_ctx : 2 * rows_ctx] * PIECE + info_all[:, 2 * rows_ctx : 3 * rows_ctx]
    ).reshape(total_rows)

    allowed = (query_doc.astype(jnp.float32)[:, None] == key_doc[None, :]) & (
        key_place[None, :] <= query_place.astype(jnp.float32)[:, None]
    )
    allowed = jnp.broadcast_to(allowed[None], (heads, rows_mine, total_rows)).reshape(
        stacked, total_rows
    )

    raw_query = query_block.reshape(rows_mine, heads, head_dim)
    rotated = rotate(raw_query, cosine_mine[:, None, :], sine_mine[:, None, :]).astype(jnp.bfloat16)
    queries = jnp.transpose(rotated, (1, 0, 2)).reshape(stacked, head_dim)

    scores = against(queries, keys_all) * factor
    masked = jnp.where(allowed, scores, NEG)
    top = jnp.max(masked, axis=1)
    weights = jnp.where(allowed, jnp.exp(masked - top[:, None]), 0.0)
    total = jnp.sum(weights, axis=1)
    summed = jnp.dot(weights.astype(jnp.bfloat16), values_all, preferred_element_type=jnp.float32)
    attended = (summed / total[:, None]).astype(jnp.bfloat16)
    logsum = top + jnp.log(total)

    rows_attended = jnp.transpose(attended.reshape(heads, rows_mine, head_dim), (1, 0, 2)).reshape(
        rows_mine, heads_width
    )
    piece = lax.all_gather(rows_attended, "tp", axis=0, tiled=True)
    out = jnp.dot(piece, w_out, preferred_element_type=jnp.float32).astype(jnp.bfloat16)
    out_weight_grad = across(piece, grad_out)

    out, grad_rows = lax.optimization_barrier((out, grad_rows))
    grad_stack = jnp.transpose(grad_rows.reshape(rows_mine, heads, head_dim), (1, 0, 2)).reshape(
        stacked, head_dim
    )
    delta = jnp.sum(grad_stack.astype(jnp.float32) * attended.astype(jnp.float32), axis=1)
    prob = jnp.where(allowed, jnp.exp(scores - logsum[:, None]), 0.0)
    dprob = against(grad_stack, values_all)
    dscore = (prob * (dprob - delta[:, None])).astype(jnp.bfloat16)
    query_sum = jnp.dot(dscore, keys_all, preferred_element_type=jnp.float32)
    key_part = across(dscore, queries) * factor
    value_part = across(prob.astype(jnp.bfloat16), grad_stack)
    pair_all = jnp.concatenate([key_part, value_part], axis=1)
    out_ring = Ring(out_weight_grad, ring, "ctx").advance(len(ring) // 4)
    pair_grad = butterfly_sum(direct_scatter(pair_all, "ctx"), "tp")
    out_ring.state, pair_grad = lax.optimization_barrier((out_ring.state, pair_grad))

    key_raw = rotate(pair_grad[:, :head_dim], cosine_all, -sine_all)
    query_grad = jnp.transpose((query_sum * factor).reshape(heads, rows_mine, head_dim), (1, 0, 2))
    query_raw = rotate(query_grad, cosine_mine[:, None, :], -sine_mine[:, None, :]).reshape(
        rows_mine, heads_width
    )
    query_rows = lax.all_gather(query_raw.astype(jnp.bfloat16), "tp", axis=0, tiled=True)
    d_qkv = jnp.concatenate(
        [query_rows, key_raw.astype(jnp.bfloat16), pair_grad[:, head_dim:].astype(jnp.bfloat16)],
        axis=1,
    )
    grad_x = jnp.dot(d_qkv, w_qkv, preferred_element_type=jnp.float32).astype(jnp.bfloat16)
    joint_weight = across(d_qkv, tokens)
    out_ring.advance(len(ring) - 1)
    out_ring.state, joint_weight = lax.optimization_barrier((out_ring.state, joint_weight))
    grad_w_qkv = ring_scatter(joint_weight, ring, "ctx")
    grad_w_out = out_ring.result()
    return (out, grad_x, grad_w_qkv, grad_w_out)


def solution(mesh):
    return jax.shard_map(
        functools.partial(shards, ring_of(mesh)),
        mesh=mesh,
        in_specs=(P("ctx", "tp"), P("ctx"), P("ctx"), P(None, "tp"), P(None, "tp"), P("ctx", "tp")),
        out_specs=(P("ctx", "tp"), P("ctx", "tp"), P("ctx", "tp"), P("ctx", "tp")),
        check_vma=False,
    )
```

```python
import functools
import math

import jax
import jax.numpy as jnp
from jax import lax
from jax.sharding import PartitionSpec as P

HD = 128
HQ = 8


THETA = 500000.0
NEG = -1e30
PIECE = 64


def angles(place, width):
    half = width // 2
    freq = THETA ** (-(jnp.arange(half, dtype=jnp.float32) * 2.0 / width))
    turn = place.astype(jnp.float32)[:, None] * freq[None, :]
    return (jnp.cos(turn), jnp.sin(turn))


def rotate(vector, cosine, sine):
    half = vector.shape[-1] // 2
    first = vector[..., :half]
    second = vector[..., half:]
    return jnp.concatenate(
        [first * cosine - second * sine, second * cosine + first * sine], axis=-1
    )


def against(left, right):
    return lax.dot_general(
        left, right, (((1,), (1,)), ((), ())), preferred_element_type=jnp.float32
    )


def across(left, right):
    return lax.dot_general(
        left, right, (((0,), (0,)), ((), ())), preferred_element_type=jnp.float32
    )


def ring_of(mesh):
    count = mesh.shape["ctx"]
    try:
        grid = mesh.devices.reshape(count, -1)
        coords = [tuple(grid[i, 0].coords) for i in range(count)]
    except Exception:
        return list(range(count))
    varying = [d for d in range(len(coords[0])) if len({c[d] for c in coords}) > 1]
    if len(varying) == 1:
        return sorted(range(count), key=lambda i: coords[i][varying[0]])
    if len(varying) != 2:
        return list(range(count))
    for short, long in (varying, varying[::-1]):
        levels = sorted({c[short] for c in coords})
        if len(levels) == 2:
            there = sorted(
                (i for i in range(count) if coords[i][short] == levels[0]),
                key=lambda i: coords[i][long],
            )
            back = sorted(
                (i for i in range(count) if coords[i][short] == levels[1]),
                key=lambda i: -coords[i][long],
            )
            return there + back
    return list(range(count))


def ring_scatter(partial, ring, axis):
    count = len(ring)
    where = [0] * count
    for spot, member in enumerate(ring):
        where[member] = spot
    spot = jnp.asarray(where, jnp.int32)[lax.axis_index(axis)]
    order = jnp.asarray(ring, jnp.int32)
    rows = partial.shape[0] // count
    half = partial.shape[1] // 2
    blocks = partial.reshape(count, rows, partial.shape[1])
    left = blocks[:, :, :half]
    right = blocks[:, :, half:]

    def block(side, offset):
        return lax.dynamic_index_in_dim(side, order[(spot + offset) % count], 0, keepdims=False)

    forward = [(ring[p], ring[(p + 1) % count]) for p in range(count)]
    backward = [(ring[p], ring[(p - 1) % count]) for p in range(count)]
    send_left = block(left, count - 1)
    send_right = block(right, 1)
    for step in range(count - 1):
        got_left = lax.ppermute(send_left.astype(jnp.bfloat16), axis, forward)
        got_right = lax.ppermute(send_right.astype(jnp.bfloat16), axis, backward)
        send_left = got_left.astype(jnp.float32) + block(left, 2 * count - step - 2)
        send_right = got_right.astype(jnp.float32) + block(right, step + 2)
    return jnp.concatenate([send_left, send_right], axis=1)


def ring_spot(ring, axis):
    where = [0] * len(ring)
    for spot, member in enumerate(ring):
        where[member] = spot
    return jnp.asarray(where, jnp.int32)[lax.axis_index(axis)]


def ring_gather(value, ring, axis):
    count = len(ring)
    forward = [(ring[p], ring[(p + 1) % count]) for p in range(count)]
    backward = [(ring[p], ring[(p - 1) % count]) for p in range(count)]
    ahead = count // 2
    behind = count - 1 - ahead
    got = [value] + [None] * (count - 1)
    from_left = value
    from_right = value
    for step in range(max(ahead, behind)):
        if step < ahead:
            from_left = lax.ppermute(from_left, axis, forward)
            got[count - step - 1] = from_left
        if step < behind:
            from_right = lax.ppermute(from_right, axis, backward)
            got[step + 1] = from_right
    return jnp.stack(got, axis=0)


def ring_scatter_relative(partial, ring, axis):
    count = len(ring)
    rows = partial.shape[0] // count
    half = partial.shape[1] // 2
    blocks = partial.reshape(count, rows, partial.shape[1])
    left = blocks[:, :, :half]
    right = blocks[:, :, half:]
    forward = [(ring[p], ring[(p + 1) % count]) for p in range(count)]
    backward = [(ring[p], ring[(p - 1) % count]) for p in range(count)]
    send_left = left[count - 1]
    send_right = right[1 % count]
    for step in range(count - 1):
        got_left = lax.ppermute(send_left.astype(jnp.bfloat16), axis, forward)
        got_right = lax.ppermute(send_right.astype(jnp.bfloat16), axis, backward)
        send_left = got_left.astype(jnp.float32) + left[(2 * count - step - 2) % count]
        send_right = got_right.astype(jnp.float32) + right[(step + 2) % count]
    return jnp.concatenate([send_left, send_right], axis=1)


class Ring:
    def __init__(self, partial, ring, axis):
        count = len(ring)
        self.count = count
        self.axis = axis
        self.spot = ring_spot(ring, axis)
        self.order = jnp.asarray(ring, jnp.int32)
        rows = partial.shape[0] // count
        half = partial.shape[1] // 2
        blocks = partial.reshape(count, rows, partial.shape[1])
        self.left = blocks[:, :, :half]
        self.right = blocks[:, :, half:]
        self.forward = [(ring[p], ring[(p + 1) % count]) for p in range(count)]
        self.backward = [(ring[p], ring[(p - 1) % count]) for p in range(count)]
        self.state = (self.block(self.left, count - 1), self.block(self.right, 1))
        self.done = 0

    def block(self, side, offset):
        index = self.order[(self.spot + offset) % self.count]
        return lax.dynamic_index_in_dim(side, index, 0, keepdims=False)

    def advance(self, upto):
        count = self.count
        send_left, send_right = self.state
        for step in range(self.done, min(upto, count - 1)):
            got_left = lax.ppermute(send_left.astype(jnp.bfloat16), self.axis, self.forward)
            got_right = lax.ppermute(send_right.astype(jnp.bfloat16), self.axis, self.backward)
            send_left = got_left.astype(jnp.float32) + self.block(self.left, 2 * count - step - 2)
            send_right = got_right.astype(jnp.float32) + self.block(self.right, step + 2)
            self.done = step + 1
        self.state = (send_left, send_right)
        return self

    def result(self):
        self.advance(self.count - 1)
        return jnp.concatenate(list(self.state), axis=1)


def tp_project(partial, rows_mine, split, axis):
    rank = lax.axis_index(axis)
    core = rank % 2
    near = [(i, i ^ 1) for i in range(4)]
    far = [(i, i ^ 2) for i in range(4)]
    chip = partial + lax.ppermute(partial, axis, near)
    head = chip[:, :split]
    tail = chip[:, split:]
    half_rows = tail.shape[0] // 2
    mine = lax.dynamic_slice_in_dim(head, rank * rows_mine, rows_mine, 0)
    theirs = lax.dynamic_slice_in_dim(head, (rank ^ 2) * rows_mine, rows_mine, 0)
    own_head = mine + lax.ppermute(theirs, axis, far)
    tail_half = lax.dynamic_slice_in_dim(tail, core * half_rows, half_rows, 0)
    tail_half = tail_half + lax.ppermute(tail_half, axis, far)
    other_half = lax.ppermute(tail_half, axis, near)
    first = jnp.where(core == 0, tail_half, other_half)
    second = jnp.where(core == 0, other_half, tail_half)
    return own_head, jnp.concatenate([first, second], axis=0)


def tp_scatter(partial, rows_mine, axis):
    rank = lax.axis_index(axis)
    far = [(i, i ^ 2) for i in range(4)]
    near = [(i, i ^ 1) for i in range(4)]
    pair_rows = 2 * rows_mine
    chip = rank // 2
    kept = lax.dynamic_slice_in_dim(partial, chip * pair_rows, pair_rows, 0)
    sent = lax.dynamic_slice_in_dim(partial, (1 - chip) * pair_rows, pair_rows, 0)
    kept = kept.astype(jnp.float32) + lax.ppermute(
        sent.astype(jnp.bfloat16), axis, far
    ).astype(jnp.float32)
    core = rank % 2
    mine = lax.dynamic_slice_in_dim(kept, core * rows_mine, rows_mine, 0)
    other = lax.dynamic_slice_in_dim(kept, (1 - core) * rows_mine, rows_mine, 0)
    return mine + lax.ppermute(other.astype(jnp.bfloat16), axis, near).astype(jnp.float32)


def direct_gather(value, axis):
    count = lax.axis_size(axis)
    got = [value] + [None] * (count - 1)
    for shift in range(1, count):
        pairs = [(i, (i + shift) % count) for i in range(count)]
        got[count - shift] = lax.ppermute(value, axis, pairs)
    return jnp.stack(got, axis=0)


def direct_scatter(partial, axis):
    count = lax.axis_size(axis)
    rows = partial.shape[0] // count
    blocks = partial.reshape(count, rows, partial.shape[1])
    total = blocks[0]
    for shift in range(1, count):
        pairs = [(i, (i + shift) % count) for i in range(count)]
        total = total + lax.ppermute(blocks[shift].astype(jnp.bfloat16), axis, pairs).astype(
            jnp.float32
        )
    return total


def butterfly_sum(value, axis):
    count = lax.axis_size(axis)
    stride = 1
    while stride < count:
        pairs = [(i, i ^ stride) for i in range(count)]
        value = value + lax.ppermute(value, axis, pairs)
        stride *= 2
    return value


def shards(ring, tokens, document, place, w_qkv, w_out, grad_out):
    rows_ctx, slice_width = tokens.shape
    ctx_size = lax.axis_size("ctx")
    tp_size = lax.axis_size("tp")
    rows_mine = rows_ctx // tp_size
    tp_rank = lax.axis_index("tp")
    head_dim = HD
    heads = HQ
    heads_width = heads * head_dim
    pair_width = 2 * head_dim
    factor = 1.0 / math.sqrt(head_dim)
    first_row = tp_rank * rows_mine
    stacked = heads * rows_mine
    total_rows = ctx_size * rows_ctx

    grad_part = against(grad_out, w_out).astype(jnp.bfloat16)

    cosine_all, sine_all = angles(place, head_dim)
    cosine_mine = lax.dynamic_slice_in_dim(cosine_all, first_row, rows_mine, 0)
    sine_mine = lax.dynamic_slice_in_dim(sine_all, first_row, rows_mine, 0)
    query_doc = lax.dynamic_slice_in_dim(document, first_row, rows_mine, 0)
    query_place = lax.dynamic_slice_in_dim(place, first_row, rows_mine, 0)

    projected = against(tokens, w_qkv)
    if tp_size == 4 and rows_ctx % (2 * tp_size) == 0:
        query_block, pair_rows = tp_project(projected, rows_mine, heads_width, "tp")
    else:
        qkv = lax.psum(projected, "tp")
        query_block = lax.dynamic_slice_in_dim(qkv[:, :heads_width], first_row, rows_mine, 0)
        pair_rows = qkv[:, heads_width:]
    keys = rotate(pair_rows[:, :head_dim], cosine_all, sine_all).astype(jnp.bfloat16)
    values = pair_rows[:, head_dim:].astype(jnp.bfloat16)

    info = jnp.concatenate(
        [document, place // PIECE, place % PIECE], axis=0
    ).astype(jnp.float32)
    info_rows = -(-info.shape[0] // pair_width)
    info = jnp.pad(info, (0, info_rows * pair_width - info.shape[0]))
    info = info.reshape(info_rows, pair_width).astype(jnp.bfloat16)
    packed = jnp.concatenate([keys, values], axis=1)
    packed = jnp.concatenate([packed, info], axis=0)
    gathered = direct_gather(packed, "ctx")
    if tp_size == 4 and rows_ctx % (2 * tp_size) == 0:
        grad_rows = tp_scatter(grad_part, rows_mine, "tp").astype(jnp.bfloat16)
    else:
        grad_rows = lax.psum_scatter(grad_part, "tp", scatter_dimension=0, tiled=True)
    keys_all = gathered[:, :rows_ctx, :head_dim].reshape(total_rows, head_dim)
    values_all = gathered[:, :rows_ctx, head_dim:].reshape(total_rows, head_dim)
    info_all = gathered[:, rows_ctx:, :].reshape(ctx_size, info_rows * pair_width).astype(
        jnp.float32
    )
    key_doc = info_all[:, :rows_ctx].reshape(total_rows)
    key_place = (
        info_all[:, rows_ctx : 2 * rows_ctx] * PIECE + info_all[:, 2 * rows_ctx : 3 * rows_ctx]
    ).reshape(total_rows)

    allowed = (query_doc.astype(jnp.float32)[:, None] == key_doc[None, :]) & (
        key_place[None, :] <= query_place.astype(jnp.float32)[:, None]
    )
    allowed = jnp.broadcast_to(allowed[None], (heads, rows_mine, total_rows)).reshape(
        stacked, total_rows
    )

    raw_query = query_block.reshape(rows_mine, heads, head_dim)
    rotated = rotate(raw_query, cosine_mine[:, None, :], sine_mine[:, None, :]).astype(jnp.bfloat16)
    queries = jnp.transpose(rotated, (1, 0, 2)).reshape(stacked, head_dim)

    scores = against(queries, keys_all) * factor
    masked = jnp.where(allowed, scores, NEG)
    top = jnp.max(masked, axis=1)
    weights = jnp.where(allowed, jnp.exp(masked - top[:, None]), 0.0)
    total = jnp.sum(weights, axis=1)
    summed = jnp.dot(weights.astype(jnp.bfloat16), values_all, preferred_element_type=jnp.float32)
    attended = (summed / total[:, None]).astype(jnp.bfloat16)
    logsum = top + jnp.log(total)

    rows_attended = jnp.transpose(attended.reshape(heads, rows_mine, head_dim), (1, 0, 2)).reshape(
        rows_mine, heads_width
    )
    piece = lax.all_gather(rows_attended, "tp", axis=0, tiled=True)
    out = jnp.dot(piece, w_out, preferred_element_type=jnp.float32).astype(jnp.bfloat16)
    out_weight_grad = across(piece, grad_out)

    grad_stack = jnp.transpose(grad_rows.reshape(rows_mine, heads, head_dim), (1, 0, 2)).reshape(
        stacked, head_dim
    )
    delta = jnp.sum(grad_stack.astype(jnp.float32) * attended.astype(jnp.float32), axis=1)
    prob = jnp.where(allowed, jnp.exp(scores - logsum[:, None]), 0.0)
    dprob = against(grad_stack, values_all)
    dscore = (prob * (dprob - delta[:, None])).astype(jnp.bfloat16)
    query_sum = jnp.dot(dscore, keys_all, preferred_element_type=jnp.float32)
    key_part = across(dscore, queries) * factor
    value_part = across(prob.astype(jnp.bfloat16), grad_stack)
    pair_all = jnp.concatenate([key_part, value_part], axis=1)
    out_ring = Ring(out_weight_grad, ring, "ctx").advance(len(ring) // 4)
    out_ring.state, pair_all = lax.optimization_barrier((out_ring.state, pair_all))
    pair_grad = butterfly_sum(direct_scatter(pair_all, "ctx"), "tp")

    key_raw = rotate(pair_grad[:, :head_dim], cosine_all, -sine_all)
    query_grad = jnp.transpose((query_sum * factor).reshape(heads, rows_mine, head_dim), (1, 0, 2))
    query_raw = rotate(query_grad, cosine_mine[:, None, :], -sine_mine[:, None, :]).reshape(
        rows_mine, heads_width
    )
    query_rows = lax.all_gather(query_raw.astype(jnp.bfloat16), "tp", axis=0, tiled=True)
    d_qkv = jnp.concatenate(
        [query_rows, key_raw.astype(jnp.bfloat16), pair_grad[:, head_dim:].astype(jnp.bfloat16)],
        axis=1,
    )
    grad_x = jnp.dot(d_qkv, w_qkv, preferred_element_type=jnp.float32).astype(jnp.bfloat16)
    joint_weight = across(d_qkv, tokens)
    out_ring.advance(len(ring) - 1)
    out_ring.state, joint_weight = lax.optimization_barrier((out_ring.state, joint_weight))
    grad_w_qkv = ring_scatter(joint_weight, ring, "ctx")
    grad_w_out = out_ring.result()
    return (out, grad_x, grad_w_qkv, grad_w_out)


def solution(mesh):
    return jax.shard_map(
        functools.partial(shards, ring_of(mesh)),
        mesh=mesh,
        in_specs=(P("ctx", "tp"), P("ctx"), P("ctx"), P(None, "tp"), P(None, "tp"), P("ctx", "tp")),
        out_specs=(P("ctx", "tp"), P("ctx", "tp"), P("ctx", "tp"), P("ctx", "tp")),
        check_vma=False,
    )
```
